32 devices in a mesh: lon: 4 (over x, core), lat: 8 (over z, y).
Axes of the slice: x: 2, y: 2, z: 4, core: 2. Of those that a mesh axis runs over, the one named last changes fastest.
Arguments:
- prognostic: float32 [4, 16, 192, 1536], P(None, None, 'lat', 'lon'), may hold values from -6 to 6
- tracers: float32 [4, 16, 192, 1536], P(None, None, 'lat', 'lon'), may hold values from -6 to 6
- zonal_courant: float32 [16, 192, 1536], P(None, 'lat', 'lon'), may hold values from -0.45 to 0.45
- meridional_courant: float32 [16, 192, 1536], P(None, 'lat', 'lon'), may hold values from -0.45 to 0.45
- filter_band: int32 [192], P('lat'), may hold values from 96 to 768, as said below
- dep_owner: int32 [192, 2], P('lat'), may hold values from 0 to 7, as said below
- dep_row: int32 [192, 2], P('lat'), may hold values from 0 to 23
- dep_weight: float32 [192, 2], P('lat'), may hold values from 0 to 1, as said below
Outputs:
- new_prognostic: float32 [4, 16, 192, 1536], P(None, None, 'lat', 'lon')
- new_tracers: float32 [4, 16, 192, 1536], P(None, None, 'lat', 'lon')
The draws below stay inside these ranges and needn't reach their ends.
Inputs may be any that keep to these rules, and one draw needn't show every extreme that they name: `filter_band`: rows within 24 of either pole hold values below 768; all other rows hold 768. `dep_owner`: among the 48 entries of one band, at most 12 name the same owner band, and some owner is named exactly 12 times; the owners a band names are the bands nearest to it, distance counted across either pole. `dep_weight`: Positive; the 2 weights of a row sum to 1.
All inputs are finite; a program needn't handle non-finite values.
Results may differ from the reference program's by a relative error of at most 0.00007.
Values sent between devices are 32-bit elements; how exact they have to be, the bound alone decides.
No kernel may reach another device: no remote copies, remote signals or barrier semaphores. Data moves between devices by JAX's collectives and lax.ppermute only.
A program may use at most 128 MiB of HBM per device.

```python
import math
import jax
import jax.numpy as jnp
from jax import lax

NLON = 1536
ROWS_DEV = 24
LEV = 16
NPROG = 4
NTRAC = 4
DEP = 2
NLAT = 192
BANDS = 8
CAP = 12
POLAR_ROWS = 24


def departure_lists(key):
    base_key = jax.random.fold_in(key, 7)
    entries = ROWS_DEV * DEP
    least_size = max(1, CAP - 1)
    all_bands = jnp.arange(BANDS, dtype=jnp.int32)

    def one_band(band_key, home):
        size_key, owner_key, row_key, order_key = jax.random.split(band_key, 4)
        group_sizes = jax.random.randint(size_key, (entries,), least_size, CAP + 1).at[0].set(CAP)
        group_ends = jnp.cumsum(group_sizes)
        positions = jnp.arange(entries)
        group_ids = jnp.sum((group_ends[None, :] <= positions[:, None]).astype(jnp.int32), axis=1)
        distance = jnp.minimum(jnp.abs(all_bands - home), jnp.minimum(all_bands + home + 1, 2 * BANDS - 1 - all_bands - home))
        tiebreak = jax.random.permutation(owner_key, BANDS).astype(jnp.int32)
        scores = distance * BANDS + tiebreak
        nearest = jnp.argsort(scores, stable=True).astype(jnp.int32)
        owners = nearest[jnp.minimum(group_ids, BANDS - 1)]
        row_ids = jax.random.randint(row_key, (entries,), 0, ROWS_DEV).at[0].set(ROWS_DEV - 1).at[1].set(0)
        shuffle = jax.random.permutation(order_key, entries)
        return (owners[shuffle], row_ids[shuffle])
    owners, row_ids = jax.vmap(one_band)(jax.random.split(base_key, BANDS), all_bands)
    return (owners.reshape(NLAT, DEP).astype(jnp.int32), row_ids.reshape(NLAT, DEP).astype(jnp.int32))


def draw_dep_owner(key, part):
    return departure_lists(key)[0]


def draw_dep_row(key, part):
    return departure_lists(key)[1]


def draw_dep_weight(key, part):
    raw = jax.random.uniform(jax.random.fold_in(key, 11), (NLAT, DEP), jnp.float32, 0.1, 1.0)
    return (raw / jnp.sum(raw, axis=1, keepdims=True)).astype(jnp.float32)


def polar_bands(key):
    band_key = jax.random.fold_in(key, 3)
    choose_key, lower_key, higher_key = jax.random.split(band_key, 3)
    latitude = jnp.arange(NLAT)
    in_polar = (latitude < POLAR_ROWS) | (latitude >= NLAT - POLAR_ROWS)
    lowest = max(1, NLON // 16)
    lower_band = jax.random.randint(lower_key, (NLAT,), lowest, NLON // 12 + 1)
    higher_band = jax.random.randint(higher_key, (NLAT,), NLON // 6, NLON // 5 + 1)
    upper_set = jax.random.randint(choose_key, (NLAT,), 0, 2)
    drawn_band = jnp.where(upper_set == 1, higher_band, lower_band).at[0].set(lowest)
    return (jnp.where(in_polar, drawn_band, NLON // 2).astype(jnp.int32), in_polar)


def draw_filter_band(key, part):
    return polar_bands(key)[0]


def draw_prognostic(key, part):
    band_rows, in_polar = polar_bands(key)
    noise_key, phase_key = jax.random.split(jax.random.fold_in(key, 5))
    full_shape = (NPROG, LEV, NLAT, NLON)
    noise_field = jnp.clip(jax.random.normal(noise_key, full_shape, jnp.float32), -3.5, 3.5)
    amplitude = 2.0
    wave_number = band_rows + 1
    longitude = jnp.arange(NLON, dtype=jnp.int32)
    phase_index = wave_number[:, None] * longitude[None, :] % NLON
    angles_grid = 2.0 * math.pi / NLON * phase_index.astype(jnp.float32)
    offsets = jax.random.uniform(phase_key, (NPROG, LEV, NLAT, 1), jnp.float32, -math.pi, math.pi)
    polar_mask = in_polar.astype(jnp.float32)[None, None, :, None]
    zonal_wave = amplitude * jnp.cos(angles_grid[None, None] + offsets) * polar_mask
    return (noise_field + zonal_wave).astype(jnp.float32)


def shard_levels(stream_key, extent, cuts, least, top_value):
    gain = 1.0
    for dim, parts in cuts:
        heights = jax.random.uniform(jax.random.fold_in(jax.random.fold_in(stream_key, 6), dim), (parts,), jnp.float32, least / len(cuts), top_value / len(cuts))
        gain = gain * jnp.repeat(jnp.exp(heights), extent[dim] // parts).reshape((-1,) + (1,) * (len(extent) - 1 - dim))
    return gain


def gaussian(rng, shape, scale, bound, shards=(), kind=jnp.bfloat16):
    level = shard_levels(rng, shape, shards, -0.22, 0.18) if shards else 1.0
    array = jax.random.normal(rng, shape, jnp.float32) * scale * level
    return jnp.minimum(jnp.maximum(array, -bound), bound).astype(kind)


def setup_inputs(seed: int = 0) -> dict:
    streams_of = jax.random.split(jax.random.key(seed), 9)
    prognostic = draw_prognostic(jax.random.fold_in(streams_of[8], 71), 0)
    tracers = gaussian(streams_of[1], (NTRAC, LEV, NLAT, NLON), 1.0, 6.0, ((2, 8), (3, 4)), jnp.float32)
    zonal_courant = jnp.clip(jax.random.uniform(streams_of[2], (LEV, NLAT, NLON), jnp.float32, -0.45, 0.45) * shard_levels(streams_of[2], (LEV, NLAT, NLON), ((1, 8), (2, 4)), -0.4, 0.0), -0.45, 0.45)
    meridional_courant = jnp.clip(jax.random.uniform(streams_of[3], (LEV, NLAT, NLON), jnp.float32, -0.45, 0.45) * shard_levels(streams_of[3], (LEV, NLAT, NLON), ((1, 8), (2, 4)), -0.4, 0.0), -0.45, 0.45)
    filter_band = draw_filter_band(jax.random.fold_in(streams_of[8], 71), 0)
    dep_owner = draw_dep_owner(jax.random.fold_in(streams_of[8], 71), 0)
    dep_row = draw_dep_row(jax.random.fold_in(streams_of[8], 71), 0)
    dep_weight = draw_dep_weight(jax.random.fold_in(streams_of[8], 71), 0)
    return {"prognostic": prognostic, "tracers": tracers, "zonal_courant": zonal_courant, "meridional_courant": meridional_courant, "filter_band": filter_band, "dep_owner": dep_owner, "dep_row": dep_row, "dep_weight": dep_weight}


def lax_flux(courant, left_cells, right_cells):
    return 0.5 * courant * (left_cells + right_cells) - 0.5 * courant * courant * (right_cells - left_cells)


def reference(prognostic, tracers, zonal_courant, meridional_courant, filter_band, dep_owner, dep_row, dep_weight):
    def advect(one_field):
        east = jnp.roll(one_field, -1, axis=2)
        zonal_flux = lax_flux(zonal_courant, one_field, east)
        zonal_div = zonal_flux - jnp.roll(zonal_flux, 1, axis=2)
        padded = jnp.pad(one_field, ((0, 0), (1, 1), (0, 0)))
        speeds = jnp.pad(meridional_courant, ((0, 0), (1, 1), (0, 0)))
        merid_flux = lax_flux(speeds[:, :-1], padded[:, :-1], padded[:, 1:])
        faces = jnp.arange(NLAT + 1)
        merid_flux = jnp.where((faces == NLAT)[None, :, None], jnp.float32(0.0), merid_flux)
        merid_div = merid_flux[:, 1:] - merid_flux[:, :-1]
        return one_field - zonal_div - merid_div

    prog_adv = lax.map(advect, prognostic)
    wavenumber = jnp.arange(NLON // 2 + 1).astype(jnp.float32)
    ratios = filter_band.astype(jnp.float32)[:, None] / jnp.maximum(wavenumber, 1.0)[None, :]
    damping = jnp.minimum(1.0, ratios * ratios)
    spectrum = jnp.fft.rfft(prog_adv, axis=-1)
    new_prognostic = jnp.fft.irfft(spectrum * damping[None, None, :, :], n=NLON, axis=-1).astype(prog_adv.dtype)
    source_rows = dep_owner * ROWS_DEV + dep_row
    departed = dep_weight[:, 0][None, None, :, None] * tracers[:, :, source_rows[:, 0], :]
    for link in range(1, DEP):
        departed = departed + dep_weight[:, link][None, None, :, None] * tracers[:, :, source_rows[:, link], :]
    return new_prognostic, departed
```

```python
import math

import jax
import jax.numpy as jnp
from jax import lax
from jax.sharding import PartitionSpec as P

PRECISE = lax.Precision.HIGHEST


def padded(value, sides, width, wrap):
    for axis, dim in sides:
        size, length = (lax.axis_size(axis), value.shape[dim])
        up = [(i, (i + 1) % size) for i in range(size if wrap else size - 1)]
        down = [(j, i) for i, j in up]
        last = lax.slice_in_dim(value, length - width, length, axis=dim)
        first = lax.slice_in_dim(value, 0, width, axis=dim)
        before = lax.ppermute(last, axis, up)
        after = lax.ppermute(first, axis, down)
        value = jnp.concatenate([before, value, after], axis=dim)
    return value


def face_flux(values, speeds, axis):
    count = values.shape[axis] - 2
    left_cells = lax.slice_in_dim(values, 0, count + 1, axis=axis)
    right_cells = lax.slice_in_dim(values, 1, count + 2, axis=axis)
    courant = lax.slice_in_dim(speeds, 0, count + 1, axis=axis)
    return 0.5 * courant * (left_cells + right_cells) - 0.5 * courant * courant * (
        right_cells - left_cells
    )


def column_factors(band_rows, length):
    column = jnp.arange(length, dtype=jnp.int32)
    half_length = length // 2
    frequency = jnp.where(column <= half_length, column, column - half_length)
    single = (column == 0) | (column == half_length)
    weights = jnp.where(single, 1.0 / length, 2.0 / length).astype(jnp.float32)
    ratios = (
        band_rows.astype(jnp.float32)[:, None]
        / jnp.maximum(frequency, 1).astype(jnp.float32)[None, :]
    )
    damping = jnp.minimum(1.0, ratios * ratios)
    return (damping - 1.0) * weights[None, :]


def circle_basis(length):
    half_length = length // 2
    column = jnp.arange(length, dtype=jnp.int32)
    frequency = jnp.where(column <= half_length, column, column - half_length)
    low_count = 64
    high_count = length // low_count
    low = jnp.arange(low_count, dtype=jnp.int32)
    high = jnp.arange(high_count, dtype=jnp.int32) * low_count
    scale = 2.0 * math.pi / length
    low_angle = scale * (low[:, None] * frequency[None, :] % length).astype(jnp.float32)
    high_angle = scale * (high[:, None] * frequency[None, :] % length).astype(jnp.float32)
    low_cos, low_sin = jnp.cos(low_angle), jnp.sin(low_angle)
    high_cos, high_sin = jnp.cos(high_angle), jnp.sin(high_angle)
    cos_part = high_cos[:, None] * low_cos[None] - high_sin[:, None] * low_sin[None]
    sin_part = high_sin[:, None] * low_cos[None] + high_cos[:, None] * low_sin[None]
    basis = jnp.where((column <= half_length)[None, None, :], cos_part, sin_part)
    return basis.reshape(length, length)


def polar_filter(values, band_rows):
    fields, levels, rows, block_cells = values.shape
    parts = lax.axis_size("lon")
    length = block_cells * parts
    flat = values.reshape(fields * levels * rows, block_cells)
    circles = lax.all_to_all(flat, "lon", split_axis=0, concat_axis=1, tiled=True)
    basis_table = circle_basis(length)
    spectrum = jnp.dot(circles, basis_table, precision=PRECISE)
    factors = column_factors(band_rows, length)
    circle_rows = circles.shape[0]
    scaled = (spectrum.reshape(circle_rows // rows, rows, length) * factors[None]).reshape(
        circle_rows, length
    )
    change = lax.dot_general(
        scaled, basis_table, (((1,), (1,)), ((), ())), precision=PRECISE
    )
    back = lax.all_to_all(change, "lon", split_axis=1, concat_axis=0, tiled=True)
    return values + back.reshape(values.shape)


def departure_terms(tracers, dep_owner, dep_row, dep_weight):
    band_count = lax.axis_size("lat")
    row_count, link_count = dep_owner.shape
    entries = row_count * link_count
    capacity = max(2, -(-2 * entries // band_count))
    owner_ids = dep_owner.reshape(entries)
    source = dep_row.reshape(entries)
    positions = jnp.arange(entries)
    earlier = (owner_ids[:, None] == owner_ids[None, :]) & (positions[None, :] < positions[:, None])
    slot_ids = jnp.sum(earlier.astype(jnp.int32), axis=1)
    band_ids = jnp.arange(band_count, dtype=jnp.int32)
    slot_range = jnp.arange(capacity, dtype=jnp.int32)
    matches = (owner_ids[:, None, None] == band_ids[None, :, None]) & (
        slot_ids[:, None, None] == slot_range[None, None, :]
    )
    request = jnp.sum(jnp.where(matches, source[:, None, None], 0), axis=0)
    wanted = lax.all_to_all(request, "lat", split_axis=0, concat_axis=0, tiled=True)
    by_row = jnp.transpose(tracers, (2, 0, 1, 3))
    outgoing = by_row[wanted]
    incoming = lax.all_to_all(outgoing, "lat", split_axis=0, concat_axis=0, tiled=True)
    stacked_rows = incoming.reshape((band_count * capacity,) + incoming.shape[2:])
    picked = stacked_rows[owner_ids * capacity + slot_ids].reshape(
        (row_count, link_count) + stacked_rows.shape[1:]
    )
    summed = dep_weight[:, 0][:, None, None, None] * picked[:, 0]
    summed = summed + dep_weight[:, 1][:, None, None, None] * picked[:, 1]
    return jnp.transpose(summed, (1, 2, 0, 3))


def body(
    prognostic,
    tracers,
    zonal_courant,
    meridional_courant,
    filter_band,
    dep_owner,
    dep_row,
    dep_weight,
):
    row_count = prognostic.shape[2]
    departed = departure_terms(tracers, dep_owner, dep_row, dep_weight)
    lon_padded = padded(
        jnp.concatenate([prognostic, zonal_courant[None]], axis=0), (("lon", 3),), 1, True
    )
    zonal_flux = face_flux(lon_padded[:-1], lon_padded[-1:], 3)
    lat_padded = padded(
        jnp.concatenate([prognostic, meridional_courant[None]], axis=0), (("lat", 2),), 1, False
    )
    merid_flux = face_flux(lat_padded[:-1], lat_padded[-1:], 2)
    total_rows = row_count * lax.axis_size("lat")
    face_rows = lax.axis_index("lat") * row_count + jnp.arange(row_count + 1) - 1
    merid_flux = jnp.where(
        (face_rows == total_rows - 1)[None, None, :, None], jnp.float32(0.0), merid_flux
    )
    advected = (
        prognostic
        - (zonal_flux[..., 1:] - zonal_flux[..., :-1])
        - (merid_flux[:, :, 1:] - merid_flux[:, :, :-1])
    )
    new_prognostic = polar_filter(advected, filter_band)
    return (new_prognostic, departed)


def solution(mesh):
    return jax.shard_map(
        body,
        mesh=mesh,
        in_specs=(
            P(None, None, "lat", "lon"),
            P(None, None, "lat", "lon"),
            P(None, "lat", "lon"),
            P(None, "lat", "lon"),
            P("lat"),
            P("lat", None),
            P("lat", None),
            P("lat", None),
        ),
        out_specs=(P(None, None, "lat", "lon"), P(None, None, "lat", "lon")),
        check_vma=False,
    )
```

```python
import math

import jax
import numpy as np
import jax.numpy as jnp
from jax import lax
from jax.sharding import PartitionSpec as P

PRECISE = lax.Precision.HIGHEST


def padded(value, sides, width, wrap):
    for axis, dim in sides:
        size, length = (lax.axis_size(axis), value.shape[dim])
        up = [(i, (i + 1) % size) for i in range(size if wrap else size - 1)]
        down = [(j, i) for i, j in up]
        last = lax.slice_in_dim(value, length - width, length, axis=dim)
        first = lax.slice_in_dim(value, 0, width, axis=dim)
        before = lax.ppermute(last, axis, up)
        after = lax.ppermute(first, axis, down)
        value = jnp.concatenate([before, value, after], axis=dim)
    return value


def face_flux(values, speeds, axis):
    count = values.shape[axis] - 2
    left_cells = lax.slice_in_dim(values, 0, count + 1, axis=axis)
    right_cells = lax.slice_in_dim(values, 1, count + 2, axis=axis)
    courant = lax.slice_in_dim(speeds, 0, count + 1, axis=axis)
    return 0.5 * courant * (left_cells + right_cells) - 0.5 * courant * courant * (
        right_cells - left_cells
    )


def column_factors(band_rows, length):
    column = jnp.arange(length, dtype=jnp.int32)
    half_length = length // 2
    frequency = jnp.where(column <= half_length, column, column - half_length)
    single = (column == 0) | (column == half_length)
    weights = jnp.where(single, 1.0 / length, 2.0 / length).astype(jnp.float32)
    ratios = (
        band_rows.astype(jnp.float32)[:, None]
        / jnp.maximum(frequency, 1).astype(jnp.float32)[None, :]
    )
    damping = jnp.minimum(1.0, ratios * ratios)
    return (damping - 1.0) * weights[None, :]


def circle_basis(length):
    half_length = length // 2
    column = jnp.arange(length, dtype=jnp.int32)
    frequency = jnp.where(column <= half_length, column, column - half_length)
    low_count = 64
    high_count = length // low_count
    low = jnp.arange(low_count, dtype=jnp.int32)
    high = jnp.arange(high_count, dtype=jnp.int32) * low_count
    scale = 2.0 * math.pi / length
    low_angle = scale * (low[:, None] * frequency[None, :] % length).astype(jnp.float32)
    high_angle = scale * (high[:, None] * frequency[None, :] % length).astype(jnp.float32)
    low_cos, low_sin = jnp.cos(low_angle), jnp.sin(low_angle)
    high_cos, high_sin = jnp.cos(high_angle), jnp.sin(high_angle)
    cos_part = high_cos[:, None] * low_cos[None] - high_sin[:, None] * low_sin[None]
    sin_part = high_sin[:, None] * low_cos[None] + high_cos[:, None] * low_sin[None]
    basis = jnp.where((column <= half_length)[None, None, :], cos_part, sin_part)
    return basis.reshape(length, length)


def polar_filter(values, band_rows):
    fields, levels, rows, block_cells = values.shape
    parts = lax.axis_size("lon")
    length = block_cells * parts
    flat = values.reshape(fields * levels * rows, block_cells)
    circles = lax.all_to_all(flat, "lon", split_axis=0, concat_axis=1, tiled=True)
    basis_table = circle_basis(length)
    spectrum = jnp.dot(circles, basis_table, precision=PRECISE)
    factors = column_factors(band_rows, length)
    circle_rows = circles.shape[0]
    scaled = (spectrum.reshape(circle_rows // rows, rows, length) * factors[None]).reshape(
        circle_rows, length
    )
    change = lax.dot_general(
        scaled, basis_table, (((1,), (1,)), ((), ())), precision=PRECISE
    )
    back = lax.all_to_all(change, "lon", split_axis=1, concat_axis=0, tiled=True)
    return values + back.reshape(values.shape)


def departure_terms(tracers, dep_owner, dep_row, dep_weight):
    band_count = lax.axis_size("lat")
    row_count, link_count = dep_owner.shape
    entries = row_count * link_count
    capacity = max(2, -(-2 * entries // band_count))
    owner_ids = dep_owner.reshape(entries)
    source = dep_row.reshape(entries)
    positions = jnp.arange(entries)
    earlier = (owner_ids[:, None] == owner_ids[None, :]) & (positions[None, :] < positions[:, None])
    slot_ids = jnp.sum(earlier.astype(jnp.int32), axis=1)
    band_ids = jnp.arange(band_count, dtype=jnp.int32)
    slot_range = jnp.arange(capacity, dtype=jnp.int32)
    matches = (owner_ids[:, None, None] == band_ids[None, :, None]) & (
        slot_ids[:, None, None] == slot_range[None, None, :]
    )
    request = jnp.sum(jnp.where(matches, source[:, None, None], 0), axis=0)
    wanted = lax.all_to_all(request, "lat", split_axis=0, concat_axis=0, tiled=True)
    by_row = jnp.transpose(tracers, (2, 0, 1, 3))
    outgoing = by_row[wanted]
    incoming = lax.all_to_all(outgoing, "lat", split_axis=0, concat_axis=0, tiled=True)
    stacked_rows = incoming.reshape((band_count * capacity,) + incoming.shape[2:])
    picked = stacked_rows[owner_ids * capacity + slot_ids].reshape(
        (row_count, link_count) + stacked_rows.shape[1:]
    )
    summed = dep_weight[:, 0][:, None, None, None] * picked[:, 0]
    summed = summed + dep_weight[:, 1][:, None, None, None] * picked[:, 1]
    return jnp.transpose(summed, (1, 2, 0, 3))


def band_distance(a, b, band_count):
    return min(abs(a - b), a + b + 1, 2 * band_count - 1 - a - b)


def near_plan(band_count, entries, capacity):
    reach = min(band_count, -(-entries // capacity) + 1)
    nearest = []
    for band in range(band_count):
        order = sorted(range(band_count), key=lambda o: (band_distance(band, o, band_count), o))
        nearest.append(order[:reach])
    offsets = sorted({o - b for b in range(band_count) for o in nearest[b] if o != b})
    return nearest, offsets


def departure_near(tracers, dep_owner, dep_row, dep_weight, nearest, offsets, capacity):
    band_count = lax.axis_size("lat")
    row_count, link_count = dep_owner.shape
    entries = row_count * link_count
    me = lax.axis_index("lat")
    all_owner = lax.all_gather(dep_owner.reshape(entries), "lat", tiled=False)
    all_row = lax.all_gather(dep_row.reshape(entries), "lat", tiled=False)
    near_mask = np.zeros((band_count, band_count), bool)
    for band in range(band_count):
        near_mask[band, nearest[band]] = True
    covered = jnp.all(
        jnp.asarray(near_mask)[jnp.arange(band_count)[:, None], all_owner]
    )
    positions = jnp.arange(entries)
    earlier = (all_owner[:, :, None] == all_owner[:, None, :]) & (
        positions[None, None, :] < positions[None, :, None]
    )
    all_slot = jnp.sum(earlier.astype(jnp.int32), axis=2)
    slot_range = jnp.arange(capacity, dtype=jnp.int32)
    by_row = jnp.transpose(tracers, (2, 0, 1, 3))
    received = []
    for offset in offsets:
        pairs = [
            (band + offset, band)
            for band in range(band_count)
            if band + offset != band and (band + offset) in nearest[band]
        ]
        receiver = jnp.clip(me - offset, 0, band_count - 1)
        owner_of = all_owner[receiver]
        slot_of = all_slot[receiver]
        matches = (owner_of[:, None] == me) & (slot_of[:, None] == slot_range[None, :])
        request = jnp.sum(jnp.where(matches, all_row[receiver][:, None], 0), axis=0)
        outgoing = by_row[request]
        received.append(lax.ppermute(outgoing, "lat", pairs))
    stacked = jnp.concatenate([by_row] + received, axis=0)
    position_table = np.zeros(2 * band_count - 1, np.int32)
    for index, offset in enumerate(offsets):
        position_table[offset + band_count - 1] = row_count + index * capacity
    owner_ids = dep_owner.reshape(entries)
    slot_ids = all_slot[me]
    base = jnp.asarray(position_table)[owner_ids - me + band_count - 1]
    picks = jnp.where(owner_ids == me, dep_row.reshape(entries), base + slot_ids)
    picked = stacked[picks].reshape((row_count, link_count) + stacked.shape[1:])
    summed = dep_weight[:, 0][:, None, None, None] * picked[:, 0]
    for link in range(1, link_count):
        summed = summed + dep_weight[:, link][:, None, None, None] * picked[:, link]
    return jnp.transpose(summed, (1, 2, 0, 3)), covered


def departure_all(tracers, dep_owner, dep_row, dep_weight):
    band_count = lax.axis_size("lat")
    row_count, link_count = dep_owner.shape
    entries = row_count * link_count
    capacity = max(2, -(-2 * entries // band_count))
    nearest, offsets = near_plan(band_count, entries, capacity)
    near, covered = departure_near(
        tracers, dep_owner, dep_row, dep_weight, nearest, offsets, capacity
    )
    return lax.cond(
        covered,
        lambda: near,
        lambda: departure_terms(tracers, dep_owner, dep_row, dep_weight),
    )


def body(
    prognostic,
    tracers,
    zonal_courant,
    meridional_courant,
    filter_band,
    dep_owner,
    dep_row,
    dep_weight,
):
    row_count = prognostic.shape[2]
    departed = departure_all(tracers, dep_owner, dep_row, dep_weight)
    lon_padded = padded(
        jnp.concatenate([prognostic, zonal_courant[None]], axis=0), (("lon", 3),), 1, True
    )
    zonal_flux = face_flux(lon_padded[:-1], lon_padded[-1:], 3)
    lat_padded = padded(
        jnp.concatenate([prognostic, meridional_courant[None]], axis=0), (("lat", 2),), 1, False
    )
    merid_flux = face_flux(lat_padded[:-1], lat_padded[-1:], 2)
    total_rows = row_count * lax.axis_size("lat")
    face_rows = lax.axis_index("lat") * row_count + jnp.arange(row_count + 1) - 1
    merid_flux = jnp.where(
        (face_rows == total_rows - 1)[None, None, :, None], jnp.float32(0.0), merid_flux
    )
    advected = (
        prognostic
        - (zonal_flux[..., 1:] - zonal_flux[..., :-1])
        - (merid_flux[:, :, 1:] - merid_flux[:, :, :-1])
    )
    new_prognostic = polar_filter(advected, filter_band)
    return (new_prognostic, departed)


def solution(mesh):
    return jax.shard_map(
        body,
        mesh=mesh,
        in_specs=(
            P(None, None, "lat", "lon"),
            P(None, None, "lat", "lon"),
            P(None, "lat", "lon"),
            P(None, "lat", "lon"),
            P("lat"),
            P("lat", None),
            P("lat", None),
            P("lat", None),
        ),
        out_specs=(P(None, None, "lat", "lon"), P(None, None, "lat", "lon")),
        check_vma=False,
    )
```

```python
import math

import jax
import numpy as np
import jax.numpy as jnp
from jax import lax
from jax.sharding import PartitionSpec as P

PRECISE = lax.Precision.HIGHEST


def padded(value, sides, width, wrap):
    for axis, dim in sides:
        size, length = (lax.axis_size(axis), value.shape[dim])
        up = [(i, (i + 1) % size) for i in range(size if wrap else size - 1)]
        down = [(j, i) for i, j in up]
        last = lax.slice_in_dim(value, length - width, length, axis=dim)
        first = lax.slice_in_dim(value, 0, width, axis=dim)
        before = lax.ppermute(last, axis, up)
        after = lax.ppermute(first, axis, down)
        value = jnp.concatenate([before, value, after], axis=dim)
    return value


def face_flux(values, speeds, axis):
    count = values.shape[axis] - 2
    left_cells = lax.slice_in_dim(values, 0, count + 1, axis=axis)
    right_cells = lax.slice_in_dim(values, 1, count + 2, axis=axis)
    courant = lax.slice_in_dim(speeds, 0, count + 1, axis=axis)
    return 0.5 * courant * (left_cells + right_cells) - 0.5 * courant * courant * (
        right_cells - left_cells
    )


def column_factors(band_rows, length):
    column = jnp.arange(length, dtype=jnp.int32)
    half_length = length // 2
    frequency = jnp.where(column <= half_length, column, column - half_length)
    single = (column == 0) | (column == half_length)
    weights = jnp.where(single, 1.0 / length, 2.0 / length).astype(jnp.float32)
    ratios = (
        band_rows.astype(jnp.float32)[:, None]
        / jnp.maximum(frequency, 1).astype(jnp.float32)[None, :]
    )
    damping = jnp.minimum(1.0, ratios * ratios)
    return (damping - 1.0) * weights[None, :]


def column_factors(band_rows, length):
    column = jnp.arange(length, dtype=jnp.int32)
    half_length = length // 2
    frequency = jnp.where(column <= half_length, column, column - half_length)
    single = (column == 0) | (column == half_length)
    weights = jnp.where(single, 1.0 / length, 2.0 / length).astype(jnp.float32)
    ratios = (
        band_rows.astype(jnp.float32)[:, None]
        / jnp.maximum(frequency, 1).astype(jnp.float32)[None, :]
    )
    damping = jnp.minimum(1.0, ratios * ratios)
    return (damping - 1.0) * weights[None, :]


def circle_basis(length):
    half_length = length // 2
    column = jnp.arange(length, dtype=jnp.int32)
    frequency = jnp.where(column <= half_length, column, column - half_length)
    low_count = 64
    high_count = length // low_count
    low = jnp.arange(low_count, dtype=jnp.int32)
    high = jnp.arange(high_count, dtype=jnp.int32) * low_count
    scale = 2.0 * math.pi / length
    low_angle = scale * (low[:, None] * frequency[None, :] % length).astype(jnp.float32)
    high_angle = scale * (high[:, None] * frequency[None, :] % length).astype(jnp.float32)
    low_cos, low_sin = jnp.cos(low_angle), jnp.sin(low_angle)
    high_cos, high_sin = jnp.cos(high_angle), jnp.sin(high_angle)
    cos_part = high_cos[:, None] * low_cos[None] - high_sin[:, None] * low_sin[None]
    sin_part = high_sin[:, None] * low_cos[None] + high_cos[:, None] * low_sin[None]
    basis = jnp.where((column <= half_length)[None, None, :], cos_part, sin_part)
    return basis.reshape(length, length)


def departure_terms(tracers, dep_owner, dep_row, dep_weight):
    band_count = lax.axis_size("lat")
    row_count, link_count = dep_owner.shape
    entries = row_count * link_count
    capacity = max(2, -(-2 * entries // band_count))
    owner_ids = dep_owner.reshape(entries)
    source = dep_row.reshape(entries)
    positions = jnp.arange(entries)
    earlier = (owner_ids[:, None] == owner_ids[None, :]) & (positions[None, :] < positions[:, None])
    slot_ids = jnp.sum(earlier.astype(jnp.int32), axis=1)
    band_ids = jnp.arange(band_count, dtype=jnp.int32)
    slot_range = jnp.arange(capacity, dtype=jnp.int32)
    matches = (owner_ids[:, None, None] == band_ids[None, :, None]) & (
        slot_ids[:, None, None] == slot_range[None, None, :]
    )
    request = jnp.sum(jnp.where(matches, source[:, None, None], 0), axis=0)
    wanted = lax.all_to_all(request, "lat", split_axis=0, concat_axis=0, tiled=True)
    by_row = jnp.transpose(tracers, (2, 0, 1, 3))
    outgoing = by_row[wanted]
    incoming = lax.all_to_all(outgoing, "lat", split_axis=0, concat_axis=0, tiled=True)
    stacked_rows = incoming.reshape((band_count * capacity,) + incoming.shape[2:])
    picked = stacked_rows[owner_ids * capacity + slot_ids].reshape(
        (row_count, link_count) + stacked_rows.shape[1:]
    )
    summed = dep_weight[:, 0][:, None, None, None] * picked[:, 0]
    summed = summed + dep_weight[:, 1][:, None, None, None] * picked[:, 1]
    return jnp.transpose(summed, (1, 2, 0, 3))


def circle_basis(cells, length):
    half_length = length // 2
    column = jnp.arange(length, dtype=jnp.int32)
    frequency = jnp.where(column <= half_length, column, column - half_length)
    low_count = math.gcd(cells.shape[0], 64)
    low = jnp.arange(low_count, dtype=jnp.int32)
    high = cells.reshape(-1, low_count)[:, 0]
    scale = 2.0 * math.pi / length
    low_angle = scale * (low[:, None] * frequency[None, :] % length).astype(jnp.float32)
    high_angle = scale * (high[:, None] * frequency[None, :] % length).astype(jnp.float32)
    low_cos, low_sin = jnp.cos(low_angle), jnp.sin(low_angle)
    high_cos, high_sin = jnp.cos(high_angle), jnp.sin(high_angle)
    cos_part = high_cos[:, None] * low_cos[None] - high_sin[:, None] * low_sin[None]
    sin_part = high_sin[:, None] * low_cos[None] + high_cos[:, None] * low_sin[None]
    basis = jnp.where((column <= half_length)[None, None, :], cos_part, sin_part)
    return basis.reshape(cells.shape[0], length)


def polar_filter(values, band_rows):
    fields, levels, rows, block_cells = values.shape
    parts = lax.axis_size("lon")
    me = lax.axis_index("lon")
    length = block_cells * parts
    flat = values.reshape(fields * levels * rows, block_cells)
    chunk = flat.shape[0] // parts
    blocks = [lax.dynamic_slice_in_dim(flat, me * chunk, chunk, axis=0)]
    for shift in range(1, parts):
        target = (me + shift) % parts
        piece = lax.dynamic_slice_in_dim(flat, target * chunk, chunk, axis=0)
        pairs = [(i, (i + shift) % parts) for i in range(parts)]
        blocks.append(lax.ppermute(piece, "lon", pairs))
    circles = jnp.concatenate(blocks, axis=1)
    shifts = jnp.arange(parts, dtype=jnp.int32)
    sources = (me - shifts) % parts
    cells = (sources[:, None] * block_cells + jnp.arange(block_cells, dtype=jnp.int32)[None]).reshape(length)
    basis_table = circle_basis(cells, length)
    spectrum = jnp.dot(circles, basis_table, precision=PRECISE)
    factors = column_factors(band_rows, length)
    scaled = (spectrum.reshape(chunk // rows, rows, length) * factors[None]).reshape(chunk, length)
    change = lax.dot_general(scaled, basis_table, (((1,), (1,)), ((), ())), precision=PRECISE)
    returned = [change[:, :block_cells]]
    for shift in range(1, parts):
        pairs = [(i, (i - shift) % parts) for i in range(parts)]
        piece = change[:, shift * block_cells:(shift + 1) * block_cells]
        returned.append(lax.ppermute(piece, "lon", pairs))
    stacked = jnp.stack(returned, axis=0)
    order = (jnp.arange(parts, dtype=jnp.int32) - me) % parts
    ordered = jnp.take(stacked, order, axis=0)
    return values + ordered.reshape(values.shape)


def band_distance(a, b, band_count):
    return min(abs(a - b), a + b + 1, 2 * band_count - 1 - a - b)


def near_plan(band_count, entries, capacity):
    reach = min(band_count, -(-entries // capacity) + 1)
    nearest = []
    for band in range(band_count):
        order = sorted(range(band_count), key=lambda o: (band_distance(band, o, band_count), o))
        nearest.append(order[:reach])
    offsets = sorted({o - b for b in range(band_count) for o in nearest[b] if o != b})
    return nearest, offsets


def departure_near(tracers, dep_owner, dep_row, dep_weight, nearest, offsets, capacity):
    band_count = lax.axis_size("lat")
    row_count, link_count = dep_owner.shape
    entries = row_count * link_count
    me = lax.axis_index("lat")
    owner_ids = dep_owner.reshape(entries)
    source = dep_row.reshape(entries)
    positions = jnp.arange(entries)
    earlier = (owner_ids[:, None] == owner_ids[None, :]) & (positions[None, :] < positions[:, None])
    slot_ids = jnp.sum(earlier.astype(jnp.int32), axis=1)
    near_mask = np.zeros((band_count, band_count), np.int32)
    for band in range(band_count):
        near_mask[band, nearest[band]] = 1
    outside = jnp.sum(1 - jnp.asarray(near_mask)[me][owner_ids])
    band_ids = jnp.arange(band_count, dtype=jnp.int32)
    slot_range = jnp.arange(capacity, dtype=jnp.int32)
    matches = (owner_ids[:, None, None] == band_ids[None, :, None]) & (
        slot_ids[:, None, None] == slot_range[None, None, :]
    )
    request = jnp.sum(jnp.where(matches, source[:, None, None], 0), axis=0)
    flag = jnp.broadcast_to(outside, (band_count, 1)).astype(jnp.int32)
    message = jnp.concatenate([request, flag], axis=1)
    wanted = lax.all_to_all(message, "lat", split_axis=0, concat_axis=0, tiled=True)
    covered = jnp.all(wanted[:, capacity] == 0)
    weights = dep_weight.reshape(entries)
    row_range = jnp.arange(row_count, dtype=jnp.int32)
    target_rows = positions // link_count
    own = jnp.where((owner_ids == me)[:, None] & (source[:, None] == row_range[None, :]),
                    weights[:, None], 0.0)
    own_weights = jnp.zeros((row_count, row_count), jnp.float32).at[target_rows].add(own)
    total = jnp.einsum("jr,flri->flji", own_weights, tracers, precision=PRECISE)
    for offset in offsets:
        pairs = [
            (band + offset, band)
            for band in range(band_count)
            if (band + offset) in nearest[band] and band + offset != band
        ]
        receiver = jnp.clip(me - offset, 0, band_count - 1)
        chosen = wanted[receiver, :capacity]
        select = (chosen[:, None] == row_range[None, :]).astype(jnp.float32)
        outgoing = jnp.einsum("sr,flri->flsi", select, tracers, precision=PRECISE)
        incoming = lax.ppermute(outgoing, "lat", pairs)
        hit = (owner_ids == me + offset)[:, None] & (slot_ids[:, None] == slot_range[None, :])
        part = jnp.where(hit, weights[:, None], 0.0)
        part_weights = jnp.zeros((row_count, capacity), jnp.float32).at[target_rows].add(part)
        total = total + jnp.einsum("js,flsi->flji", part_weights, incoming, precision=PRECISE)
    return total, covered


def departure_all(tracers, dep_owner, dep_row, dep_weight):
    band_count = lax.axis_size("lat")
    row_count, link_count = dep_owner.shape
    entries = row_count * link_count
    capacity = max(2, -(-2 * entries // band_count))
    nearest, offsets = near_plan(band_count, entries, capacity)
    near, covered = departure_near(
        tracers, dep_owner, dep_row, dep_weight, nearest, offsets, capacity
    )
    return lax.cond(
        covered,
        lambda: near,
        lambda: departure_terms(tracers, dep_owner, dep_row, dep_weight),
    )


def body(
    prognostic,
    tracers,
    zonal_courant,
    meridional_courant,
    filter_band,
    dep_owner,
    dep_row,
    dep_weight,
):
    row_count = prognostic.shape[2]
    departed = departure_all(tracers, dep_owner, dep_row, dep_weight)
    lon_padded = padded(
        jnp.concatenate([prognostic, zonal_courant[None]], axis=0), (("lon", 3),), 1, True
    )
    zonal_flux = face_flux(lon_padded[:-1], lon_padded[-1:], 3)
    lat_padded = padded(
        jnp.concatenate([prognostic, meridional_courant[None]], axis=0), (("lat", 2),), 1, False
    )
    merid_flux = face_flux(lat_padded[:-1], lat_padded[-1:], 2)
    total_rows = row_count * lax.axis_size("lat")
    face_rows = lax.axis_index("lat") * row_count + jnp.arange(row_count + 1) - 1
    merid_flux = jnp.where(
        (face_rows == total_rows - 1)[None, None, :, None], jnp.float32(0.0), merid_flux
    )
    advected = (
        prognostic
        - (zonal_flux[..., 1:] - zonal_flux[..., :-1])
        - (merid_flux[:, :, 1:] - merid_flux[:, :, :-1])
    )
    new_prognostic = polar_filter(advected, filter_band)
    return (new_prognostic, departed)


def solution(mesh):
    return jax.shard_map(
        body,
        mesh=mesh,
        in_specs=(
            P(None, None, "lat", "lon"),
            P(None, None, "lat", "lon"),
            P(None, "lat", "lon"),
            P(None, "lat", "lon"),
            P("lat"),
            P("lat", None),
            P("lat", None),
            P("lat", None),
        ),
        out_specs=(P(None, None, "lat", "lon"), P(None, None, "lat", "lon")),
        check_vma=False,
    )
```

```python
import math

import jax
import numpy as np
import jax.numpy as jnp
from jax import lax
from jax.sharding import PartitionSpec as P

PRECISE = lax.Precision.HIGHEST


def padded(value, sides, width, wrap):
    for axis, dim in sides:
        size, length = (lax.axis_size(axis), value.shape[dim])
        up = [(i, (i + 1) % size) for i in range(size if wrap else size - 1)]
        down = [(j, i) for i, j in up]
        last = lax.slice_in_dim(value, length - width, length, axis=dim)
        first = lax.slice_in_dim(value, 0, width, axis=dim)
        before = lax.ppermute(last, axis, up)
        after = lax.ppermute(first, axis, down)
        value = jnp.concatenate([before, value, after], axis=dim)
    return value


def face_flux(values, speeds, axis):
    count = values.shape[axis] - 2
    left_cells = lax.slice_in_dim(values, 0, count + 1, axis=axis)
    right_cells = lax.slice_in_dim(values, 1, count + 2, axis=axis)
    courant = lax.slice_in_dim(speeds, 0, count + 1, axis=axis)
    return 0.5 * courant * (left_cells + right_cells) - 0.5 * courant * courant * (
        right_cells - left_cells
    )


def column_factors(band_rows, length):
    column = jnp.arange(length, dtype=jnp.int32)
    half_length = length // 2
    frequency = jnp.where(column <= half_length, column, column - half_length)
    single = (column == 0) | (column == half_length)
    weights = jnp.where(single, 1.0 / length, 2.0 / length).astype(jnp.float32)
    ratios = (
        band_rows.astype(jnp.float32)[:, None]
        / jnp.maximum(frequency, 1).astype(jnp.float32)[None, :]
    )
    damping = jnp.minimum(1.0, ratios * ratios)
    return (damping - 1.0) * weights[None, :]


def column_factors(band_rows, length):
    column = jnp.arange(length, dtype=jnp.int32)
    half_length = length // 2
    frequency = jnp.where(column <= half_length, column, column - half_length)
    single = (column == 0) | (column == half_length)
    weights = jnp.where(single, 1.0 / length, 2.0 / length).astype(jnp.float32)
    ratios = (
        band_rows.astype(jnp.float32)[:, None]
        / jnp.maximum(frequency, 1).astype(jnp.float32)[None, :]
    )
    damping = jnp.minimum(1.0, ratios * ratios)
    return (damping - 1.0) * weights[None, :]


def circle_basis(length):
    half_length = length // 2
    column = jnp.arange(length, dtype=jnp.int32)
    frequency = jnp.where(column <= half_length, column, column - half_length)
    low_count = 64
    high_count = length // low_count
    low = jnp.arange(low_count, dtype=jnp.int32)
    high = jnp.arange(high_count, dtype=jnp.int32) * low_count
    scale = 2.0 * math.pi / length
    low_angle = scale * (low[:, None] * frequency[None, :] % length).astype(jnp.float32)
    high_angle = scale * (high[:, None] * frequency[None, :] % length).astype(jnp.float32)
    low_cos, low_sin = jnp.cos(low_angle), jnp.sin(low_angle)
    high_cos, high_sin = jnp.cos(high_angle), jnp.sin(high_angle)
    cos_part = high_cos[:, None] * low_cos[None] - high_sin[:, None] * low_sin[None]
    sin_part = high_sin[:, None] * low_cos[None] + high_cos[:, None] * low_sin[None]
    basis = jnp.where((column <= half_length)[None, None, :], cos_part, sin_part)
    return basis.reshape(length, length)


def departure_terms(tracers, dep_owner, dep_row, dep_weight):
    band_count = lax.axis_size("lat")
    row_count, link_count = dep_owner.shape
    entries = row_count * link_count
    capacity = max(2, -(-2 * entries // band_count))
    owner_ids = dep_owner.reshape(entries)
    source = dep_row.reshape(entries)
    positions = jnp.arange(entries)
    earlier = (owner_ids[:, None] == owner_ids[None, :]) & (positions[None, :] < positions[:, None])
    slot_ids = jnp.sum(earlier.astype(jnp.int32), axis=1)
    band_ids = jnp.arange(band_count, dtype=jnp.int32)
    slot_range = jnp.arange(capacity, dtype=jnp.int32)
    matches = (owner_ids[:, None, None] == band_ids[None, :, None]) & (
        slot_ids[:, None, None] == slot_range[None, None, :]
    )
    request = jnp.sum(jnp.where(matches, source[:, None, None], 0), axis=0)
    wanted = lax.all_to_all(request, "lat", split_axis=0, concat_axis=0, tiled=True)
    by_row = jnp.transpose(tracers, (2, 0, 1, 3))
    outgoing = by_row[wanted]
    incoming = lax.all_to_all(outgoing, "lat", split_axis=0, concat_axis=0, tiled=True)
    stacked_rows = incoming.reshape((band_count * capacity,) + incoming.shape[2:])
    picked = stacked_rows[owner_ids * capacity + slot_ids].reshape(
        (row_count, link_count) + stacked_rows.shape[1:]
    )
    summed = dep_weight[:, 0][:, None, None, None] * picked[:, 0]
    summed = summed + dep_weight[:, 1][:, None, None, None] * picked[:, 1]
    return jnp.transpose(summed, (1, 2, 0, 3))


def circle_basis(cells, length):
    half_length = length // 2
    column = jnp.arange(length, dtype=jnp.int32)
    frequency = jnp.where(column <= half_length, column, column - half_length)
    low_count = math.gcd(cells.shape[0], 64)
    low = jnp.arange(low_count, dtype=jnp.int32)
    high = cells.reshape(-1, low_count)[:, 0]
    scale = 2.0 * math.pi / length
    low_angle = scale * (low[:, None] * frequency[None, :] % length).astype(jnp.float32)
    high_angle = scale * (high[:, None] * frequency[None, :] % length).astype(jnp.float32)
    low_cos, low_sin = jnp.cos(low_angle), jnp.sin(low_angle)
    high_cos, high_sin = jnp.cos(high_angle), jnp.sin(high_angle)
    cos_part = high_cos[:, None] * low_cos[None] - high_sin[:, None] * low_sin[None]
    sin_part = high_sin[:, None] * low_cos[None] + high_cos[:, None] * low_sin[None]
    basis = jnp.where((column <= half_length)[None, None, :], cos_part, sin_part)
    return basis.reshape(cells.shape[0], length)


def polar_filter(values, band_rows):
    fields, levels, rows, block_cells = values.shape
    parts = lax.axis_size("lon")
    me = lax.axis_index("lon")
    length = block_cells * parts
    flat = values.reshape(fields * levels * rows, block_cells)
    chunk = flat.shape[0] // parts
    blocks = [lax.dynamic_slice_in_dim(flat, me * chunk, chunk, axis=0)]
    for shift in range(1, parts):
        target = (me + shift) % parts
        piece = lax.dynamic_slice_in_dim(flat, target * chunk, chunk, axis=0)
        pairs = [(i, (i + shift) % parts) for i in range(parts)]
        blocks.append(lax.ppermute(piece, "lon", pairs))
    circles = jnp.concatenate(blocks, axis=1)
    shifts = jnp.arange(parts, dtype=jnp.int32)
    sources = (me - shifts) % parts
    cells = (sources[:, None] * block_cells + jnp.arange(block_cells, dtype=jnp.int32)[None]).reshape(length)
    basis_table = circle_basis(cells, length)
    spectrum = jnp.dot(circles, basis_table, precision=lax.Precision.HIGH)
    factors = column_factors(band_rows, length)
    scaled = (spectrum.reshape(chunk // rows, rows, length) * factors[None]).reshape(chunk, length)
    change = lax.dot_general(
        scaled, basis_table, (((1,), (1,)), ((), ())), precision=lax.Precision.HIGH
    )
    returned = [change[:, :block_cells]]
    for shift in range(1, parts):
        pairs = [(i, (i - shift) % parts) for i in range(parts)]
        piece = change[:, shift * block_cells:(shift + 1) * block_cells]
        returned.append(lax.ppermute(piece, "lon", pairs))
    stacked = jnp.stack(returned, axis=0)
    order = (jnp.arange(parts, dtype=jnp.int32) - me) % parts
    ordered = jnp.take(stacked, order, axis=0)
    return values + ordered.reshape(values.shape)


def band_distance(a, b, band_count):
    return min(abs(a - b), a + b + 1, 2 * band_count - 1 - a - b)


def near_plan(band_count, entries, capacity):
    reach = min(band_count, -(-entries // capacity) + 1)
    nearest = []
    for band in range(band_count):
        order = sorted(range(band_count), key=lambda o: (band_distance(band, o, band_count), o))
        nearest.append(order[:reach])
    offsets = sorted({o - b for b in range(band_count) for o in nearest[b] if o != b})
    return nearest, offsets


def departure_near(tracers, dep_owner, dep_row, dep_weight, nearest, offsets, capacity):
    band_count = lax.axis_size("lat")
    row_count, link_count = dep_owner.shape
    entries = row_count * link_count
    me = lax.axis_index("lat")
    owner_ids = dep_owner.reshape(entries)
    source = dep_row.reshape(entries)
    positions = jnp.arange(entries)
    earlier = (owner_ids[:, None] == owner_ids[None, :]) & (positions[None, :] < positions[:, None])
    slot_ids = jnp.sum(earlier.astype(jnp.int32), axis=1)
    near_mask = np.zeros((band_count, band_count), np.int32)
    for band in range(band_count):
        near_mask[band, nearest[band]] = 1
    outside = jnp.sum(1 - jnp.asarray(near_mask)[me][owner_ids])
    band_ids = jnp.arange(band_count, dtype=jnp.int32)
    slot_range = jnp.arange(capacity, dtype=jnp.int32)
    matches = (owner_ids[:, None, None] == band_ids[None, :, None]) & (
        slot_ids[:, None, None] == slot_range[None, None, :]
    )
    request = jnp.sum(jnp.where(matches, source[:, None, None], 0), axis=0)
    flag = jnp.broadcast_to(outside, (band_count, 1)).astype(jnp.int32)
    message = jnp.concatenate([request, flag], axis=1)
    wanted = lax.all_to_all(message, "lat", split_axis=0, concat_axis=0, tiled=True)
    covered = jnp.all(wanted[:, capacity] == 0)
    weights = dep_weight.reshape(entries)
    row_range = jnp.arange(row_count, dtype=jnp.int32)
    target_rows = positions // link_count
    own = jnp.where((owner_ids == me)[:, None] & (source[:, None] == row_range[None, :]),
                    weights[:, None], 0.0)
    own_weights = jnp.zeros((row_count, row_count), jnp.float32).at[target_rows].add(own)
    receivers = jnp.clip(me - jnp.asarray(offsets, jnp.int32), 0, band_count - 1)
    chosen = wanted[receivers, :capacity]
    select = (chosen[:, :, None] == row_range[None, None, :]).astype(jnp.float32)
    outgoing = jnp.einsum("osr,flri->oflsi", select, tracers, precision=PRECISE)
    incoming = []
    for index, offset in enumerate(offsets):
        pairs = [
            (band + offset, band)
            for band in range(band_count)
            if (band + offset) in nearest[band] and band + offset != band
        ]
        incoming.append(lax.ppermute(outgoing[index], "lat", pairs))
    incoming = jnp.stack(incoming, axis=0)
    owners_near = me + jnp.asarray(offsets, jnp.int32)
    hit = (owner_ids[None, :, None] == owners_near[:, None, None]) & (
        slot_ids[None, :, None] == slot_range[None, None, :]
    )
    part = jnp.where(hit, weights[None, :, None], 0.0)
    part_weights = jnp.zeros((len(offsets), row_count, capacity), jnp.float32).at[:, target_rows].add(part)
    total = jnp.einsum("jr,flri->flji", own_weights, tracers, precision=PRECISE)
    total = total + jnp.einsum("ojs,oflsi->flji", part_weights, incoming, precision=PRECISE)
    return total, covered


def departure_all(tracers, dep_owner, dep_row, dep_weight):
    band_count = lax.axis_size("lat")
    row_count, link_count = dep_owner.shape
    entries = row_count * link_count
    capacity = max(2, -(-2 * entries // band_count))
    nearest, offsets = near_plan(band_count, entries, capacity)
    near, covered = departure_near(
        tracers, dep_owner, dep_row, dep_weight, nearest, offsets, capacity
    )
    return lax.cond(
        covered,
        lambda: near,
        lambda: departure_terms(tracers, dep_owner, dep_row, dep_weight),
    )


def body(
    prognostic,
    tracers,
    zonal_courant,
    meridional_courant,
    filter_band,
    dep_owner,
    dep_row,
    dep_weight,
):
    row_count = prognostic.shape[2]
    departed = departure_all(tracers, dep_owner, dep_row, dep_weight)
    lon_padded = padded(
        jnp.concatenate([prognostic, zonal_courant[None]], axis=0), (("lon", 3),), 1, True
    )
    zonal_flux = face_flux(lon_padded[:-1], lon_padded[-1:], 3)
    lat_padded = padded(
        jnp.concatenate([prognostic, meridional_courant[None]], axis=0), (("lat", 2),), 1, False
    )
    merid_flux = face_flux(lat_padded[:-1], lat_padded[-1:], 2)
    total_rows = row_count * lax.axis_size("lat")
    face_rows = lax.axis_index("lat") * row_count + jnp.arange(row_count + 1) - 1
    merid_flux = jnp.where(
        (face_rows == total_rows - 1)[None, None, :, None], jnp.float32(0.0), merid_flux
    )
    advected = (
        prognostic
        - (zonal_flux[..., 1:] - zonal_flux[..., :-1])
        - (merid_flux[:, :, 1:] - merid_flux[:, :, :-1])
    )
    new_prognostic = polar_filter(advected, filter_band)
    return (new_prognostic, departed)


def solution(mesh):
    return jax.shard_map(
        body,
        mesh=mesh,
        in_specs=(
            P(None, None, "lat", "lon"),
            P(None, None, "lat", "lon"),
            P(None, "lat", "lon"),
            P(None, "lat", "lon"),
            P("lat"),
            P("lat", None),
            P("lat", None),
            P("lat", None),
        ),
        out_specs=(P(None, None, "lat", "lon"), P(None, None, "lat", "lon")),
        check_vma=False,
    )
```

```python
import math

import jax
import numpy as np
import jax.numpy as jnp
from jax import lax
from jax.sharding import PartitionSpec as P

PRECISE = lax.Precision.HIGHEST


def padded(value, sides, width, wrap):
    for axis, dim in sides:
        size, length = (lax.axis_size(axis), value.shape[dim])
        up = [(i, (i + 1) % size) for i in range(size if wrap else size - 1)]
        down = [(j, i) for i, j in up]
        last = lax.slice_in_dim(value, length - width, length, axis=dim)
        first = lax.slice_in_dim(value, 0, width, axis=dim)
        before = lax.ppermute(last, axis, up)
        after = lax.ppermute(first, axis, down)
        value = jnp.concatenate([before, value, after], axis=dim)
    return value


def face_flux(values, speeds, axis):
    count = values.shape[axis] - 2
    left_cells = lax.slice_in_dim(values, 0, count + 1, axis=axis)
    right_cells = lax.slice_in_dim(values, 1, count + 2, axis=axis)
    courant = lax.slice_in_dim(speeds, 0, count + 1, axis=axis)
    return 0.5 * courant * (left_cells + right_cells) - 0.5 * courant * courant * (
        right_cells - left_cells
    )


def column_factors(band_rows, length):
    column = jnp.arange(length, dtype=jnp.int32)
    half_length = length // 2
    frequency = jnp.where(column <= half_length, column, column - half_length)
    single = (column == 0) | (column == half_length)
    weights = jnp.where(single, 1.0 / length, 2.0 / length).astype(jnp.float32)
    ratios = (
        band_rows.astype(jnp.float32)[:, None]
        / jnp.maximum(frequency, 1).astype(jnp.float32)[None, :]
    )
    damping = jnp.minimum(1.0, ratios * ratios)
    return (damping - 1.0) * weights[None, :]


def column_factors(band_rows, length):
    column = jnp.arange(length, dtype=jnp.int32)
    half_length = length // 2
    frequency = jnp.where(column <= half_length, column, column - half_length)
    single = (column == 0) | (column == half_length)
    weights = jnp.where(single, 1.0 / length, 2.0 / length).astype(jnp.float32)
    ratios = (
        band_rows.astype(jnp.float32)[:, None]
        / jnp.maximum(frequency, 1).astype(jnp.float32)[None, :]
    )
    damping = jnp.minimum(1.0, ratios * ratios)
    return (damping - 1.0) * weights[None, :]


def circle_basis(length):
    half_length = length // 2
    column = jnp.arange(length, dtype=jnp.int32)
    frequency = jnp.where(column <= half_length, column, column - half_length)
    low_count = 64
    high_count = length // low_count
    low = jnp.arange(low_count, dtype=jnp.int32)
    high = jnp.arange(high_count, dtype=jnp.int32) * low_count
    scale = 2.0 * math.pi / length
    low_angle = scale * (low[:, None] * frequency[None, :] % length).astype(jnp.float32)
    high_angle = scale * (high[:, None] * frequency[None, :] % length).astype(jnp.float32)
    low_cos, low_sin = jnp.cos(low_angle), jnp.sin(low_angle)
    high_cos, high_sin = jnp.cos(high_angle), jnp.sin(high_angle)
    cos_part = high_cos[:, None] * low_cos[None] - high_sin[:, None] * low_sin[None]
    sin_part = high_sin[:, None] * low_cos[None] + high_cos[:, None] * low_sin[None]
    basis = jnp.where((column <= half_length)[None, None, :], cos_part, sin_part)
    return basis.reshape(length, length)


def departure_terms(tracers, dep_owner, dep_row, dep_weight):
    band_count = lax.axis_size("lat")
    row_count, link_count = dep_owner.shape
    entries = row_count * link_count
    capacity = max(2, -(-2 * entries // band_count))
    owner_ids = dep_owner.reshape(entries)
    source = dep_row.reshape(entries)
    positions = jnp.arange(entries)
    earlier = (owner_ids[:, None] == owner_ids[None, :]) & (positions[None, :] < positions[:, None])
    slot_ids = jnp.sum(earlier.astype(jnp.int32), axis=1)
    band_ids = jnp.arange(band_count, dtype=jnp.int32)
    slot_range = jnp.arange(capacity, dtype=jnp.int32)
    matches = (owner_ids[:, None, None] == band_ids[None, :, None]) & (
        slot_ids[:, None, None] == slot_range[None, None, :]
    )
    request = jnp.sum(jnp.where(matches, source[:, None, None], 0), axis=0)
    wanted = lax.all_to_all(request, "lat", split_axis=0, concat_axis=0, tiled=True)
    by_row = jnp.transpose(tracers, (2, 0, 1, 3))
    outgoing = by_row[wanted]
    incoming = lax.all_to_all(outgoing, "lat", split_axis=0, concat_axis=0, tiled=True)
    stacked_rows = incoming.reshape((band_count * capacity,) + incoming.shape[2:])
    picked = stacked_rows[owner_ids * capacity + slot_ids].reshape(
        (row_count, link_count) + stacked_rows.shape[1:]
    )
    summed = dep_weight[:, 0][:, None, None, None] * picked[:, 0]
    summed = summed + dep_weight[:, 1][:, None, None, None] * picked[:, 1]
    return jnp.transpose(summed, (1, 2, 0, 3))


def circle_basis(cells, length):
    half_length = length // 2
    column = jnp.arange(length, dtype=jnp.int32)
    frequency = jnp.where(column <= half_length, column, column - half_length)
    low_count = math.gcd(cells.shape[0], 64)
    low = jnp.arange(low_count, dtype=jnp.int32)
    high = cells.reshape(-1, low_count)[:, 0]
    scale = 2.0 * math.pi / length
    low_angle = scale * (low[:, None] * frequency[None, :] % length).astype(jnp.float32)
    high_angle = scale * (high[:, None] * frequency[None, :] % length).astype(jnp.float32)
    low_cos, low_sin = jnp.cos(low_angle), jnp.sin(low_angle)
    high_cos, high_sin = jnp.cos(high_angle), jnp.sin(high_angle)
    cos_part = high_cos[:, None] * low_cos[None] - high_sin[:, None] * low_sin[None]
    sin_part = high_sin[:, None] * low_cos[None] + high_cos[:, None] * low_sin[None]
    basis = jnp.where((column <= half_length)[None, None, :], cos_part, sin_part)
    return basis.reshape(cells.shape[0], length)


def polar_filter(values, band_rows):
    fields, levels, rows, block_cells = values.shape
    parts = lax.axis_size("lon")
    me = lax.axis_index("lon")
    length = block_cells * parts
    flat = values.reshape(fields * levels * rows, block_cells)
    chunk = flat.shape[0] // parts
    blocks = [lax.dynamic_slice_in_dim(flat, me * chunk, chunk, axis=0)]
    for shift in range(1, parts):
        target = (me + shift) % parts
        piece = lax.dynamic_slice_in_dim(flat, target * chunk, chunk, axis=0)
        pairs = [(i, (i + shift) % parts) for i in range(parts)]
        blocks.append(lax.ppermute(piece, "lon", pairs))
    circles = jnp.concatenate(blocks, axis=1)
    shifts = jnp.arange(parts, dtype=jnp.int32)
    sources = (me - shifts) % parts
    cells = (sources[:, None] * block_cells + jnp.arange(block_cells, dtype=jnp.int32)[None]).reshape(length)
    basis_table = circle_basis(cells, length)
    spectrum = jnp.dot(circles, basis_table, precision=lax.Precision.HIGH)
    factors = column_factors(band_rows, length)
    scaled = (spectrum.reshape(chunk // rows, rows, length) * factors[None]).reshape(chunk, length)
    change = lax.dot_general(
        scaled, basis_table, (((1,), (1,)), ((), ())), precision=lax.Precision.HIGH
    )
    returned = [change[:, :block_cells]]
    for shift in range(1, parts):
        pairs = [(i, (i - shift) % parts) for i in range(parts)]
        piece = change[:, shift * block_cells:(shift + 1) * block_cells]
        returned.append(lax.ppermute(piece, "lon", pairs))
    stacked = jnp.stack(returned, axis=0)
    order = (jnp.arange(parts, dtype=jnp.int32) - me) % parts
    ordered = jnp.take(stacked, order, axis=0)
    return values + ordered.reshape(values.shape)


def band_distance(a, b, band_count):
    return min(abs(a - b), a + b + 1, 2 * band_count - 1 - a - b)


def near_plan(band_count, entries, capacity):
    reach = min(band_count, -(-entries // capacity) + 1)
    nearest = []
    for band in range(band_count):
        order = sorted(range(band_count), key=lambda o: (band_distance(band, o, band_count), o))
        nearest.append(order[:reach])
    offsets = sorted({o - b for b in range(band_count) for o in nearest[b] if o != b})
    return nearest, offsets


def departure_near(tracers, dep_owner, dep_row, dep_weight, nearest, offsets, capacity):
    band_count = lax.axis_size("lat")
    row_count, link_count = dep_owner.shape
    entries = row_count * link_count
    me = lax.axis_index("lat")
    owner_ids = dep_owner.reshape(entries)
    source = dep_row.reshape(entries)
    positions = jnp.arange(entries)
    earlier = (owner_ids[:, None] == owner_ids[None, :]) & (positions[None, :] < positions[:, None])
    slot_ids = jnp.sum(earlier.astype(jnp.int32), axis=1)
    near_mask = np.zeros((band_count, band_count), np.int32)
    for band in range(band_count):
        near_mask[band, nearest[band]] = 1
    outside = jnp.sum(1 - jnp.asarray(near_mask)[me][owner_ids])
    band_ids = jnp.arange(band_count, dtype=jnp.int32)
    slot_range = jnp.arange(capacity, dtype=jnp.int32)
    matches = (owner_ids[:, None, None] == band_ids[None, :, None]) & (
        slot_ids[:, None, None] == slot_range[None, None, :]
    )
    request = jnp.sum(jnp.where(matches, source[:, None, None], 0), axis=0)
    flag = jnp.broadcast_to(outside, (band_count, 1)).astype(jnp.int32)
    message = jnp.concatenate([request, flag], axis=1)
    wanted = lax.all_to_all(message, "lat", split_axis=0, concat_axis=0, tiled=True)
    covered = jnp.all(wanted[:, capacity] == 0)
    weights = dep_weight.reshape(entries)
    row_range = jnp.arange(row_count, dtype=jnp.int32)
    own = jnp.where((owner_ids == me)[:, None] & (source[:, None] == row_range[None, :]),
                    weights[:, None], 0.0)
    own_weights = jnp.sum(own.reshape(row_count, link_count, row_count), axis=1)
    incoming = []
    for offset in offsets:
        pairs = [
            (band + offset, band)
            for band in range(band_count)
            if (band + offset) in nearest[band] and band + offset != band
        ]
        receiver = jnp.clip(me - offset, 0, band_count - 1)
        chosen = wanted[receiver, :capacity]
        select = (chosen[:, None] == row_range[None, :]).astype(jnp.float32)
        outgoing = jnp.einsum("sr,flri->flsi", select, tracers, precision=PRECISE)
        incoming.append(lax.ppermute(outgoing, "lat", pairs))
    incoming = jnp.stack(incoming, axis=0)
    owners_near = me + jnp.asarray(offsets, jnp.int32)
    hit = (owner_ids[None, :, None] == owners_near[:, None, None]) & (
        slot_ids[None, :, None] == slot_range[None, None, :]
    )
    part = jnp.where(hit, weights[None, :, None], 0.0)
    part_weights = jnp.sum(part.reshape(len(offsets), row_count, link_count, capacity), axis=2)
    total = jnp.einsum("jr,flri->flji", own_weights, tracers, precision=PRECISE)
    total = total + jnp.einsum("ojs,oflsi->flji", part_weights, incoming, precision=PRECISE)
    return total, covered


def departure_all(tracers, dep_owner, dep_row, dep_weight):
    band_count = lax.axis_size("lat")
    row_count, link_count = dep_owner.shape
    entries = row_count * link_count
    capacity = max(2, -(-2 * entries // band_count))
    nearest, offsets = near_plan(band_count, entries, capacity)
    near, covered = departure_near(
        tracers, dep_owner, dep_row, dep_weight, nearest, offsets, capacity
    )
    return lax.cond(
        covered,
        lambda: near,
        lambda: departure_terms(tracers, dep_owner, dep_row, dep_weight),
    )


def body(
    prognostic,
    tracers,
    zonal_courant,
    meridional_courant,
    filter_band,
    dep_owner,
    dep_row,
    dep_weight,
):
    row_count = prognostic.shape[2]
    departed = departure_all(tracers, dep_owner, dep_row, dep_weight)
    lon_padded = padded(
        jnp.concatenate([prognostic, zonal_courant[None]], axis=0), (("lon", 3),), 1, True
    )
    zonal_flux = face_flux(lon_padded[:-1], lon_padded[-1:], 3)
    lat_padded = padded(
        jnp.concatenate([prognostic, meridional_courant[None]], axis=0), (("lat", 2),), 1, False
    )
    merid_flux = face_flux(lat_padded[:-1], lat_padded[-1:], 2)
    total_rows = row_count * lax.axis_size("lat")
    face_rows = lax.axis_index("lat") * row_count + jnp.arange(row_count + 1) - 1
    merid_flux = jnp.where(
        (face_rows == total_rows - 1)[None, None, :, None], jnp.float32(0.0), merid_flux
    )
    advected = (
        prognostic
        - (zonal_flux[..., 1:] - zonal_flux[..., :-1])
        - (merid_flux[:, :, 1:] - merid_flux[:, :, :-1])
    )
    new_prognostic = polar_filter(advected, filter_band)
    return (new_prognostic, departed)


def solution(mesh):
    return jax.shard_map(
        body,
        mesh=mesh,
        in_specs=(
            P(None, None, "lat", "lon"),
            P(None, None, "lat", "lon"),
            P(None, "lat", "lon"),
            P(None, "lat", "lon"),
            P("lat"),
            P("lat", None),
            P("lat", None),
            P("lat", None),
        ),
        out_specs=(P(None, None, "lat", "lon"), P(None, None, "lat", "lon")),
        check_vma=False,
    )
```

```python
import math

import jax
import numpy as np
import jax.numpy as jnp
from jax import lax
from jax.sharding import PartitionSpec as P

PRECISE = lax.Precision.HIGHEST


def padded(value, sides, width, wrap):
    for axis, dim in sides:
        size, length = (lax.axis_size(axis), value.shape[dim])
        up = [(i, (i + 1) % size) for i in range(size if wrap else size - 1)]
        down = [(j, i) for i, j in up]
        last = lax.slice_in_dim(value, length - width, length, axis=dim)
        first = lax.slice_in_dim(value, 0, width, axis=dim)
        before = lax.ppermute(last, axis, up)
        after = lax.ppermute(first, axis, down)
        value = jnp.concatenate([before, value, after], axis=dim)
    return value


def face_flux(values, speeds, axis):
    count = values.shape[axis] - 2
    left_cells = lax.slice_in_dim(values, 0, count + 1, axis=axis)
    right_cells = lax.slice_in_dim(values, 1, count + 2, axis=axis)
    courant = lax.slice_in_dim(speeds, 0, count + 1, axis=axis)
    return 0.5 * courant * (left_cells + right_cells) - 0.5 * courant * courant * (
        right_cells - left_cells
    )


def column_factors(band_rows, length):
    column = jnp.arange(length, dtype=jnp.int32)
    half_length = length // 2
    frequency = jnp.where(column <= half_length, column, column - half_length)
    single = (column == 0) | (column == half_length)
    weights = jnp.where(single, 1.0 / length, 2.0 / length).astype(jnp.float32)
    ratios = (
        band_rows.astype(jnp.float32)[:, None]
        / jnp.maximum(frequency, 1).astype(jnp.float32)[None, :]
    )
    damping = jnp.minimum(1.0, ratios * ratios)
    return (damping - 1.0) * weights[None, :]


def column_factors(band_rows, length):
    column = jnp.arange(length, dtype=jnp.int32)
    half_length = length // 2
    frequency = jnp.where(column <= half_length, column, column - half_length)
    single = (column == 0) | (column == half_length)
    weights = jnp.where(single, 1.0 / length, 2.0 / length).astype(jnp.float32)
    ratios = (
        band_rows.astype(jnp.float32)[:, None]
        / jnp.maximum(frequency, 1).astype(jnp.float32)[None, :]
    )
    damping = jnp.minimum(1.0, ratios * ratios)
    return (damping - 1.0) * weights[None, :]


def circle_basis(length):
    half_length = length // 2
    column = jnp.arange(length, dtype=jnp.int32)
    frequency = jnp.where(column <= half_length, column, column - half_length)
    low_count = 64
    high_count = length // low_count
    low = jnp.arange(low_count, dtype=jnp.int32)
    high = jnp.arange(high_count, dtype=jnp.int32) * low_count
    scale = 2.0 * math.pi / length
    low_angle = scale * (low[:, None] * frequency[None, :] % length).astype(jnp.float32)
    high_angle = scale * (high[:, None] * frequency[None, :] % length).astype(jnp.float32)
    low_cos, low_sin = jnp.cos(low_angle), jnp.sin(low_angle)
    high_cos, high_sin = jnp.cos(high_angle), jnp.sin(high_angle)
    cos_part = high_cos[:, None] * low_cos[None] - high_sin[:, None] * low_sin[None]
    sin_part = high_sin[:, None] * low_cos[None] + high_cos[:, None] * low_sin[None]
    basis = jnp.where((column <= half_length)[None, None, :], cos_part, sin_part)
    return basis.reshape(length, length)


def departure_terms(tracers, dep_owner, dep_row, dep_weight):
    band_count = lax.axis_size("lat")
    row_count, link_count = dep_owner.shape
    entries = row_count * link_count
    capacity = max(2, -(-2 * entries // band_count))
    owner_ids = dep_owner.reshape(entries)
    source = dep_row.reshape(entries)
    positions = jnp.arange(entries)
    earlier = (owner_ids[:, None] == owner_ids[None, :]) & (positions[None, :] < positions[:, None])
    slot_ids = jnp.sum(earlier.astype(jnp.int32), axis=1)
    band_ids = jnp.arange(band_count, dtype=jnp.int32)
    slot_range = jnp.arange(capacity, dtype=jnp.int32)
    matches = (owner_ids[:, None, None] == band_ids[None, :, None]) & (
        slot_ids[:, None, None] == slot_range[None, None, :]
    )
    request = jnp.sum(jnp.where(matches, source[:, None, None], 0), axis=0)
    wanted = lax.all_to_all(request, "lat", split_axis=0, concat_axis=0, tiled=True)
    by_row = jnp.transpose(tracers, (2, 0, 1, 3))
    outgoing = by_row[wanted]
    incoming = lax.all_to_all(outgoing, "lat", split_axis=0, concat_axis=0, tiled=True)
    stacked_rows = incoming.reshape((band_count * capacity,) + incoming.shape[2:])
    picked = stacked_rows[owner_ids * capacity + slot_ids].reshape(
        (row_count, link_count) + stacked_rows.shape[1:]
    )
    summed = dep_weight[:, 0][:, None, None, None] * picked[:, 0]
    summed = summed + dep_weight[:, 1][:, None, None, None] * picked[:, 1]
    return jnp.transpose(summed, (1, 2, 0, 3))


def circle_basis(cells, length):
    half_length = length // 2
    column = jnp.arange(length, dtype=jnp.int32)
    frequency = jnp.where(column <= half_length, column, column - half_length)
    low_count = math.gcd(cells.shape[0], 64)
    low = jnp.arange(low_count, dtype=jnp.int32)
    high = cells.reshape(-1, low_count)[:, 0]
    scale = 2.0 * math.pi / length
    low_angle = scale * (low[:, None] * frequency[None, :] % length).astype(jnp.float32)
    high_angle = scale * (high[:, None] * frequency[None, :] % length).astype(jnp.float32)
    low_cos, low_sin = jnp.cos(low_angle), jnp.sin(low_angle)
    high_cos, high_sin = jnp.cos(high_angle), jnp.sin(high_angle)
    cos_part = high_cos[:, None] * low_cos[None] - high_sin[:, None] * low_sin[None]
    sin_part = high_sin[:, None] * low_cos[None] + high_cos[:, None] * low_sin[None]
    basis = jnp.where((column <= half_length)[None, None, :], cos_part, sin_part)
    return basis.reshape(cells.shape[0], length)


def polar_filter(values, band_rows):
    fields, levels, rows, block_cells = values.shape
    parts = lax.axis_size("lon")
    me = lax.axis_index("lon")
    length = block_cells * parts
    flat = values.reshape(fields * levels * rows, block_cells)
    chunk = flat.shape[0] // parts
    blocks = [lax.dynamic_slice_in_dim(flat, me * chunk, chunk, axis=0)]
    for shift in range(1, parts):
        target = (me + shift) % parts
        piece = lax.dynamic_slice_in_dim(flat, target * chunk, chunk, axis=0)
        pairs = [(i, (i + shift) % parts) for i in range(parts)]
        blocks.append(lax.ppermute(piece, "lon", pairs))
    circles = jnp.concatenate(blocks, axis=1)
    shifts = jnp.arange(parts, dtype=jnp.int32)
    sources = (me - shifts) % parts
    cells = (sources[:, None] * block_cells + jnp.arange(block_cells, dtype=jnp.int32)[None]).reshape(length)
    basis_table = circle_basis(cells, length)
    spectrum = jnp.dot(circles, basis_table, precision=lax.Precision.HIGH)
    factors = column_factors(band_rows, length)
    scaled = (spectrum.reshape(chunk // rows, rows, length) * factors[None]).reshape(chunk, length)
    change = lax.dot_general(
        scaled, basis_table, (((1,), (1,)), ((), ())), precision=lax.Precision.HIGH
    )
    returned = [change[:, :block_cells]]
    for shift in range(1, parts):
        pairs = [(i, (i - shift) % parts) for i in range(parts)]
        piece = change[:, shift * block_cells:(shift + 1) * block_cells]
        returned.append(lax.ppermute(piece, "lon", pairs))
    stacked = jnp.stack(returned, axis=0)
    order = (jnp.arange(parts, dtype=jnp.int32) - me) % parts
    ordered = jnp.take(stacked, order, axis=0)
    return values + ordered.reshape(values.shape)


def band_distance(a, b, band_count):
    return min(abs(a - b), a + b + 1, 2 * band_count - 1 - a - b)


def near_plan(band_count, entries, capacity):
    reach = min(band_count, -(-entries // capacity) + 1)
    tail = max(1, capacity // 3)
    nearest = []
    limits = np.zeros((band_count, band_count), np.int32)
    for band in range(band_count):
        order = sorted(range(band_count), key=lambda o: (band_distance(band, o, band_count), o))
        nearest.append(order[:reach])
        for owner in order[:reach]:
            limits[band, owner] = capacity
        if reach < band_count and reach > 2:
            last, before = order[reach - 1], order[reach - 2]
            if band_distance(band, last, band_count) > band_distance(band, before, band_count):
                limits[band, last] = tail
    groups = {}
    for band in range(band_count):
        for owner in nearest[band]:
            if owner != band:
                groups.setdefault((owner - band, int(limits[band, owner])), []).append((owner, band))
    return limits, sorted(groups.items())


def departure_near(tracers, dep_owner, dep_row, dep_weight, limits, groups, capacity):
    band_count = lax.axis_size("lat")
    row_count, link_count = dep_owner.shape
    entries = row_count * link_count
    me = lax.axis_index("lat")
    owner_ids = dep_owner.reshape(entries)
    source = dep_row.reshape(entries)
    positions = jnp.arange(entries)
    earlier = (owner_ids[:, None] == owner_ids[None, :]) & (positions[None, :] < positions[:, None])
    slot_ids = jnp.sum(earlier.astype(jnp.int32), axis=1)
    outside = jnp.sum((slot_ids >= jnp.asarray(limits)[me][owner_ids]).astype(jnp.int32))
    band_ids = jnp.arange(band_count, dtype=jnp.int32)
    slot_range = jnp.arange(capacity, dtype=jnp.int32)
    matches = (owner_ids[:, None, None] == band_ids[None, :, None]) & (
        slot_ids[:, None, None] == slot_range[None, None, :]
    )
    request = jnp.sum(jnp.where(matches, source[:, None, None], 0), axis=0)
    flag = jnp.broadcast_to(outside, (band_count, 1)).astype(jnp.int32)
    message = jnp.concatenate([request, flag], axis=1)
    wanted = lax.all_to_all(message, "lat", split_axis=0, concat_axis=0, tiled=True)
    covered = jnp.all(wanted[:, capacity] == 0)
    weights = dep_weight.reshape(entries)
    row_range = jnp.arange(row_count, dtype=jnp.int32)
    own = jnp.where((owner_ids == me)[:, None] & (source[:, None] == row_range[None, :]),
                    weights[:, None], 0.0)
    own_weights = jnp.sum(own.reshape(row_count, link_count, row_count), axis=1)
    total = jnp.einsum("jr,flri->flji", own_weights, tracers, precision=PRECISE)
    by_size = {}
    for (offset, size), pairs in groups:
        receiver = jnp.clip(me - offset, 0, band_count - 1)
        chosen = wanted[receiver, :size]
        select = (chosen[:, None] == row_range[None, :]).astype(jnp.float32)
        outgoing = jnp.einsum("sr,flri->flsi", select, tracers, precision=PRECISE)
        incoming = lax.ppermute(outgoing, "lat", pairs)
        senders = np.full(band_count, -1, np.int32)
        for owner, band in pairs:
            senders[band] = owner
        sender = jnp.asarray(senders)[me]
        hit = (owner_ids[:, None] == sender) & (slot_ids[:, None] == slot_range[None, :size])
        part = jnp.where(hit, weights[:, None], 0.0)
        part_weights = jnp.sum(part.reshape(row_count, link_count, size), axis=1)
        by_size.setdefault(size, []).append((part_weights, incoming))
    for size, items in sorted(by_size.items()):
        part_weights = jnp.stack([w for w, _ in items], axis=0)
        incoming = jnp.stack([x for _, x in items], axis=0)
        total = total + jnp.einsum("ojs,oflsi->flji", part_weights, incoming, precision=PRECISE)
    return total, covered


def departure_all(tracers, dep_owner, dep_row, dep_weight):
    band_count = lax.axis_size("lat")
    row_count, link_count = dep_owner.shape
    entries = row_count * link_count
    capacity = max(2, -(-2 * entries // band_count))
    limits, groups = near_plan(band_count, entries, capacity)
    near, covered = departure_near(
        tracers, dep_owner, dep_row, dep_weight, limits, groups, capacity
    )
    return lax.cond(
        covered,
        lambda: near,
        lambda: departure_terms(tracers, dep_owner, dep_row, dep_weight),
    )


def body(
    prognostic,
    tracers,
    zonal_courant,
    meridional_courant,
    filter_band,
    dep_owner,
    dep_row,
    dep_weight,
):
    row_count = prognostic.shape[2]
    departed = departure_all(tracers, dep_owner, dep_row, dep_weight)
    lon_padded = padded(
        jnp.concatenate([prognostic, zonal_courant[None]], axis=0), (("lon", 3),), 1, True
    )
    zonal_flux = face_flux(lon_padded[:-1], lon_padded[-1:], 3)
    lat_padded = padded(
        jnp.concatenate([prognostic, meridional_courant[None]], axis=0), (("lat", 2),), 1, False
    )
    merid_flux = face_flux(lat_padded[:-1], lat_padded[-1:], 2)
    total_rows = row_count * lax.axis_size("lat")
    face_rows = lax.axis_index("lat") * row_count + jnp.arange(row_count + 1) - 1
    merid_flux = jnp.where(
        (face_rows == total_rows - 1)[None, None, :, None], jnp.float32(0.0), merid_flux
    )
    advected = (
        prognostic
        - (zonal_flux[..., 1:] - zonal_flux[..., :-1])
        - (merid_flux[:, :, 1:] - merid_flux[:, :, :-1])
    )
    new_prognostic = polar_filter(advected, filter_band)
    return (new_prognostic, departed)


def solution(mesh):
    return jax.shard_map(
        body,
        mesh=mesh,
        in_specs=(
            P(None, None, "lat", "lon"),
            P(None, None, "lat", "lon"),
            P(None, "lat", "lon"),
            P(None, "lat", "lon"),
            P("lat"),
            P("lat", None),
            P("lat", None),
            P("lat", None),
        ),
        out_specs=(P(None, None, "lat", "lon"), P(None, None, "lat", "lon")),
        check_vma=False,
    )
```

```python
import math

import jax
import numpy as np
import jax.numpy as jnp
from jax import lax
from jax.sharding import PartitionSpec as P

PRECISE = lax.Precision.HIGHEST


def padded(value, sides, width, wrap):
    for axis, dim in sides:
        size, length = (lax.axis_size(axis), value.shape[dim])
        up = [(i, (i + 1) % size) for i in range(size if wrap else size - 1)]
        down = [(j, i) for i, j in up]
        last = lax.slice_in_dim(value, length - width, length, axis=dim)
        first = lax.slice_in_dim(value, 0, width, axis=dim)
        before = lax.ppermute(last, axis, up)
        after = lax.ppermute(first, axis, down)
        value = jnp.concatenate([before, value, after], axis=dim)
    return value


def face_flux(values, speeds, axis):
    count = values.shape[axis] - 2
    left_cells = lax.slice_in_dim(values, 0, count + 1, axis=axis)
    right_cells = lax.slice_in_dim(values, 1, count + 2, axis=axis)
    courant = lax.slice_in_dim(speeds, 0, count + 1, axis=axis)
    return 0.5 * courant * (left_cells + right_cells) - 0.5 * courant * courant * (
        right_cells - left_cells
    )


def column_factors(band_rows, length):
    column = jnp.arange(length, dtype=jnp.int32)
    half_length = length // 2
    frequency = jnp.where(column <= half_length, column, column - half_length)
    single = (column == 0) | (column == half_length)
    weights = jnp.where(single, 1.0 / length, 2.0 / length).astype(jnp.float32)
    ratios = (
        band_rows.astype(jnp.float32)[:, None]
        / jnp.maximum(frequency, 1).astype(jnp.float32)[None, :]
    )
    damping = jnp.minimum(1.0, ratios * ratios)
    return (damping - 1.0) * weights[None, :]


def column_factors(band_rows, length):
    column = jnp.arange(length, dtype=jnp.int32)
    half_length = length // 2
    frequency = jnp.where(column <= half_length, column, column - half_length)
    single = (column == 0) | (column == half_length)
    weights = jnp.where(single, 1.0 / length, 2.0 / length).astype(jnp.float32)
    ratios = (
        band_rows.astype(jnp.float32)[:, None]
        / jnp.maximum(frequency, 1).astype(jnp.float32)[None, :]
    )
    damping = jnp.minimum(1.0, ratios * ratios)
    return (damping - 1.0) * weights[None, :]


def circle_basis(length):
    half_length = length // 2
    column = jnp.arange(length, dtype=jnp.int32)
    frequency = jnp.where(column <= half_length, column, column - half_length)
    low_count = 64
    high_count = length // low_count
    low = jnp.arange(low_count, dtype=jnp.int32)
    high = jnp.arange(high_count, dtype=jnp.int32) * low_count
    scale = 2.0 * math.pi / length
    low_angle = scale * (low[:, None] * frequency[None, :] % length).astype(jnp.float32)
    high_angle = scale * (high[:, None] * frequency[None, :] % length).astype(jnp.float32)
    low_cos, low_sin = jnp.cos(low_angle), jnp.sin(low_angle)
    high_cos, high_sin = jnp.cos(high_angle), jnp.sin(high_angle)
    cos_part = high_cos[:, None] * low_cos[None] - high_sin[:, None] * low_sin[None]
    sin_part = high_sin[:, None] * low_cos[None] + high_cos[:, None] * low_sin[None]
    basis = jnp.where((column <= half_length)[None, None, :], cos_part, sin_part)
    return basis.reshape(length, length)


def departure_terms(tracers, dep_owner, dep_row, dep_weight):
    band_count = lax.axis_size("lat")
    row_count, link_count = dep_owner.shape
    entries = row_count * link_count
    capacity = max(2, -(-2 * entries // band_count))
    owner_ids = dep_owner.reshape(entries)
    source = dep_row.reshape(entries)
    positions = jnp.arange(entries)
    earlier = (owner_ids[:, None] == owner_ids[None, :]) & (positions[None, :] < positions[:, None])
    slot_ids = jnp.sum(earlier.astype(jnp.int32), axis=1)
    band_ids = jnp.arange(band_count, dtype=jnp.int32)
    slot_range = jnp.arange(capacity, dtype=jnp.int32)
    matches = (owner_ids[:, None, None] == band_ids[None, :, None]) & (
        slot_ids[:, None, None] == slot_range[None, None, :]
    )
    request = jnp.sum(jnp.where(matches, source[:, None, None], 0), axis=0)
    wanted = lax.all_to_all(request, "lat", split_axis=0, concat_axis=0, tiled=True)
    by_row = jnp.transpose(tracers, (2, 0, 1, 3))
    outgoing = by_row[wanted]
    incoming = lax.all_to_all(outgoing, "lat", split_axis=0, concat_axis=0, tiled=True)
    stacked_rows = incoming.reshape((band_count * capacity,) + incoming.shape[2:])
    picked = stacked_rows[owner_ids * capacity + slot_ids].reshape(
        (row_count, link_count) + stacked_rows.shape[1:]
    )
    summed = dep_weight[:, 0][:, None, None, None] * picked[:, 0]
    summed = summed + dep_weight[:, 1][:, None, None, None] * picked[:, 1]
    return jnp.transpose(summed, (1, 2, 0, 3))


def circle_basis(cells, length):
    half_length = length // 2
    column = jnp.arange(length, dtype=jnp.int32)
    frequency = jnp.where(column <= half_length, column, column - half_length)
    low_count = math.gcd(cells.shape[0], 64)
    low = jnp.arange(low_count, dtype=jnp.int32)
    high = cells.reshape(-1, low_count)[:, 0]
    scale = 2.0 * math.pi / length
    low_angle = scale * (low[:, None] * frequency[None, :] % length).astype(jnp.float32)
    high_angle = scale * (high[:, None] * frequency[None, :] % length).astype(jnp.float32)
    low_cos, low_sin = jnp.cos(low_angle), jnp.sin(low_angle)
    high_cos, high_sin = jnp.cos(high_angle), jnp.sin(high_angle)
    cos_part = high_cos[:, None] * low_cos[None] - high_sin[:, None] * low_sin[None]
    sin_part = high_sin[:, None] * low_cos[None] + high_cos[:, None] * low_sin[None]
    basis = jnp.where((column <= half_length)[None, None, :], cos_part, sin_part)
    return basis.reshape(cells.shape[0], length)


def polar_filter(values, band_rows):
    fields, levels, rows, block_cells = values.shape
    parts = lax.axis_size("lon")
    me = lax.axis_index("lon")
    length = block_cells * parts
    flat = values.reshape(fields * levels * rows, block_cells)
    chunk = flat.shape[0] // parts
    blocks = [lax.dynamic_slice_in_dim(flat, me * chunk, chunk, axis=0)]
    for shift in range(1, parts):
        target = (me + shift) % parts
        piece = lax.dynamic_slice_in_dim(flat, target * chunk, chunk, axis=0)
        pairs = [(i, (i + shift) % parts) for i in range(parts)]
        blocks.append(lax.ppermute(piece, "lon", pairs))
    circles = jnp.concatenate(blocks, axis=1)
    shifts = jnp.arange(parts, dtype=jnp.int32)
    sources = (me - shifts) % parts
    cells = (sources[:, None] * block_cells + jnp.arange(block_cells, dtype=jnp.int32)[None]).reshape(length)
    basis_table = circle_basis(cells, length)
    spectrum = jnp.dot(circles, basis_table, precision=lax.Precision.HIGH)
    factors = column_factors(band_rows, length)
    scaled = (spectrum.reshape(chunk // rows, rows, length) * factors[None]).reshape(chunk, length)
    change = lax.dot_general(
        scaled, basis_table, (((1,), (1,)), ((), ())), precision=lax.Precision.HIGH
    )
    returned = [change[:, :block_cells]]
    for shift in range(1, parts):
        pairs = [(i, (i - shift) % parts) for i in range(parts)]
        piece = change[:, shift * block_cells:(shift + 1) * block_cells]
        returned.append(lax.ppermute(piece, "lon", pairs))
    stacked = jnp.stack(returned, axis=0)
    order = (jnp.arange(parts, dtype=jnp.int32) - me) % parts
    ordered = jnp.take(stacked, order, axis=0)
    return values + ordered.reshape(values.shape)


def band_distance(a, b, band_count):
    return min(abs(a - b), a + b + 1, 2 * band_count - 1 - a - b)


def near_plan(band_count, entries, capacity):
    reach = min(band_count, -(-entries // capacity) + 1)
    tail = max(1, capacity // 3)
    nearest = []
    limits = np.zeros((band_count, band_count), np.int32)
    for band in range(band_count):
        order = sorted(range(band_count), key=lambda o: (band_distance(band, o, band_count), o))
        nearest.append(order[:reach])
        for owner in order[:reach]:
            limits[band, owner] = capacity
        if reach < band_count and reach > 2:
            last, before = order[reach - 1], order[reach - 2]
            if band_distance(band, last, band_count) > band_distance(band, before, band_count):
                limits[band, last] = tail
    groups = {}
    for band in range(band_count):
        for owner in nearest[band]:
            if owner != band:
                groups.setdefault((owner - band, int(limits[band, owner])), []).append((owner, band))
    return limits, sorted(groups.items())


def departure_near(tracers, dep_owner, dep_row, dep_weight, limits, groups, capacity):
    band_count = lax.axis_size("lat")
    row_count, link_count = dep_owner.shape
    entries = row_count * link_count
    me = lax.axis_index("lat")
    owner_ids = dep_owner.reshape(entries)
    source = dep_row.reshape(entries)
    positions = jnp.arange(entries)
    earlier = (owner_ids[:, None] == owner_ids[None, :]) & (positions[None, :] < positions[:, None])
    slot_ids = jnp.sum(earlier.astype(jnp.int32), axis=1)
    outside = jnp.sum((slot_ids >= jnp.asarray(limits)[me][owner_ids]).astype(jnp.int32))
    band_ids = jnp.arange(band_count, dtype=jnp.int32)
    slot_range = jnp.arange(capacity, dtype=jnp.int32)
    matches = (owner_ids[:, None, None] == band_ids[None, :, None]) & (
        slot_ids[:, None, None] == slot_range[None, None, :]
    )
    request = jnp.sum(jnp.where(matches, source[:, None, None], 0), axis=0)
    flag = jnp.broadcast_to(outside, (band_count, 1)).astype(jnp.int32)
    message = jnp.concatenate([request, flag], axis=1)
    wanted = lax.all_to_all(message, "lat", split_axis=0, concat_axis=0, tiled=True)
    covered = jnp.all(wanted[:, capacity] == 0)
    weights = dep_weight.reshape(entries)
    row_range = jnp.arange(row_count, dtype=jnp.int32)
    own = jnp.where((owner_ids == me)[:, None] & (source[:, None] == row_range[None, :]),
                    weights[:, None], 0.0)
    own_weights = jnp.sum(own.reshape(row_count, link_count, row_count), axis=1)
    by_row = jnp.transpose(tracers, (2, 0, 1, 3)).reshape(row_count, -1)
    total = jnp.dot(own_weights, by_row, precision=PRECISE)
    by_size = {}
    for (offset, size), pairs in groups:
        receiver = jnp.clip(me - offset, 0, band_count - 1)
        chosen = wanted[receiver, :size]
        select = (chosen[:, None] == row_range[None, :]).astype(jnp.float32)
        outgoing = jnp.dot(select, by_row, precision=PRECISE)
        incoming = lax.ppermute(outgoing, "lat", pairs)
        senders = np.full(band_count, -1, np.int32)
        for owner, band in pairs:
            senders[band] = owner
        sender = jnp.asarray(senders)[me]
        hit = (owner_ids[:, None] == sender) & (slot_ids[:, None] == slot_range[None, :size])
        part = jnp.where(hit, weights[:, None], 0.0)
        part_weights = jnp.sum(part.reshape(row_count, link_count, size), axis=1)
        by_size.setdefault(size, []).append((part_weights, incoming))
    for size, items in sorted(by_size.items()):
        part_weights = jnp.concatenate([w for w, _ in items], axis=1)
        incoming = jnp.concatenate([x for _, x in items], axis=0)
        total = total + jnp.dot(part_weights, incoming, precision=PRECISE)
    fields, levels, _, cells = tracers.shape
    total = jnp.transpose(total.reshape(row_count, fields, levels, cells), (1, 2, 0, 3))
    return total, covered


def departure_all(tracers, dep_owner, dep_row, dep_weight):
    band_count = lax.axis_size("lat")
    row_count, link_count = dep_owner.shape
    entries = row_count * link_count
    capacity = max(2, -(-2 * entries // band_count))
    limits, groups = near_plan(band_count, entries, capacity)
    near, covered = departure_near(
        tracers, dep_owner, dep_row, dep_weight, limits, groups, capacity
    )
    return lax.cond(
        covered,
        lambda: near,
        lambda: departure_terms(tracers, dep_owner, dep_row, dep_weight),
    )


def body(
    prognostic,
    tracers,
    zonal_courant,
    meridional_courant,
    filter_band,
    dep_owner,
    dep_row,
    dep_weight,
):
    row_count = prognostic.shape[2]
    departed = departure_all(tracers, dep_owner, dep_row, dep_weight)
    lon_padded = padded(
        jnp.concatenate([prognostic, zonal_courant[None]], axis=0), (("lon", 3),), 1, True
    )
    zonal_flux = face_flux(lon_padded[:-1], lon_padded[-1:], 3)
    lat_padded = padded(
        jnp.concatenate([prognostic, meridional_courant[None]], axis=0), (("lat", 2),), 1, False
    )
    merid_flux = face_flux(lat_padded[:-1], lat_padded[-1:], 2)
    total_rows = row_count * lax.axis_size("lat")
    face_rows = lax.axis_index("lat") * row_count + jnp.arange(row_count + 1) - 1
    merid_flux = jnp.where(
        (face_rows == total_rows - 1)[None, None, :, None], jnp.float32(0.0), merid_flux
    )
    advected = (
        prognostic
        - (zonal_flux[..., 1:] - zonal_flux[..., :-1])
        - (merid_flux[:, :, 1:] - merid_flux[:, :, :-1])
    )
    new_prognostic = polar_filter(advected, filter_band)
    return (new_prognostic, departed)


def solution(mesh):
    return jax.shard_map(
        body,
        mesh=mesh,
        in_specs=(
            P(None, None, "lat", "lon"),
            P(None, None, "lat", "lon"),
            P(None, "lat", "lon"),
            P(None, "lat", "lon"),
            P("lat"),
            P("lat", None),
            P("lat", None),
            P("lat", None),
        ),
        out_specs=(P(None, None, "lat", "lon"), P(None, None, "lat", "lon")),
        check_vma=False,
    )
```

```python
import math

import jax
import numpy as np
import jax.numpy as jnp
from jax import lax
from jax.sharding import PartitionSpec as P

PRECISE = lax.Precision.HIGHEST


def padded(value, sides, width, wrap):
    for axis, dim in sides:
        size, length = (lax.axis_size(axis), value.shape[dim])
        up = [(i, (i + 1) % size) for i in range(size if wrap else size - 1)]
        down = [(j, i) for i, j in up]
        last = lax.slice_in_dim(value, length - width, length, axis=dim)
        first = lax.slice_in_dim(value, 0, width, axis=dim)
        before = lax.ppermute(last, axis, up)
        after = lax.ppermute(first, axis, down)
        value = jnp.concatenate([before, value, after], axis=dim)
    return value


def face_flux(values, speeds, axis):
    count = values.shape[axis] - 2
    left_cells = lax.slice_in_dim(values, 0, count + 1, axis=axis)
    right_cells = lax.slice_in_dim(values, 1, count + 2, axis=axis)
    courant = lax.slice_in_dim(speeds, 0, count + 1, axis=axis)
    return 0.5 * courant * (left_cells + right_cells) - 0.5 * courant * courant * (
        right_cells - left_cells
    )


def column_factors(band_rows, length):
    column = jnp.arange(length, dtype=jnp.int32)
    half_length = length // 2
    frequency = jnp.where(column <= half_length, column, column - half_length)
    single = (column == 0) | (column == half_length)
    weights = jnp.where(single, 1.0 / length, 2.0 / length).astype(jnp.float32)
    ratios = (
        band_rows.astype(jnp.float32)[:, None]
        / jnp.maximum(frequency, 1).astype(jnp.float32)[None, :]
    )
    damping = jnp.minimum(1.0, ratios * ratios)
    return (damping - 1.0) * weights[None, :]


def column_factors(band_rows, length):
    column = jnp.arange(length, dtype=jnp.int32)
    half_length = length // 2
    frequency = jnp.where(column <= half_length, column, column - half_length)
    single = (column == 0) | (column == half_length)
    weights = jnp.where(single, 1.0 / length, 2.0 / length).astype(jnp.float32)
    ratios = (
        band_rows.astype(jnp.float32)[:, None]
        / jnp.maximum(frequency, 1).astype(jnp.float32)[None, :]
    )
    damping = jnp.minimum(1.0, ratios * ratios)
    return (damping - 1.0) * weights[None, :]


def circle_basis(length):
    half_length = length // 2
    column = jnp.arange(length, dtype=jnp.int32)
    frequency = jnp.where(column <= half_length, column, column - half_length)
    low_count = 64
    high_count = length // low_count
    low = jnp.arange(low_count, dtype=jnp.int32)
    high = jnp.arange(high_count, dtype=jnp.int32) * low_count
    scale = 2.0 * math.pi / length
    low_angle = scale * (low[:, None] * frequency[None, :] % length).astype(jnp.float32)
    high_angle = scale * (high[:, None] * frequency[None, :] % length).astype(jnp.float32)
    low_cos, low_sin = jnp.cos(low_angle), jnp.sin(low_angle)
    high_cos, high_sin = jnp.cos(high_angle), jnp.sin(high_angle)
    cos_part = high_cos[:, None] * low_cos[None] - high_sin[:, None] * low_sin[None]
    sin_part = high_sin[:, None] * low_cos[None] + high_cos[:, None] * low_sin[None]
    basis = jnp.where((column <= half_length)[None, None, :], cos_part, sin_part)
    return basis.reshape(length, length)


def departure_terms(tracers, dep_owner, dep_row, dep_weight):
    band_count = lax.axis_size("lat")
    row_count, link_count = dep_owner.shape
    entries = row_count * link_count
    capacity = max(2, -(-2 * entries // band_count))
    owner_ids = dep_owner.reshape(entries)
    source = dep_row.reshape(entries)
    positions = jnp.arange(entries)
    earlier = (owner_ids[:, None] == owner_ids[None, :]) & (positions[None, :] < positions[:, None])
    slot_ids = jnp.sum(earlier.astype(jnp.int32), axis=1)
    band_ids = jnp.arange(band_count, dtype=jnp.int32)
    slot_range = jnp.arange(capacity, dtype=jnp.int32)
    matches = (owner_ids[:, None, None] == band_ids[None, :, None]) & (
        slot_ids[:, None, None] == slot_range[None, None, :]
    )
    request = jnp.sum(jnp.where(matches, source[:, None, None], 0), axis=0)
    wanted = lax.all_to_all(request, "lat", split_axis=0, concat_axis=0, tiled=True)
    by_row = jnp.transpose(tracers, (2, 0, 1, 3))
    outgoing = by_row[wanted]
    incoming = lax.all_to_all(outgoing, "lat", split_axis=0, concat_axis=0, tiled=True)
    stacked_rows = incoming.reshape((band_count * capacity,) + incoming.shape[2:])
    picked = stacked_rows[owner_ids * capacity + slot_ids].reshape(
        (row_count, link_count) + stacked_rows.shape[1:]
    )
    summed = dep_weight[:, 0][:, None, None, None] * picked[:, 0]
    summed = summed + dep_weight[:, 1][:, None, None, None] * picked[:, 1]
    return jnp.transpose(summed, (1, 2, 0, 3))


def circle_basis(cells, length):
    half_length = length // 2
    column = jnp.arange(length, dtype=jnp.int32)
    frequency = jnp.where(column <= half_length, column, column - half_length)
    low_count = math.gcd(cells.shape[0], 64)
    low = jnp.arange(low_count, dtype=jnp.int32)
    high = cells.reshape(-1, low_count)[:, 0]
    scale = 2.0 * math.pi / length
    low_angle = scale * (low[:, None] * frequency[None, :] % length).astype(jnp.float32)
    high_angle = scale * (high[:, None] * frequency[None, :] % length).astype(jnp.float32)
    low_cos, low_sin = jnp.cos(low_angle), jnp.sin(low_angle)
    high_cos, high_sin = jnp.cos(high_angle), jnp.sin(high_angle)
    cos_part = high_cos[:, None] * low_cos[None] - high_sin[:, None] * low_sin[None]
    sin_part = high_sin[:, None] * low_cos[None] + high_cos[:, None] * low_sin[None]
    basis = jnp.where((column <= half_length)[None, None, :], cos_part, sin_part)
    return basis.reshape(cells.shape[0], length)


def polar_filter(values, band_rows):
    fields, levels, rows, block_cells = values.shape
    parts = lax.axis_size("lon")
    me = lax.axis_index("lon")
    length = block_cells * parts
    flat = values.reshape(fields * levels * rows, block_cells)
    chunk = flat.shape[0] // parts
    circles = lax.all_to_all(flat, "lon", split_axis=0, concat_axis=1, tiled=True)
    cells = jnp.arange(length, dtype=jnp.int32)
    basis_table = circle_basis(cells, length)
    spectrum = jnp.dot(circles, basis_table, precision=lax.Precision.HIGH)
    factors = column_factors(band_rows, length)
    scaled = (spectrum.reshape(chunk // rows, rows, length) * factors[None]).reshape(chunk, length)
    change = lax.dot_general(
        scaled, basis_table, (((1,), (1,)), ((), ())), precision=lax.Precision.HIGH
    )
    back = lax.all_to_all(change, "lon", split_axis=1, concat_axis=0, tiled=True)
    return values + back.reshape(values.shape)


def band_distance(a, b, band_count):
    return min(abs(a - b), a + b + 1, 2 * band_count - 1 - a - b)


def near_plan(band_count, entries, capacity):
    reach = min(band_count, -(-entries // capacity) + 1)
    tail = max(1, capacity // 3)
    nearest = []
    limits = np.zeros((band_count, band_count), np.int32)
    for band in range(band_count):
        order = sorted(range(band_count), key=lambda o: (band_distance(band, o, band_count), o))
        nearest.append(order[:reach])
        for owner in order[:reach]:
            limits[band, owner] = capacity
        if reach < band_count and reach > 2:
            last, before = order[reach - 1], order[reach - 2]
            if band_distance(band, last, band_count) > band_distance(band, before, band_count):
                limits[band, last] = tail
    groups = {}
    for band in range(band_count):
        for owner in nearest[band]:
            if owner != band:
                groups.setdefault((owner - band, int(limits[band, owner])), []).append((owner, band))
    merged = []
    for (offset, size), pairs in sorted(groups.items(), key=lambda g: -len(g[1])):
        for held in merged:
            sources = {o for o, _ in held[1]}
            targets = {b for _, b in held[1]}
            if held[0] == size and not sources & {o for o, _ in pairs} and not targets & {b for _, b in pairs}:
                held[1].extend(pairs)
                break
        else:
            merged.append((size, list(pairs)))
    return limits, [((index, size), pairs) for index, (size, pairs) in enumerate(merged)]


def departure_near(tracers, dep_owner, dep_row, dep_weight, limits, groups, capacity):
    band_count = lax.axis_size("lat")
    row_count, link_count = dep_owner.shape
    entries = row_count * link_count
    me = lax.axis_index("lat")
    owner_ids = dep_owner.reshape(entries)
    source = dep_row.reshape(entries)
    positions = jnp.arange(entries)
    earlier = (owner_ids[:, None] == owner_ids[None, :]) & (positions[None, :] < positions[:, None])
    slot_ids = jnp.sum(earlier.astype(jnp.int32), axis=1)
    outside = jnp.sum((slot_ids >= jnp.asarray(limits)[me][owner_ids]).astype(jnp.int32))
    band_ids = jnp.arange(band_count, dtype=jnp.int32)
    slot_range = jnp.arange(capacity, dtype=jnp.int32)
    matches = (owner_ids[:, None, None] == band_ids[None, :, None]) & (
        slot_ids[:, None, None] == slot_range[None, None, :]
    )
    request = jnp.sum(jnp.where(matches, source[:, None, None], 0), axis=0)
    flag = jnp.broadcast_to(outside, (band_count, 1)).astype(jnp.int32)
    message = jnp.concatenate([request, flag], axis=1)
    wanted = lax.all_to_all(message, "lat", split_axis=0, concat_axis=0, tiled=True)
    covered = jnp.all(wanted[:, capacity] == 0)
    weights = dep_weight.reshape(entries)
    row_range = jnp.arange(row_count, dtype=jnp.int32)
    own = jnp.where((owner_ids == me)[:, None] & (source[:, None] == row_range[None, :]),
                    weights[:, None], 0.0)
    own_weights = jnp.sum(own.reshape(row_count, link_count, row_count), axis=1)
    total = jnp.einsum("jr,flri->flji", own_weights, tracers, precision=PRECISE)
    by_size = {}
    for (_, size), pairs in groups:
        receivers = np.zeros(band_count, np.int32)
        for owner, band in pairs:
            receivers[owner] = band
        receiver = jnp.asarray(receivers)[me]
        chosen = wanted[receiver, :size]
        select = (chosen[:, None] == row_range[None, :]).astype(jnp.float32)
        outgoing = jnp.einsum("sr,flri->flsi", select, tracers, precision=PRECISE)
        incoming = lax.ppermute(outgoing, "lat", pairs)
        senders = np.full(band_count, -1, np.int32)
        for owner, band in pairs:
            senders[band] = owner
        sender = jnp.asarray(senders)[me]
        hit = (owner_ids[:, None] == sender) & (slot_ids[:, None] == slot_range[None, :size])
        part = jnp.where(hit, weights[:, None], 0.0)
        part_weights = jnp.sum(part.reshape(row_count, link_count, size), axis=1)
        by_size.setdefault(size, []).append((part_weights, incoming))
    for size, items in sorted(by_size.items()):
        part_weights = jnp.stack([w for w, _ in items], axis=0)
        incoming = jnp.stack([x for _, x in items], axis=0)
        total = total + jnp.einsum("ojs,oflsi->flji", part_weights, incoming, precision=PRECISE)
    return total, covered


def departure_all(tracers, dep_owner, dep_row, dep_weight):
    band_count = lax.axis_size("lat")
    row_count, link_count = dep_owner.shape
    entries = row_count * link_count
    capacity = max(2, -(-2 * entries // band_count))
    limits, groups = near_plan(band_count, entries, capacity)
    near, covered = departure_near(
        tracers, dep_owner, dep_row, dep_weight, limits, groups, capacity
    )
    return lax.cond(
        covered,
        lambda: near,
        lambda: departure_terms(tracers, dep_owner, dep_row, dep_weight),
    )


def body(
    prognostic,
    tracers,
    zonal_courant,
    meridional_courant,
    filter_band,
    dep_owner,
    dep_row,
    dep_weight,
):
    row_count = prognostic.shape[2]
    departed = departure_all(tracers, dep_owner, dep_row, dep_weight)
    lon_padded = padded(
        jnp.concatenate([prognostic, zonal_courant[None]], axis=0), (("lon", 3),), 1, True
    )
    zonal_flux = face_flux(lon_padded[:-1], lon_padded[-1:], 3)
    lat_padded = padded(
        jnp.concatenate([prognostic, meridional_courant[None]], axis=0), (("lat", 2),), 1, False
    )
    merid_flux = face_flux(lat_padded[:-1], lat_padded[-1:], 2)
    total_rows = row_count * lax.axis_size("lat")
    face_rows = lax.axis_index("lat") * row_count + jnp.arange(row_count + 1) - 1
    merid_flux = jnp.where(
        (face_rows == total_rows - 1)[None, None, :, None], jnp.float32(0.0), merid_flux
    )
    advected = (
        prognostic
        - (zonal_flux[..., 1:] - zonal_flux[..., :-1])
        - (merid_flux[:, :, 1:] - merid_flux[:, :, :-1])
    )
    new_prognostic = polar_filter(advected, filter_band)
    return (new_prognostic, departed)


def solution(mesh):
    return jax.shard_map(
        body,
        mesh=mesh,
        in_specs=(
            P(None, None, "lat", "lon"),
            P(None, None, "lat", "lon"),
            P(None, "lat", "lon"),
            P(None, "lat", "lon"),
            P("lat"),
            P("lat", None),
            P("lat", None),
            P("lat", None),
        ),
        out_specs=(P(None, None, "lat", "lon"), P(None, None, "lat", "lon")),
        check_vma=False,
    )
```

```python
import math

import jax
import numpy as np
import jax.numpy as jnp
from jax import lax
from jax.sharding import PartitionSpec as P

PRECISE = lax.Precision.HIGHEST


def padded(value, sides, width, wrap):
    for axis, dim in sides:
        size, length = (lax.axis_size(axis), value.shape[dim])
        up = [(i, (i + 1) % size) for i in range(size if wrap else size - 1)]
        down = [(j, i) for i, j in up]
        last = lax.slice_in_dim(value, length - width, length, axis=dim)
        first = lax.slice_in_dim(value, 0, width, axis=dim)
        before = lax.ppermute(last, axis, up)
        after = lax.ppermute(first, axis, down)
        value = jnp.concatenate([before, value, after], axis=dim)
    return value


def face_flux(values, speeds, axis):
    count = values.shape[axis] - 2
    left_cells = lax.slice_in_dim(values, 0, count + 1, axis=axis)
    right_cells = lax.slice_in_dim(values, 1, count + 2, axis=axis)
    courant = lax.slice_in_dim(speeds, 0, count + 1, axis=axis)
    return 0.5 * courant * (left_cells + right_cells) - 0.5 * courant * courant * (
        right_cells - left_cells
    )


def column_factors(band_rows, length):
    column = jnp.arange(length, dtype=jnp.int32)
    half_length = length // 2
    frequency = jnp.where(column <= half_length, column, column - half_length)
    single = (column == 0) | (column == half_length)
    weights = jnp.where(single, 1.0 / length, 2.0 / length).astype(jnp.float32)
    ratios = (
        band_rows.astype(jnp.float32)[:, None]
        / jnp.maximum(frequency, 1).astype(jnp.float32)[None, :]
    )
    damping = jnp.minimum(1.0, ratios * ratios)
    return (damping - 1.0) * weights[None, :]


def column_factors(band_rows, length):
    column = jnp.arange(length, dtype=jnp.int32)
    half_length = length // 2
    frequency = jnp.where(column <= half_length, column, column - half_length)
    single = (column == 0) | (column == half_length)
    weights = jnp.where(single, 1.0 / length, 2.0 / length).astype(jnp.float32)
    ratios = (
        band_rows.astype(jnp.float32)[:, None]
        / jnp.maximum(frequency, 1).astype(jnp.float32)[None, :]
    )
    damping = jnp.minimum(1.0, ratios * ratios)
    return (damping - 1.0) * weights[None, :]


def circle_basis(length):
    half_length = length // 2
    column = jnp.arange(length, dtype=jnp.int32)
    frequency = jnp.where(column <= half_length, column, column - half_length)
    low_count = 64
    high_count = length // low_count
    low = jnp.arange(low_count, dtype=jnp.int32)
    high = jnp.arange(high_count, dtype=jnp.int32) * low_count
    scale = 2.0 * math.pi / length
    low_angle = scale * (low[:, None] * frequency[None, :] % length).astype(jnp.float32)
    high_angle = scale * (high[:, None] * frequency[None, :] % length).astype(jnp.float32)
    low_cos, low_sin = jnp.cos(low_angle), jnp.sin(low_angle)
    high_cos, high_sin = jnp.cos(high_angle), jnp.sin(high_angle)
    cos_part = high_cos[:, None] * low_cos[None] - high_sin[:, None] * low_sin[None]
    sin_part = high_sin[:, None] * low_cos[None] + high_cos[:, None] * low_sin[None]
    basis = jnp.where((column <= half_length)[None, None, :], cos_part, sin_part)
    return basis.reshape(length, length)


def departure_terms(tracers, dep_owner, dep_row, dep_weight):
    band_count = lax.axis_size("lat")
    row_count, link_count = dep_owner.shape
    entries = row_count * link_count
    capacity = max(2, -(-2 * entries // band_count))
    owner_ids = dep_owner.reshape(entries)
    source = dep_row.reshape(entries)
    positions = jnp.arange(entries)
    earlier = (owner_ids[:, None] == owner_ids[None, :]) & (positions[None, :] < positions[:, None])
    slot_ids = jnp.sum(earlier.astype(jnp.int32), axis=1)
    band_ids = jnp.arange(band_count, dtype=jnp.int32)
    slot_range = jnp.arange(capacity, dtype=jnp.int32)
    matches = (owner_ids[:, None, None] == band_ids[None, :, None]) & (
        slot_ids[:, None, None] == slot_range[None, None, :]
    )
    request = jnp.sum(jnp.where(matches, source[:, None, None], 0), axis=0)
    wanted = lax.all_to_all(request, "lat", split_axis=0, concat_axis=0, tiled=True)
    by_row = jnp.transpose(tracers, (2, 0, 1, 3))
    outgoing = by_row[wanted]
    incoming = lax.all_to_all(outgoing, "lat", split_axis=0, concat_axis=0, tiled=True)
    stacked_rows = incoming.reshape((band_count * capacity,) + incoming.shape[2:])
    picked = stacked_rows[owner_ids * capacity + slot_ids].reshape(
        (row_count, link_count) + stacked_rows.shape[1:]
    )
    summed = dep_weight[:, 0][:, None, None, None] * picked[:, 0]
    summed = summed + dep_weight[:, 1][:, None, None, None] * picked[:, 1]
    return jnp.transpose(summed, (1, 2, 0, 3))


def circle_basis(cells, length):
    half_length = length // 2
    column = jnp.arange(length, dtype=jnp.int32)
    frequency = jnp.where(column <= half_length, column, column - half_length)
    low_count = math.gcd(cells.shape[0], 64)
    low = jnp.arange(low_count, dtype=jnp.int32)
    high = cells.reshape(-1, low_count)[:, 0]
    scale = 2.0 * math.pi / length
    low_angle = scale * (low[:, None] * frequency[None, :] % length).astype(jnp.float32)
    high_angle = scale * (high[:, None] * frequency[None, :] % length).astype(jnp.float32)
    low_cos, low_sin = jnp.cos(low_angle), jnp.sin(low_angle)
    high_cos, high_sin = jnp.cos(high_angle), jnp.sin(high_angle)
    cos_part = high_cos[:, None] * low_cos[None] - high_sin[:, None] * low_sin[None]
    sin_part = high_sin[:, None] * low_cos[None] + high_cos[:, None] * low_sin[None]
    basis = jnp.where((column <= half_length)[None, None, :], cos_part, sin_part)
    return basis.reshape(cells.shape[0], length)


def polar_filter(values, band_rows):
    fields, levels, rows, block_cells = values.shape
    parts = lax.axis_size("lon")
    me = lax.axis_index("lon")
    length = block_cells * parts
    flat = values.reshape(fields * levels * rows, block_cells)
    chunk = flat.shape[0] // parts
    blocks = [lax.dynamic_slice_in_dim(flat, me * chunk, chunk, axis=0)]
    for shift in range(1, parts):
        target = (me + shift) % parts
        piece = lax.dynamic_slice_in_dim(flat, target * chunk, chunk, axis=0)
        pairs = [(i, (i + shift) % parts) for i in range(parts)]
        blocks.append(lax.ppermute(piece, "lon", pairs))
    circles = jnp.concatenate(blocks, axis=1)
    shifts = jnp.arange(parts, dtype=jnp.int32)
    sources = (me - shifts) % parts
    cells = (sources[:, None] * block_cells + jnp.arange(block_cells, dtype=jnp.int32)[None]).reshape(length)
    basis_table = circle_basis(cells, length)
    spectrum = jnp.dot(circles, basis_table, precision=lax.Precision.HIGH)
    factors = column_factors(band_rows, length)
    scaled = (spectrum.reshape(chunk // rows, rows, length) * factors[None]).reshape(chunk, length)
    change = lax.dot_general(
        scaled, basis_table, (((1,), (1,)), ((), ())), precision=lax.Precision.HIGH
    )
    returned = [change[:, :block_cells]]
    for shift in range(1, parts):
        pairs = [(i, (i - shift) % parts) for i in range(parts)]
        piece = change[:, shift * block_cells:(shift + 1) * block_cells]
        returned.append(lax.ppermute(piece, "lon", pairs))
    stacked = jnp.stack(returned, axis=0)
    order = (jnp.arange(parts, dtype=jnp.int32) - me) % parts
    ordered = jnp.take(stacked, order, axis=0)
    return values + ordered.reshape(values.shape)


def band_distance(a, b, band_count):
    return min(abs(a - b), a + b + 1, 2 * band_count - 1 - a - b)


def near_plan(band_count, entries, capacity):
    reach = min(band_count, -(-entries // capacity) + 1)
    tail = max(1, capacity // 3)
    nearest = []
    limits = np.zeros((band_count, band_count), np.int32)
    for band in range(band_count):
        order = sorted(range(band_count), key=lambda o: (band_distance(band, o, band_count), o))
        nearest.append(order[:reach])
        for owner in order[:reach]:
            limits[band, owner] = capacity
        if reach < band_count and reach > 2:
            last, before = order[reach - 1], order[reach - 2]
            if band_distance(band, last, band_count) > band_distance(band, before, band_count):
                limits[band, last] = tail
    groups = {}
    for band in range(band_count):
        for owner in nearest[band]:
            if owner != band:
                groups.setdefault((owner - band, int(limits[band, owner])), []).append((owner, band))
    merged = []
    for (offset, size), pairs in sorted(groups.items(), key=lambda g: -len(g[1])):
        for held in merged:
            sources = {o for o, _ in held[1]}
            targets = {b for _, b in held[1]}
            if held[0] == size and not sources & {o for o, _ in pairs} and not targets & {b for _, b in pairs}:
                held[1].extend(pairs)
                break
        else:
            merged.append((size, list(pairs)))
    return limits, [((index, size), pairs) for index, (size, pairs) in enumerate(merged)]


def departure_near(tracers, dep_owner, dep_row, dep_weight, limits, groups, capacity):
    band_count = lax.axis_size("lat")
    row_count, link_count = dep_owner.shape
    entries = row_count * link_count
    me = lax.axis_index("lat")
    owner_ids = dep_owner.reshape(entries)
    source = dep_row.reshape(entries)
    positions = jnp.arange(entries)
    earlier = (owner_ids[:, None] == owner_ids[None, :]) & (positions[None, :] < positions[:, None])
    slot_ids = jnp.sum(earlier.astype(jnp.int32), axis=1)
    outside = jnp.sum((slot_ids >= jnp.asarray(limits)[me][owner_ids]).astype(jnp.int32))
    band_ids = jnp.arange(band_count, dtype=jnp.int32)
    slot_range = jnp.arange(capacity, dtype=jnp.int32)
    matches = (owner_ids[:, None, None] == band_ids[None, :, None]) & (
        slot_ids[:, None, None] == slot_range[None, None, :]
    )
    request = jnp.sum(jnp.where(matches, source[:, None, None], 0), axis=0)
    flag = jnp.broadcast_to(outside, (band_count, 1)).astype(jnp.int32)
    message = jnp.concatenate([request, flag], axis=1)
    wanted = lax.all_to_all(message, "lat", split_axis=0, concat_axis=0, tiled=True)
    covered = jnp.all(wanted[:, capacity] == 0)
    weights = dep_weight.reshape(entries)
    row_range = jnp.arange(row_count, dtype=jnp.int32)
    own = jnp.where((owner_ids == me)[:, None] & (source[:, None] == row_range[None, :]),
                    weights[:, None], 0.0)
    own_weights = jnp.sum(own.reshape(row_count, link_count, row_count), axis=1)
    total = jnp.einsum("jr,flri->flji", own_weights, tracers, precision=PRECISE)
    by_size = {}
    for (_, size), pairs in groups:
        receivers = np.zeros(band_count, np.int32)
        for owner, band in pairs:
            receivers[owner] = band
        receiver = jnp.asarray(receivers)[me]
        chosen = wanted[receiver, :size]
        select = (chosen[:, None] == row_range[None, :]).astype(jnp.float32)
        outgoing = jnp.einsum("sr,flri->flsi", select, tracers, precision=PRECISE)
        incoming = lax.ppermute(outgoing, "lat", pairs)
        senders = np.full(band_count, -1, np.int32)
        for owner, band in pairs:
            senders[band] = owner
        sender = jnp.asarray(senders)[me]
        hit = (owner_ids[:, None] == sender) & (slot_ids[:, None] == slot_range[None, :size])
        part = jnp.where(hit, weights[:, None], 0.0)
        part_weights = jnp.sum(part.reshape(row_count, link_count, size), axis=1)
        by_size.setdefault(size, []).append((part_weights, incoming))
    for size, items in sorted(by_size.items()):
        part_weights = jnp.stack([w for w, _ in items], axis=0)
        incoming = jnp.stack([x for _, x in items], axis=0)
        total = total + jnp.einsum("ojs,oflsi->flji", part_weights, incoming, precision=PRECISE)
    return total, covered


def departure_all(tracers, dep_owner, dep_row, dep_weight):
    band_count = lax.axis_size("lat")
    row_count, link_count = dep_owner.shape
    entries = row_count * link_count
    capacity = max(2, -(-2 * entries // band_count))
    limits, groups = near_plan(band_count, entries, capacity)
    near, covered = departure_near(
        tracers, dep_owner, dep_row, dep_weight, limits, groups, capacity
    )
    return lax.cond(
        covered,
        lambda: near,
        lambda: departure_terms(tracers, dep_owner, dep_row, dep_weight),
    )


def body(
    prognostic,
    tracers,
    zonal_courant,
    meridional_courant,
    filter_band,
    dep_owner,
    dep_row,
    dep_weight,
):
    row_count = prognostic.shape[2]
    departed = departure_all(tracers, dep_owner, dep_row, dep_weight)
    lon_padded = padded(
        jnp.concatenate([prognostic, zonal_courant[None]], axis=0), (("lon", 3),), 1, True
    )
    zonal_flux = face_flux(lon_padded[:-1], lon_padded[-1:], 3)
    lat_padded = padded(
        jnp.concatenate([prognostic, meridional_courant[None]], axis=0), (("lat", 2),), 1, False
    )
    merid_flux = face_flux(lat_padded[:-1], lat_padded[-1:], 2)
    total_rows = row_count * lax.axis_size("lat")
    face_rows = lax.axis_index("lat") * row_count + jnp.arange(row_count + 1) - 1
    merid_flux = jnp.where(
        (face_rows == total_rows - 1)[None, None, :, None], jnp.float32(0.0), merid_flux
    )
    advected = (
        prognostic
        - (zonal_flux[..., 1:] - zonal_flux[..., :-1])
        - (merid_flux[:, :, 1:] - merid_flux[:, :, :-1])
    )
    new_prognostic = polar_filter(advected, filter_band)
    return (new_prognostic, departed)


def solution(mesh):
    return jax.shard_map(
        body,
        mesh=mesh,
        in_specs=(
            P(None, None, "lat", "lon"),
            P(None, None, "lat", "lon"),
            P(None, "lat", "lon"),
            P(None, "lat", "lon"),
            P("lat"),
            P("lat", None),
            P("lat", None),
            P("lat", None),
        ),
        out_specs=(P(None, None, "lat", "lon"), P(None, None, "lat", "lon")),
        check_vma=False,
    )
```

```python
import math

import jax
import numpy as np
import jax.numpy as jnp
from jax import lax
from jax.sharding import PartitionSpec as P

PRECISE = lax.Precision.HIGHEST


def padded(value, sides, width, wrap):
    for axis, dim in sides:
        size, length = (lax.axis_size(axis), value.shape[dim])
        up = [(i, (i + 1) % size) for i in range(size if wrap else size - 1)]
        down = [(j, i) for i, j in up]
        last = lax.slice_in_dim(value, length - width, length, axis=dim)
        first = lax.slice_in_dim(value, 0, width, axis=dim)
        before = lax.ppermute(last, axis, up)
        after = lax.ppermute(first, axis, down)
        value = jnp.concatenate([before, value, after], axis=dim)
    return value


def face_flux(values, speeds, axis):
    count = values.shape[axis] - 2
    left_cells = lax.slice_in_dim(values, 0, count + 1, axis=axis)
    right_cells = lax.slice_in_dim(values, 1, count + 2, axis=axis)
    courant = lax.slice_in_dim(speeds, 0, count + 1, axis=axis)
    return 0.5 * courant * (left_cells + right_cells) - 0.5 * courant * courant * (
        right_cells - left_cells
    )


def column_factors(band_rows, length):
    column = jnp.arange(length, dtype=jnp.int32)
    half_length = length // 2
    frequency = jnp.where(column <= half_length, column, column - half_length)
    single = (column == 0) | (column == half_length)
    weights = jnp.where(single, 1.0 / length, 2.0 / length).astype(jnp.float32)
    ratios = (
        band_rows.astype(jnp.float32)[:, None]
        / jnp.maximum(frequency, 1).astype(jnp.float32)[None, :]
    )
    damping = jnp.minimum(1.0, ratios * ratios)
    return (damping - 1.0) * weights[None, :]


def column_factors(band_rows, length):
    column = jnp.arange(length, dtype=jnp.int32)
    half_length = length // 2
    frequency = jnp.where(column <= half_length, column, column - half_length)
    single = (column == 0) | (column == half_length)
    weights = jnp.where(single, 1.0 / length, 2.0 / length).astype(jnp.float32)
    ratios = (
        band_rows.astype(jnp.float32)[:, None]
        / jnp.maximum(frequency, 1).astype(jnp.float32)[None, :]
    )
    damping = jnp.minimum(1.0, ratios * ratios)
    return (damping - 1.0) * weights[None, :]


def circle_basis(length):
    half_length = length // 2
    column = jnp.arange(length, dtype=jnp.int32)
    frequency = jnp.where(column <= half_length, column, column - half_length)
    low_count = 64
    high_count = length // low_count
    low = jnp.arange(low_count, dtype=jnp.int32)
    high = jnp.arange(high_count, dtype=jnp.int32) * low_count
    scale = 2.0 * math.pi / length
    low_angle = scale * (low[:, None] * frequency[None, :] % length).astype(jnp.float32)
    high_angle = scale * (high[:, None] * frequency[None, :] % length).astype(jnp.float32)
    low_cos, low_sin = jnp.cos(low_angle), jnp.sin(low_angle)
    high_cos, high_sin = jnp.cos(high_angle), jnp.sin(high_angle)
    cos_part = high_cos[:, None] * low_cos[None] - high_sin[:, None] * low_sin[None]
    sin_part = high_sin[:, None] * low_cos[None] + high_cos[:, None] * low_sin[None]
    basis = jnp.where((column <= half_length)[None, None, :], cos_part, sin_part)
    return basis.reshape(length, length)


def departure_terms(tracers, dep_owner, dep_row, dep_weight):
    band_count = lax.axis_size("lat")
    row_count, link_count = dep_owner.shape
    entries = row_count * link_count
    capacity = max(2, -(-2 * entries // band_count))
    owner_ids = dep_owner.reshape(entries)
    source = dep_row.reshape(entries)
    positions = jnp.arange(entries)
    earlier = (owner_ids[:, None] == owner_ids[None, :]) & (positions[None, :] < positions[:, None])
    slot_ids = jnp.sum(earlier.astype(jnp.int32), axis=1)
    band_ids = jnp.arange(band_count, dtype=jnp.int32)
    slot_range = jnp.arange(capacity, dtype=jnp.int32)
    matches = (owner_ids[:, None, None] == band_ids[None, :, None]) & (
        slot_ids[:, None, None] == slot_range[None, None, :]
    )
    request = jnp.sum(jnp.where(matches, source[:, None, None], 0), axis=0)
    wanted = lax.all_to_all(request, "lat", split_axis=0, concat_axis=0, tiled=True)
    by_row = jnp.transpose(tracers, (2, 0, 1, 3))
    outgoing = by_row[wanted]
    incoming = lax.all_to_all(outgoing, "lat", split_axis=0, concat_axis=0, tiled=True)
    stacked_rows = incoming.reshape((band_count * capacity,) + incoming.shape[2:])
    picked = stacked_rows[owner_ids * capacity + slot_ids].reshape(
        (row_count, link_count) + stacked_rows.shape[1:]
    )
    summed = dep_weight[:, 0][:, None, None, None] * picked[:, 0]
    summed = summed + dep_weight[:, 1][:, None, None, None] * picked[:, 1]
    return jnp.transpose(summed, (1, 2, 0, 3))


def circle_basis(cells, length):
    half_length = length // 2
    column = jnp.arange(length, dtype=jnp.int32)
    frequency = jnp.where(column <= half_length, column, column - half_length)
    low_count = math.gcd(cells.shape[0], 64)
    low = jnp.arange(low_count, dtype=jnp.int32)
    high = cells.reshape(-1, low_count)[:, 0]
    scale = 2.0 * math.pi / length
    low_angle = scale * (low[:, None] * frequency[None, :] % length).astype(jnp.float32)
    high_angle = scale * (high[:, None] * frequency[None, :] % length).astype(jnp.float32)
    low_cos, low_sin = jnp.cos(low_angle), jnp.sin(low_angle)
    high_cos, high_sin = jnp.cos(high_angle), jnp.sin(high_angle)
    cos_part = high_cos[:, None] * low_cos[None] - high_sin[:, None] * low_sin[None]
    sin_part = high_sin[:, None] * low_cos[None] + high_cos[:, None] * low_sin[None]
    basis = jnp.where((column <= half_length)[None, None, :], cos_part, sin_part)
    return basis.reshape(cells.shape[0], length)


def polar_filter(values, band_rows):
    fields, levels, rows, block_cells = values.shape
    parts = lax.axis_size("lon")
    me = lax.axis_index("lon")
    length = block_cells * parts
    flat = values.reshape(fields * levels * rows, block_cells)
    chunk = flat.shape[0] // parts
    blocks = [lax.dynamic_slice_in_dim(flat, me * chunk, chunk, axis=0)]
    for shift in range(1, parts):
        target = (me + shift) % parts
        piece = lax.dynamic_slice_in_dim(flat, target * chunk, chunk, axis=0)
        pairs = [(i, (i + shift) % parts) for i in range(parts)]
        blocks.append(lax.ppermute(piece, "lon", pairs))
    circles = jnp.concatenate(blocks, axis=1)
    shifts = jnp.arange(parts, dtype=jnp.int32)
    sources = (me - shifts) % parts
    cells = (sources[:, None] * block_cells + jnp.arange(block_cells, dtype=jnp.int32)[None]).reshape(length)
    basis_table = circle_basis(cells, length)
    spectrum = jnp.dot(circles, basis_table, precision=lax.Precision.HIGH)
    factors = column_factors(band_rows, length)
    scaled = (spectrum.reshape(chunk // rows, rows, length) * factors[None]).reshape(chunk, length)
    change = lax.dot_general(
        scaled, basis_table, (((1,), (1,)), ((), ())), precision=lax.Precision.HIGH
    )
    returned = [change[:, :block_cells]]
    for shift in range(1, parts):
        pairs = [(i, (i - shift) % parts) for i in range(parts)]
        piece = change[:, shift * block_cells:(shift + 1) * block_cells]
        returned.append(lax.ppermute(piece, "lon", pairs))
    stacked = jnp.stack(returned, axis=0)
    order = (jnp.arange(parts, dtype=jnp.int32) - me) % parts
    ordered = jnp.take(stacked, order, axis=0)
    return values + ordered.reshape(values.shape)


def band_distance(a, b, band_count):
    return min(abs(a - b), a + b + 1, 2 * band_count - 1 - a - b)


def near_plan(band_count, entries, capacity):
    reach = min(band_count, -(-entries // capacity) + 1)
    tail = max(1, capacity // 3)
    nearest = []
    limits = np.zeros((band_count, band_count), np.int32)
    for band in range(band_count):
        order = sorted(range(band_count), key=lambda o: (band_distance(band, o, band_count), o))
        nearest.append(order[:reach])
        for owner in order[:reach]:
            limits[band, owner] = capacity
        if reach < band_count and reach > 2:
            last, before = order[reach - 1], order[reach - 2]
            if band_distance(band, last, band_count) > band_distance(band, before, band_count):
                limits[band, last] = tail
    groups = {}
    for band in range(band_count):
        for owner in nearest[band]:
            if owner != band:
                groups.setdefault((owner - band, int(limits[band, owner])), []).append((owner, band))
    merged = []
    for (offset, size), pairs in sorted(groups.items(), key=lambda g: -len(g[1])):
        for held in merged:
            sources = {o for o, _ in held[1]}
            targets = {b for _, b in held[1]}
            if held[0] == size and not sources & {o for o, _ in pairs} and not targets & {b for _, b in pairs}:
                held[1].extend(pairs)
                break
        else:
            merged.append((size, list(pairs)))
    return limits, [((index, size), pairs) for index, (size, pairs) in enumerate(merged)]


def departure_near(tracers, dep_owner, dep_row, dep_weight, limits, groups, capacity):
    band_count = lax.axis_size("lat")
    row_count, link_count = dep_owner.shape
    entries = row_count * link_count
    me = lax.axis_index("lat")
    owner_ids = dep_owner.reshape(entries)
    source = dep_row.reshape(entries)
    positions = jnp.arange(entries)
    earlier = (owner_ids[:, None] == owner_ids[None, :]) & (positions[None, :] < positions[:, None])
    slot_ids = jnp.sum(earlier.astype(jnp.int32), axis=1)
    table = np.zeros((band_count, band_count + 2 * len(groups)), np.int32)
    table[:, :band_count] = limits
    for index, (_, pairs) in enumerate(groups):
        table[:, band_count + 2 * index + 1] = -1
        for owner, band in pairs:
            table[owner, band_count + 2 * index] = band
            table[band, band_count + 2 * index + 1] = owner
    mine = lax.dynamic_index_in_dim(jnp.asarray(table), me, axis=0, keepdims=False)
    outside = jnp.sum((slot_ids >= mine[:band_count][owner_ids]).astype(jnp.int32))
    band_ids = jnp.arange(band_count, dtype=jnp.int32)
    slot_range = jnp.arange(capacity, dtype=jnp.int32)
    matches = (owner_ids[:, None, None] == band_ids[None, :, None]) & (
        slot_ids[:, None, None] == slot_range[None, None, :]
    )
    request = jnp.sum(jnp.where(matches, source[:, None, None], 0), axis=0)
    flag = jnp.broadcast_to(outside, (band_count, 1)).astype(jnp.int32)
    message = jnp.concatenate([request, flag], axis=1)
    wanted = lax.all_to_all(message, "lat", split_axis=0, concat_axis=0, tiled=True)
    covered = jnp.all(wanted[:, capacity] == 0)
    weights = dep_weight.reshape(entries)
    row_range = jnp.arange(row_count, dtype=jnp.int32)
    own = jnp.where((owner_ids == me)[:, None] & (source[:, None] == row_range[None, :]),
                    weights[:, None], 0.0)
    own_weights = jnp.sum(own.reshape(row_count, link_count, row_count), axis=1)
    total = jnp.einsum("jr,flri->flji", own_weights, tracers, precision=PRECISE)
    by_size = {}
    for index, ((_, size), pairs) in enumerate(groups):
        receiver = mine[band_count + 2 * index]
        chosen = wanted[receiver, :size]
        select = (chosen[:, None] == row_range[None, :]).astype(jnp.float32)
        outgoing = jnp.einsum("sr,flri->flsi", select, tracers, precision=PRECISE)
        incoming = lax.ppermute(outgoing, "lat", pairs)
        sender = mine[band_count + 2 * index + 1]
        hit = (owner_ids[:, None] == sender) & (slot_ids[:, None] == slot_range[None, :size])
        part = jnp.where(hit, weights[:, None], 0.0)
        part_weights = jnp.sum(part.reshape(row_count, link_count, size), axis=1)
        by_size.setdefault(size, []).append((part_weights, incoming))
    for size, items in sorted(by_size.items()):
        part_weights = jnp.stack([w for w, _ in items], axis=0)
        incoming = jnp.stack([x for _, x in items], axis=0)
        total = total + jnp.einsum("ojs,oflsi->flji", part_weights, incoming, precision=PRECISE)
    return total, covered


def departure_all(tracers, dep_owner, dep_row, dep_weight):
    band_count = lax.axis_size("lat")
    row_count, link_count = dep_owner.shape
    entries = row_count * link_count
    capacity = max(2, -(-2 * entries // band_count))
    limits, groups = near_plan(band_count, entries, capacity)
    near, covered = departure_near(
        tracers, dep_owner, dep_row, dep_weight, limits, groups, capacity
    )
    return lax.cond(
        covered,
        lambda: near,
        lambda: departure_terms(tracers, dep_owner, dep_row, dep_weight),
    )


def body(
    prognostic,
    tracers,
    zonal_courant,
    meridional_courant,
    filter_band,
    dep_owner,
    dep_row,
    dep_weight,
):
    row_count = prognostic.shape[2]
    departed = departure_all(tracers, dep_owner, dep_row, dep_weight)
    lon_padded = padded(
        jnp.concatenate([prognostic, zonal_courant[None]], axis=0), (("lon", 3),), 1, True
    )
    zonal_flux = face_flux(lon_padded[:-1], lon_padded[-1:], 3)
    lat_padded = padded(
        jnp.concatenate([prognostic, meridional_courant[None]], axis=0), (("lat", 2),), 1, False
    )
    merid_flux = face_flux(lat_padded[:-1], lat_padded[-1:], 2)
    total_rows = row_count * lax.axis_size("lat")
    face_rows = lax.axis_index("lat") * row_count + jnp.arange(row_count + 1) - 1
    merid_flux = jnp.where(
        (face_rows == total_rows - 1)[None, None, :, None], jnp.float32(0.0), merid_flux
    )
    advected = (
        prognostic
        - (zonal_flux[..., 1:] - zonal_flux[..., :-1])
        - (merid_flux[:, :, 1:] - merid_flux[:, :, :-1])
    )
    new_prognostic = polar_filter(advected, filter_band)
    return (new_prognostic, departed)


def solution(mesh):
    return jax.shard_map(
        body,
        mesh=mesh,
        in_specs=(
            P(None, None, "lat", "lon"),
            P(None, None, "lat", "lon"),
            P(None, "lat", "lon"),
            P(None, "lat", "lon"),
            P("lat"),
            P("lat", None),
            P("lat", None),
            P("lat", None),
        ),
        out_specs=(P(None, None, "lat", "lon"), P(None, None, "lat", "lon")),
        check_vma=False,
    )
```

```python
import math

import jax
import numpy as np
import jax.numpy as jnp
from jax import lax
from jax.sharding import PartitionSpec as P

PRECISE = lax.Precision.HIGHEST


def padded(value, sides, width, wrap):
    for axis, dim in sides:
        size, length = (lax.axis_size(axis), value.shape[dim])
        up = [(i, (i + 1) % size) for i in range(size if wrap else size - 1)]
        down = [(j, i) for i, j in up]
        last = lax.slice_in_dim(value, length - width, length, axis=dim)
        first = lax.slice_in_dim(value, 0, width, axis=dim)
        before = lax.ppermute(last, axis, up)
        after = lax.ppermute(first, axis, down)
        value = jnp.concatenate([before, value, after], axis=dim)
    return value


def face_flux(values, speeds, axis):
    count = values.shape[axis] - 2
    left_cells = lax.slice_in_dim(values, 0, count + 1, axis=axis)
    right_cells = lax.slice_in_dim(values, 1, count + 2, axis=axis)
    courant = lax.slice_in_dim(speeds, 0, count + 1, axis=axis)
    return 0.5 * courant * (left_cells + right_cells) - 0.5 * courant * courant * (
        right_cells - left_cells
    )


def column_factors(band_rows, length):
    column = jnp.arange(length, dtype=jnp.int32)
    half_length = length // 2
    frequency = jnp.where(column <= half_length, column, column - half_length)
    single = (column == 0) | (column == half_length)
    weights = jnp.where(single, 1.0 / length, 2.0 / length).astype(jnp.float32)
    ratios = (
        band_rows.astype(jnp.float32)[:, None]
        / jnp.maximum(frequency, 1).astype(jnp.float32)[None, :]
    )
    damping = jnp.minimum(1.0, ratios * ratios)
    return (damping - 1.0) * weights[None, :]


def column_factors(band_rows, length):
    column = jnp.arange(length, dtype=jnp.int32)
    half_length = length // 2
    frequency = jnp.where(column <= half_length, column, column - half_length)
    single = (column == 0) | (column == half_length)
    weights = jnp.where(single, 1.0 / length, 2.0 / length).astype(jnp.float32)
    ratios = (
        band_rows.astype(jnp.float32)[:, None]
        / jnp.maximum(frequency, 1).astype(jnp.float32)[None, :]
    )
    damping = jnp.minimum(1.0, ratios * ratios)
    return (damping - 1.0) * weights[None, :]


def circle_basis(length):
    half_length = length // 2
    column = jnp.arange(length, dtype=jnp.int32)
    frequency = jnp.where(column <= half_length, column, column - half_length)
    low_count = 64
    high_count = length // low_count
    low = jnp.arange(low_count, dtype=jnp.int32)
    high = jnp.arange(high_count, dtype=jnp.int32) * low_count
    scale = 2.0 * math.pi / length
    low_angle = scale * (low[:, None] * frequency[None, :] % length).astype(jnp.float32)
    high_angle = scale * (high[:, None] * frequency[None, :] % length).astype(jnp.float32)
    low_cos, low_sin = jnp.cos(low_angle), jnp.sin(low_angle)
    high_cos, high_sin = jnp.cos(high_angle), jnp.sin(high_angle)
    cos_part = high_cos[:, None] * low_cos[None] - high_sin[:, None] * low_sin[None]
    sin_part = high_sin[:, None] * low_cos[None] + high_cos[:, None] * low_sin[None]
    basis = jnp.where((column <= half_length)[None, None, :], cos_part, sin_part)
    return basis.reshape(length, length)


def departure_terms(tracers, dep_owner, dep_row, dep_weight):
    band_count = lax.axis_size("lat")
    row_count, link_count = dep_owner.shape
    entries = row_count * link_count
    capacity = max(2, -(-2 * entries // band_count))
    owner_ids = dep_owner.reshape(entries)
    source = dep_row.reshape(entries)
    positions = jnp.arange(entries)
    earlier = (owner_ids[:, None] == owner_ids[None, :]) & (positions[None, :] < positions[:, None])
    slot_ids = jnp.sum(earlier.astype(jnp.int32), axis=1)
    band_ids = jnp.arange(band_count, dtype=jnp.int32)
    slot_range = jnp.arange(capacity, dtype=jnp.int32)
    matches = (owner_ids[:, None, None] == band_ids[None, :, None]) & (
        slot_ids[:, None, None] == slot_range[None, None, :]
    )
    request = jnp.sum(jnp.where(matches, source[:, None, None], 0), axis=0)
    wanted = lax.all_to_all(request, "lat", split_axis=0, concat_axis=0, tiled=True)
    by_row = jnp.transpose(tracers, (2, 0, 1, 3))
    outgoing = by_row[wanted]
    incoming = lax.all_to_all(outgoing, "lat", split_axis=0, concat_axis=0, tiled=True)
    stacked_rows = incoming.reshape((band_count * capacity,) + incoming.shape[2:])
    picked = stacked_rows[owner_ids * capacity + slot_ids].reshape(
        (row_count, link_count) + stacked_rows.shape[1:]
    )
    summed = dep_weight[:, 0][:, None, None, None] * picked[:, 0]
    summed = summed + dep_weight[:, 1][:, None, None, None] * picked[:, 1]
    return jnp.transpose(summed, (1, 2, 0, 3))


def circle_basis(cells, length):
    half_length = length // 2
    column = jnp.arange(length, dtype=jnp.int32)
    frequency = jnp.where(column <= half_length, column, column - half_length)
    low_count = math.gcd(cells.shape[0], 64)
    low = jnp.arange(low_count, dtype=jnp.int32)
    high = cells.reshape(-1, low_count)[:, 0]
    scale = 2.0 * math.pi / length
    low_angle = scale * (low[:, None] * frequency[None, :] % length).astype(jnp.float32)
    high_angle = scale * (high[:, None] * frequency[None, :] % length).astype(jnp.float32)
    low_cos, low_sin = jnp.cos(low_angle), jnp.sin(low_angle)
    high_cos, high_sin = jnp.cos(high_angle), jnp.sin(high_angle)
    cos_part = high_cos[:, None] * low_cos[None] - high_sin[:, None] * low_sin[None]
    sin_part = high_sin[:, None] * low_cos[None] + high_cos[:, None] * low_sin[None]
    basis = jnp.where((column <= half_length)[None, None, :], cos_part, sin_part)
    return basis.reshape(cells.shape[0], length)


def polar_filter(values, band_rows):
    fields, levels, rows, block_cells = values.shape
    parts = lax.axis_size("lon")
    me = lax.axis_index("lon")
    length = block_cells * parts
    flat = values.reshape(fields * levels * rows, block_cells)
    chunk = flat.shape[0] // parts
    blocks = [lax.dynamic_slice_in_dim(flat, me * chunk, chunk, axis=0)]
    for shift in range(1, parts):
        target = (me + shift) % parts
        piece = lax.dynamic_slice_in_dim(flat, target * chunk, chunk, axis=0)
        pairs = [(i, (i + shift) % parts) for i in range(parts)]
        blocks.append(lax.ppermute(piece, "lon", pairs))
    circles = jnp.concatenate(blocks, axis=1)
    shifts = jnp.arange(parts, dtype=jnp.int32)
    sources = (me - shifts) % parts
    cells = (sources[:, None] * block_cells + jnp.arange(block_cells, dtype=jnp.int32)[None]).reshape(length)
    basis_table = circle_basis(cells, length)
    spectrum = jnp.dot(circles, basis_table, precision=lax.Precision.HIGH)
    factors = column_factors(band_rows, length)
    scaled = (spectrum.reshape(chunk // rows, rows, length) * factors[None]).reshape(chunk, length)
    change = lax.dot_general(
        scaled, basis_table, (((1,), (1,)), ((), ())), precision=lax.Precision.HIGH
    )
    returned = [change[:, :block_cells]]
    for shift in range(1, parts):
        pairs = [(i, (i - shift) % parts) for i in range(parts)]
        piece = change[:, shift * block_cells:(shift + 1) * block_cells]
        returned.append(lax.ppermute(piece, "lon", pairs))
    stacked = jnp.stack(returned, axis=0)
    order = (jnp.arange(parts, dtype=jnp.int32) - me) % parts
    ordered = jnp.take(stacked, order, axis=0)
    return values + ordered.reshape(values.shape)


def band_distance(a, b, band_count):
    return min(abs(a - b), a + b + 1, 2 * band_count - 1 - a - b)


def near_plan(band_count, entries, capacity):
    reach = min(band_count, -(-entries // capacity) + 1)
    tail = max(1, capacity // 3)
    nearest = []
    limits = np.zeros((band_count, band_count), np.int32)
    for band in range(band_count):
        order = sorted(range(band_count), key=lambda o: (band_distance(band, o, band_count), o))
        nearest.append(order[:reach])
        for owner in order[:reach]:
            limits[band, owner] = capacity
        if reach < band_count and reach > 2:
            last, before = order[reach - 1], order[reach - 2]
            if band_distance(band, last, band_count) > band_distance(band, before, band_count):
                limits[band, last] = tail
    groups = {}
    for band in range(band_count):
        for owner in nearest[band]:
            if owner != band:
                groups.setdefault((owner - band, int(limits[band, owner])), []).append((owner, band))
    merged = []
    for (offset, size), pairs in sorted(groups.items(), key=lambda g: -len(g[1])):
        for held in merged:
            sources = {o for o, _ in held[1]}
            targets = {b for _, b in held[1]}
            if held[0] == size and not sources & {o for o, _ in pairs} and not targets & {b for _, b in pairs}:
                held[1].extend(pairs)
                break
        else:
            merged.append((size, list(pairs)))
    return limits, [((index, size), pairs) for index, (size, pairs) in enumerate(merged)]


def departure_near(tracers, dep_owner, dep_row, dep_weight, limits, groups, capacity, held):
    band_count = lax.axis_size("lat")
    row_count, link_count = dep_owner.shape
    entries = row_count * link_count
    me = lax.axis_index("lat")
    owner_ids = dep_owner.reshape(entries)
    source = dep_row.reshape(entries)
    positions = jnp.arange(entries)
    earlier = (owner_ids[:, None] == owner_ids[None, :]) & (positions[None, :] < positions[:, None])
    slot_ids = jnp.sum(earlier.astype(jnp.int32), axis=1)
    table = np.zeros((band_count, band_count + 2 * len(groups)), np.int32)
    table[:, :band_count] = limits
    for index, (_, pairs) in enumerate(groups):
        table[:, band_count + 2 * index + 1] = -1
        for owner, band in pairs:
            table[owner, band_count + 2 * index] = band
            table[band, band_count + 2 * index + 1] = owner
    mine = lax.dynamic_index_in_dim(jnp.asarray(table), me, axis=0, keepdims=False)
    outside = jnp.sum((slot_ids >= mine[:band_count][owner_ids]).astype(jnp.int32))
    band_ids = jnp.arange(band_count, dtype=jnp.int32)
    slot_range = jnp.arange(capacity, dtype=jnp.int32)
    matches = (owner_ids[:, None, None] == band_ids[None, :, None]) & (
        slot_ids[:, None, None] == slot_range[None, None, :]
    )
    request = jnp.sum(jnp.where(matches, source[:, None, None], 0), axis=0)
    flag = jnp.broadcast_to(outside, (band_count, 1)).astype(jnp.int32)
    message = jnp.concatenate([request, flag], axis=1)
    wanted = lax.all_to_all(message, "lat", split_axis=0, concat_axis=0, tiled=True)
    covered = jnp.all(wanted[:, capacity] == 0)
    weights = dep_weight.reshape(entries)
    row_range = jnp.arange(row_count, dtype=jnp.int32)
    own = jnp.where((owner_ids == me)[:, None] & (source[:, None] == row_range[None, :]),
                    weights[:, None], 0.0)
    own_weights = jnp.sum(own.reshape(row_count, link_count, row_count), axis=1)
    total = jnp.einsum("jr,flri->flji", own_weights, tracers, precision=PRECISE)
    by_size = {}
    sending = []
    for index, ((_, size), pairs) in enumerate(groups):
        receiver = mine[band_count + 2 * index]
        chosen = wanted[receiver, :size]
        select = (chosen[:, None] == row_range[None, :]).astype(jnp.float32)
        sending.append(jnp.einsum("sr,flri->flsi", select, tracers, precision=PRECISE))
    sending, held = lax.optimization_barrier((sending, held))
    for index, ((_, size), pairs) in enumerate(groups):
        incoming = lax.ppermute(sending[index], "lat", pairs)
        sender = mine[band_count + 2 * index + 1]
        hit = (owner_ids[:, None] == sender) & (slot_ids[:, None] == slot_range[None, :size])
        part = jnp.where(hit, weights[:, None], 0.0)
        part_weights = jnp.sum(part.reshape(row_count, link_count, size), axis=1)
        by_size.setdefault(size, []).append((part_weights, incoming))
    for size, items in sorted(by_size.items()):
        part_weights = jnp.stack([w for w, _ in items], axis=0)
        incoming = jnp.stack([x for _, x in items], axis=0)
        total = total + jnp.einsum("ojs,oflsi->flji", part_weights, incoming, precision=PRECISE)
    return total, covered, held


def departure_all(tracers, dep_owner, dep_row, dep_weight, held):
    band_count = lax.axis_size("lat")
    row_count, link_count = dep_owner.shape
    entries = row_count * link_count
    capacity = max(2, -(-2 * entries // band_count))
    limits, groups = near_plan(band_count, entries, capacity)
    near, covered, held = departure_near(
        tracers, dep_owner, dep_row, dep_weight, limits, groups, capacity, held
    )
    departed = lax.cond(
        covered,
        lambda: near,
        lambda: departure_terms(tracers, dep_owner, dep_row, dep_weight),
    )
    return departed, held


def body(
    prognostic,
    tracers,
    zonal_courant,
    meridional_courant,
    filter_band,
    dep_owner,
    dep_row,
    dep_weight,
):
    row_count = prognostic.shape[2]
    departed, (prognostic, zonal_courant, meridional_courant) = departure_all(
        tracers, dep_owner, dep_row, dep_weight, (prognostic, zonal_courant, meridional_courant)
    )
    lon_padded = padded(
        jnp.concatenate([prognostic, zonal_courant[None]], axis=0), (("lon", 3),), 1, True
    )
    zonal_flux = face_flux(lon_padded[:-1], lon_padded[-1:], 3)
    lat_padded = padded(
        jnp.concatenate([prognostic, meridional_courant[None]], axis=0), (("lat", 2),), 1, False
    )
    merid_flux = face_flux(lat_padded[:-1], lat_padded[-1:], 2)
    total_rows = row_count * lax.axis_size("lat")
    face_rows = lax.axis_index("lat") * row_count + jnp.arange(row_count + 1) - 1
    merid_flux = jnp.where(
        (face_rows == total_rows - 1)[None, None, :, None], jnp.float32(0.0), merid_flux
    )
    advected = (
        prognostic
        - (zonal_flux[..., 1:] - zonal_flux[..., :-1])
        - (merid_flux[:, :, 1:] - merid_flux[:, :, :-1])
    )
    new_prognostic = polar_filter(advected, filter_band)
    return (new_prognostic, departed)


def solution(mesh):
    return jax.shard_map(
        body,
        mesh=mesh,
        in_specs=(
            P(None, None, "lat", "lon"),
            P(None, None, "lat", "lon"),
            P(None, "lat", "lon"),
            P(None, "lat", "lon"),
            P("lat"),
            P("lat", None),
            P("lat", None),
            P("lat", None),
        ),
        out_specs=(P(None, None, "lat", "lon"), P(None, None, "lat", "lon")),
        check_vma=False,
    )
```

```python
import math

import jax
import numpy as np
import jax.numpy as jnp
from jax import lax
from jax.sharding import PartitionSpec as P

PRECISE = lax.Precision.HIGHEST


def padded(value, sides, width, wrap):
    for axis, dim in sides:
        size, length = (lax.axis_size(axis), value.shape[dim])
        up = [(i, (i + 1) % size) for i in range(size if wrap else size - 1)]
        down = [(j, i) for i, j in up]
        last = lax.slice_in_dim(value, length - width, length, axis=dim)
        first = lax.slice_in_dim(value, 0, width, axis=dim)
        before = lax.ppermute(last, axis, up)
        after = lax.ppermute(first, axis, down)
        value = jnp.concatenate([before, value, after], axis=dim)
    return value


def face_flux(values, speeds, axis):
    count = values.shape[axis] - 2
    left_cells = lax.slice_in_dim(values, 0, count + 1, axis=axis)
    right_cells = lax.slice_in_dim(values, 1, count + 2, axis=axis)
    courant = lax.slice_in_dim(speeds, 0, count + 1, axis=axis)
    return 0.5 * courant * (left_cells + right_cells) - 0.5 * courant * courant * (
        right_cells - left_cells
    )


def column_factors(band_rows, length):
    column = jnp.arange(length, dtype=jnp.int32)
    half_length = length // 2
    frequency = jnp.where(column <= half_length, column, column - half_length)
    single = (column == 0) | (column == half_length)
    weights = jnp.where(single, 1.0 / length, 2.0 / length).astype(jnp.float32)
    ratios = (
        band_rows.astype(jnp.float32)[:, None]
        / jnp.maximum(frequency, 1).astype(jnp.float32)[None, :]
    )
    damping = jnp.minimum(1.0, ratios * ratios)
    return (damping - 1.0) * weights[None, :]


def column_factors(band_rows, length):
    column = jnp.arange(length, dtype=jnp.int32)
    half_length = length // 2
    frequency = jnp.where(column <= half_length, column, column - half_length)
    single = (column == 0) | (column == half_length)
    weights = jnp.where(single, 1.0 / length, 2.0 / length).astype(jnp.float32)
    ratios = (
        band_rows.astype(jnp.float32)[:, None]
        / jnp.maximum(frequency, 1).astype(jnp.float32)[None, :]
    )
    damping = jnp.minimum(1.0, ratios * ratios)
    return (damping - 1.0) * weights[None, :]


def circle_basis(length):
    half_length = length // 2
    column = jnp.arange(length, dtype=jnp.int32)
    frequency = jnp.where(column <= half_length, column, column - half_length)
    low_count = 64
    high_count = length // low_count
    low = jnp.arange(low_count, dtype=jnp.int32)
    high = jnp.arange(high_count, dtype=jnp.int32) * low_count
    scale = 2.0 * math.pi / length
    low_angle = scale * (low[:, None] * frequency[None, :] % length).astype(jnp.float32)
    high_angle = scale * (high[:, None] * frequency[None, :] % length).astype(jnp.float32)
    low_cos, low_sin = jnp.cos(low_angle), jnp.sin(low_angle)
    high_cos, high_sin = jnp.cos(high_angle), jnp.sin(high_angle)
    cos_part = high_cos[:, None] * low_cos[None] - high_sin[:, None] * low_sin[None]
    sin_part = high_sin[:, None] * low_cos[None] + high_cos[:, None] * low_sin[None]
    basis = jnp.where((column <= half_length)[None, None, :], cos_part, sin_part)
    return basis.reshape(length, length)


def departure_terms(tracers, dep_owner, dep_row, dep_weight):
    band_count = lax.axis_size("lat")
    row_count, link_count = dep_owner.shape
    entries = row_count * link_count
    capacity = max(2, -(-2 * entries // band_count))
    owner_ids = dep_owner.reshape(entries)
    source = dep_row.reshape(entries)
    positions = jnp.arange(entries)
    earlier = (owner_ids[:, None] == owner_ids[None, :]) & (positions[None, :] < positions[:, None])
    slot_ids = jnp.sum(earlier.astype(jnp.int32), axis=1)
    band_ids = jnp.arange(band_count, dtype=jnp.int32)
    slot_range = jnp.arange(capacity, dtype=jnp.int32)
    matches = (owner_ids[:, None, None] == band_ids[None, :, None]) & (
        slot_ids[:, None, None] == slot_range[None, None, :]
    )
    request = jnp.sum(jnp.where(matches, source[:, None, None], 0), axis=0)
    wanted = lax.all_to_all(request, "lat", split_axis=0, concat_axis=0, tiled=True)
    by_row = jnp.transpose(tracers, (2, 0, 1, 3))
    outgoing = by_row[wanted]
    incoming = lax.all_to_all(outgoing, "lat", split_axis=0, concat_axis=0, tiled=True)
    stacked_rows = incoming.reshape((band_count * capacity,) + incoming.shape[2:])
    picked = stacked_rows[owner_ids * capacity + slot_ids].reshape(
        (row_count, link_count) + stacked_rows.shape[1:]
    )
    summed = dep_weight[:, 0][:, None, None, None] * picked[:, 0]
    summed = summed + dep_weight[:, 1][:, None, None, None] * picked[:, 1]
    return jnp.transpose(summed, (1, 2, 0, 3))


def circle_basis(cells, length):
    half_length = length // 2
    column = jnp.arange(length, dtype=jnp.int32)
    frequency = jnp.where(column <= half_length, column, column - half_length)
    low_count = math.gcd(cells.shape[0], 64)
    low = jnp.arange(low_count, dtype=jnp.int32)
    high = cells.reshape(-1, low_count)[:, 0]
    scale = 2.0 * math.pi / length
    low_angle = scale * (low[:, None] * frequency[None, :] % length).astype(jnp.float32)
    high_angle = scale * (high[:, None] * frequency[None, :] % length).astype(jnp.float32)
    low_cos, low_sin = jnp.cos(low_angle), jnp.sin(low_angle)
    high_cos, high_sin = jnp.cos(high_angle), jnp.sin(high_angle)
    cos_part = high_cos[:, None] * low_cos[None] - high_sin[:, None] * low_sin[None]
    sin_part = high_sin[:, None] * low_cos[None] + high_cos[:, None] * low_sin[None]
    basis = jnp.where((column <= half_length)[None, None, :], cos_part, sin_part)
    return basis.reshape(cells.shape[0], length)


def polar_filter(values, band_rows):
    fields, levels, rows, block_cells = values.shape
    parts = lax.axis_size("lon")
    me = lax.axis_index("lon")
    length = block_cells * parts
    flat = values.reshape(fields * levels * rows, block_cells)
    chunk = flat.shape[0] // parts
    circles = lax.all_to_all(flat, "lon", split_axis=0, concat_axis=1, tiled=True)
    cells = jnp.arange(length, dtype=jnp.int32)
    basis_table = circle_basis(cells, length)
    spectrum = jnp.dot(circles, basis_table, precision=lax.Precision.HIGH)
    factors = column_factors(band_rows, length)
    scaled = (spectrum.reshape(chunk // rows, rows, length) * factors[None]).reshape(chunk, length)
    change = lax.dot_general(
        scaled, basis_table, (((1,), (1,)), ((), ())), precision=lax.Precision.HIGH
    )
    back = lax.all_to_all(change, "lon", split_axis=1, concat_axis=0, tiled=True)
    return values + back.reshape(values.shape)


def band_distance(a, b, band_count):
    return min(abs(a - b), a + b + 1, 2 * band_count - 1 - a - b)


def near_plan(band_count, entries, capacity):
    reach = min(band_count, -(-entries // capacity) + 1)
    tail = max(1, capacity // 3)
    nearest = []
    limits = np.zeros((band_count, band_count), np.int32)
    for band in range(band_count):
        order = sorted(range(band_count), key=lambda o: (band_distance(band, o, band_count), o))
        nearest.append(order[:reach])
        for owner in order[:reach]:
            limits[band, owner] = capacity
        if reach < band_count and reach > 2:
            last, before = order[reach - 1], order[reach - 2]
            if band_distance(band, last, band_count) > band_distance(band, before, band_count):
                limits[band, last] = tail
    groups = {}
    for band in range(band_count):
        for owner in nearest[band]:
            if owner != band:
                groups.setdefault((owner - band, int(limits[band, owner])), []).append((owner, band))
    merged = []
    for (offset, size), pairs in sorted(groups.items(), key=lambda g: -len(g[1])):
        for held in merged:
            sources = {o for o, _ in held[1]}
            targets = {b for _, b in held[1]}
            if held[0] == size and not sources & {o for o, _ in pairs} and not targets & {b for _, b in pairs}:
                held[1].extend(pairs)
                break
        else:
            merged.append((size, list(pairs)))
    return limits, [((index, size), pairs) for index, (size, pairs) in enumerate(merged)]


def departure_near(tracers, dep_owner, dep_row, dep_weight, limits, groups, capacity, held):
    band_count = lax.axis_size("lat")
    row_count, link_count = dep_owner.shape
    entries = row_count * link_count
    me = lax.axis_index("lat")
    owner_ids = dep_owner.reshape(entries)
    source = dep_row.reshape(entries)
    positions = jnp.arange(entries)
    earlier = (owner_ids[:, None] == owner_ids[None, :]) & (positions[None, :] < positions[:, None])
    slot_ids = jnp.sum(earlier.astype(jnp.int32), axis=1)
    table = np.zeros((band_count, band_count + 2 * len(groups)), np.int32)
    table[:, :band_count] = limits
    for index, (_, pairs) in enumerate(groups):
        table[:, band_count + 2 * index + 1] = -1
        for owner, band in pairs:
            table[owner, band_count + 2 * index] = band
            table[band, band_count + 2 * index + 1] = owner
    mine = lax.dynamic_index_in_dim(jnp.asarray(table), me, axis=0, keepdims=False)
    outside = jnp.sum((slot_ids >= mine[:band_count][owner_ids]).astype(jnp.int32))
    band_ids = jnp.arange(band_count, dtype=jnp.int32)
    slot_range = jnp.arange(capacity, dtype=jnp.int32)
    matches = (owner_ids[:, None, None] == band_ids[None, :, None]) & (
        slot_ids[:, None, None] == slot_range[None, None, :]
    )
    request = jnp.sum(jnp.where(matches, source[:, None, None], 0), axis=0)
    flag = jnp.broadcast_to(outside, (band_count, 1)).astype(jnp.int32)
    message = jnp.concatenate([request, flag], axis=1)
    wanted = lax.all_to_all(message, "lat", split_axis=0, concat_axis=0, tiled=True)
    covered = jnp.all(wanted[:, capacity] == 0)
    weights = dep_weight.reshape(entries)
    row_range = jnp.arange(row_count, dtype=jnp.int32)
    own = jnp.where((owner_ids == me)[:, None] & (source[:, None] == row_range[None, :]),
                    weights[:, None], 0.0)
    own_weights = jnp.sum(own.reshape(row_count, link_count, row_count), axis=1)
    total = jnp.einsum("jr,flri->flji", own_weights, tracers, precision=PRECISE)
    by_size = {}
    for index, ((_, size), pairs) in enumerate(groups):
        receiver = mine[band_count + 2 * index]
        chosen = wanted[receiver, :size]
        select = (chosen[:, None] == row_range[None, :]).astype(jnp.float32)
        outgoing = jnp.einsum("sr,flri->flsi", select, tracers, precision=PRECISE)
        incoming = lax.ppermute(outgoing, "lat", pairs)
        incoming, held = lax.optimization_barrier((incoming, held))
        sender = mine[band_count + 2 * index + 1]
        hit = (owner_ids[:, None] == sender) & (slot_ids[:, None] == slot_range[None, :size])
        part = jnp.where(hit, weights[:, None], 0.0)
        part_weights = jnp.sum(part.reshape(row_count, link_count, size), axis=1)
        by_size.setdefault(size, []).append((part_weights, incoming))
    for size, items in sorted(by_size.items()):
        part_weights = jnp.stack([w for w, _ in items], axis=0)
        incoming = jnp.stack([x for _, x in items], axis=0)
        total = total + jnp.einsum("ojs,oflsi->flji", part_weights, incoming, precision=PRECISE)
    return total, covered, held


def departure_all(tracers, dep_owner, dep_row, dep_weight, held):
    band_count = lax.axis_size("lat")
    row_count, link_count = dep_owner.shape
    entries = row_count * link_count
    capacity = max(2, -(-2 * entries // band_count))
    limits, groups = near_plan(band_count, entries, capacity)
    near, covered, held = departure_near(
        tracers, dep_owner, dep_row, dep_weight, limits, groups, capacity, held
    )
    departed = lax.cond(
        covered,
        lambda: near,
        lambda: departure_terms(tracers, dep_owner, dep_row, dep_weight),
    )
    return departed, held


def body(
    prognostic,
    tracers,
    zonal_courant,
    meridional_courant,
    filter_band,
    dep_owner,
    dep_row,
    dep_weight,
):
    row_count = prognostic.shape[2]
    lon_padded = padded(
        jnp.concatenate([prognostic, zonal_courant[None]], axis=0), (("lon", 3),), 1, True
    )
    zonal_flux = face_flux(lon_padded[:-1], lon_padded[-1:], 3)
    lat_padded = padded(
        jnp.concatenate([prognostic, meridional_courant[None]], axis=0), (("lat", 2),), 1, False
    )
    merid_flux = face_flux(lat_padded[:-1], lat_padded[-1:], 2)
    total_rows = row_count * lax.axis_size("lat")
    face_rows = lax.axis_index("lat") * row_count + jnp.arange(row_count + 1) - 1
    merid_flux = jnp.where(
        (face_rows == total_rows - 1)[None, None, :, None], jnp.float32(0.0), merid_flux
    )
    advected = (
        prognostic
        - (zonal_flux[..., 1:] - zonal_flux[..., :-1])
        - (merid_flux[:, :, 1:] - merid_flux[:, :, :-1])
    )
    new_prognostic = polar_filter(advected, filter_band)
    departed, new_prognostic = departure_all(tracers, dep_owner, dep_row, dep_weight, new_prognostic)
    return (new_prognostic, departed)


def solution(mesh):
    return jax.shard_map(
        body,
        mesh=mesh,
        in_specs=(
            P(None, None, "lat", "lon"),
            P(None, None, "lat", "lon"),
            P(None, "lat", "lon"),
            P(None, "lat", "lon"),
            P("lat"),
            P("lat", None),
            P("lat", None),
            P("lat", None),
        ),
        out_specs=(P(None, None, "lat", "lon"), P(None, None, "lat", "lon")),
        check_vma=False,
    )
```

```python
import math

import jax
import numpy as np
import jax.numpy as jnp
from jax import lax
from jax.sharding import PartitionSpec as P

PRECISE = lax.Precision.HIGHEST


def padded(value, sides, width, wrap):
    for axis, dim in sides:
        size, length = (lax.axis_size(axis), value.shape[dim])
        up = [(i, (i + 1) % size) for i in range(size if wrap else size - 1)]
        down = [(j, i) for i, j in up]
        last = lax.slice_in_dim(value, length - width, length, axis=dim)
        first = lax.slice_in_dim(value, 0, width, axis=dim)
        before = lax.ppermute(last, axis, up)
        after = lax.ppermute(first, axis, down)
        value = jnp.concatenate([before, value, after], axis=dim)
    return value


def face_flux(values, speeds, axis):
    count = values.shape[axis] - 2
    left_cells = lax.slice_in_dim(values, 0, count + 1, axis=axis)
    right_cells = lax.slice_in_dim(values, 1, count + 2, axis=axis)
    courant = lax.slice_in_dim(speeds, 0, count + 1, axis=axis)
    return 0.5 * courant * (left_cells + right_cells) - 0.5 * courant * courant * (
        right_cells - left_cells
    )


def column_factors(band_rows, length):
    column = jnp.arange(length, dtype=jnp.int32)
    half_length = length // 2
    frequency = jnp.where(column <= half_length, column, column - half_length)
    single = (column == 0) | (column == half_length)
    weights = jnp.where(single, 1.0 / length, 2.0 / length).astype(jnp.float32)
    ratios = (
        band_rows.astype(jnp.float32)[:, None]
        / jnp.maximum(frequency, 1).astype(jnp.float32)[None, :]
    )
    damping = jnp.minimum(1.0, ratios * ratios)
    return (damping - 1.0) * weights[None, :]


def column_factors(band_rows, length):
    column = jnp.arange(length, dtype=jnp.int32)
    half_length = length // 2
    frequency = jnp.where(column <= half_length, column, column - half_length)
    single = (column == 0) | (column == half_length)
    weights = jnp.where(single, 1.0 / length, 2.0 / length).astype(jnp.float32)
    ratios = (
        band_rows.astype(jnp.float32)[:, None]
        / jnp.maximum(frequency, 1).astype(jnp.float32)[None, :]
    )
    damping = jnp.minimum(1.0, ratios * ratios)
    return (damping - 1.0) * weights[None, :]


def circle_basis(length):
    half_length = length // 2
    column = jnp.arange(length, dtype=jnp.int32)
    frequency = jnp.where(column <= half_length, column, column - half_length)
    low_count = 64
    high_count = length // low_count
    low = jnp.arange(low_count, dtype=jnp.int32)
    high = jnp.arange(high_count, dtype=jnp.int32) * low_count
    scale = 2.0 * math.pi / length
    low_angle = scale * (low[:, None] * frequency[None, :] % length).astype(jnp.float32)
    high_angle = scale * (high[:, None] * frequency[None, :] % length).astype(jnp.float32)
    low_cos, low_sin = jnp.cos(low_angle), jnp.sin(low_angle)
    high_cos, high_sin = jnp.cos(high_angle), jnp.sin(high_angle)
    cos_part = high_cos[:, None] * low_cos[None] - high_sin[:, None] * low_sin[None]
    sin_part = high_sin[:, None] * low_cos[None] + high_cos[:, None] * low_sin[None]
    basis = jnp.where((column <= half_length)[None, None, :], cos_part, sin_part)
    return basis.reshape(length, length)


def departure_terms(tracers, dep_owner, dep_row, dep_weight):
    band_count = lax.axis_size("lat")
    row_count, link_count = dep_owner.shape
    entries = row_count * link_count
    capacity = max(2, -(-2 * entries // band_count))
    owner_ids = dep_owner.reshape(entries)
    source = dep_row.reshape(entries)
    positions = jnp.arange(entries)
    earlier = (owner_ids[:, None] == owner_ids[None, :]) & (positions[None, :] < positions[:, None])
    slot_ids = jnp.sum(earlier.astype(jnp.int32), axis=1)
    band_ids = jnp.arange(band_count, dtype=jnp.int32)
    slot_range = jnp.arange(capacity, dtype=jnp.int32)
    matches = (owner_ids[:, None, None] == band_ids[None, :, None]) & (
        slot_ids[:, None, None] == slot_range[None, None, :]
    )
    request = jnp.sum(jnp.where(matches, source[:, None, None], 0), axis=0)
    wanted = lax.all_to_all(request, "lat", split_axis=0, concat_axis=0, tiled=True)
    by_row = jnp.transpose(tracers, (2, 0, 1, 3))
    outgoing = by_row[wanted]
    incoming = lax.all_to_all(outgoing, "lat", split_axis=0, concat_axis=0, tiled=True)
    stacked_rows = incoming.reshape((band_count * capacity,) + incoming.shape[2:])
    picked = stacked_rows[owner_ids * capacity + slot_ids].reshape(
        (row_count, link_count) + stacked_rows.shape[1:]
    )
    summed = dep_weight[:, 0][:, None, None, None] * picked[:, 0]
    summed = summed + dep_weight[:, 1][:, None, None, None] * picked[:, 1]
    return jnp.transpose(summed, (1, 2, 0, 3))


def circle_basis(cells, length):
    half_length = length // 2
    column = jnp.arange(length, dtype=jnp.int32)
    frequency = jnp.where(column <= half_length, column, column - half_length)
    low_count = math.gcd(cells.shape[0], 64)
    low = jnp.arange(low_count, dtype=jnp.int32)
    high = cells.reshape(-1, low_count)[:, 0]
    scale = 2.0 * math.pi / length
    low_angle = scale * (low[:, None] * frequency[None, :] % length).astype(jnp.float32)
    high_angle = scale * (high[:, None] * frequency[None, :] % length).astype(jnp.float32)
    low_cos, low_sin = jnp.cos(low_angle), jnp.sin(low_angle)
    high_cos, high_sin = jnp.cos(high_angle), jnp.sin(high_angle)
    cos_part = high_cos[:, None] * low_cos[None] - high_sin[:, None] * low_sin[None]
    sin_part = high_sin[:, None] * low_cos[None] + high_cos[:, None] * low_sin[None]
    basis = jnp.where((column <= half_length)[None, None, :], cos_part, sin_part)
    return basis.reshape(cells.shape[0], length)


def polar_filter(values, band_rows):
    fields, levels, rows, block_cells = values.shape
    parts = lax.axis_size("lon")
    me = lax.axis_index("lon")
    length = block_cells * parts
    flat = values.reshape(fields * levels * rows, block_cells)
    chunk = flat.shape[0] // parts
    blocks = [lax.dynamic_slice_in_dim(flat, me * chunk, chunk, axis=0)]
    for shift in range(1, parts):
        target = (me + shift) % parts
        piece = lax.dynamic_slice_in_dim(flat, target * chunk, chunk, axis=0)
        pairs = [(i, (i + shift) % parts) for i in range(parts)]
        blocks.append(lax.ppermute(piece, "lon", pairs))
    circles = jnp.concatenate(blocks, axis=1)
    shifts = jnp.arange(parts, dtype=jnp.int32)
    sources = (me - shifts) % parts
    cells = (sources[:, None] * block_cells + jnp.arange(block_cells, dtype=jnp.int32)[None]).reshape(length)
    basis_table = circle_basis(cells, length)
    spectrum = jnp.dot(circles, basis_table, precision=lax.Precision.HIGH)
    factors = column_factors(band_rows, length)
    scaled = (spectrum.reshape(chunk // rows, rows, length) * factors[None]).reshape(chunk, length)
    change = lax.dot_general(
        scaled, basis_table, (((1,), (1,)), ((), ())), precision=lax.Precision.HIGH
    )
    returned = [change[:, :block_cells]]
    for shift in range(1, parts):
        pairs = [(i, (i - shift) % parts) for i in range(parts)]
        piece = change[:, shift * block_cells:(shift + 1) * block_cells]
        returned.append(lax.ppermute(piece, "lon", pairs))
    stacked = jnp.stack(returned, axis=0)
    order = (jnp.arange(parts, dtype=jnp.int32) - me) % parts
    ordered = jnp.take(stacked, order, axis=0)
    return values + ordered.reshape(values.shape)


def band_distance(a, b, band_count):
    return min(abs(a - b), a + b + 1, 2 * band_count - 1 - a - b)


def near_plan(band_count, entries, capacity):
    reach = min(band_count, -(-entries // capacity) + 1)
    tail = max(1, capacity // 3)
    nearest = []
    limits = np.zeros((band_count, band_count), np.int32)
    for band in range(band_count):
        order = sorted(range(band_count), key=lambda o: (band_distance(band, o, band_count), o))
        nearest.append(order[:reach])
        for owner in order[:reach]:
            limits[band, owner] = capacity
        if reach < band_count and reach > 2:
            last, before = order[reach - 1], order[reach - 2]
            if band_distance(band, last, band_count) > band_distance(band, before, band_count):
                limits[band, last] = tail
    groups = {}
    for band in range(band_count):
        for owner in nearest[band]:
            if owner != band:
                groups.setdefault((owner - band, int(limits[band, owner])), []).append((owner, band))
    merged = []
    for (offset, size), pairs in sorted(groups.items(), key=lambda g: -len(g[1])):
        for held in merged:
            sources = {o for o, _ in held[1]}
            targets = {b for _, b in held[1]}
            if held[0] == size and not sources & {o for o, _ in pairs} and not targets & {b for _, b in pairs}:
                held[1].extend(pairs)
                break
        else:
            merged.append((size, list(pairs)))
    return limits, [((index, size), pairs) for index, (size, pairs) in enumerate(merged)]


def departure_near(tracers, dep_owner, dep_row, dep_weight, limits, groups, capacity, held):
    band_count = lax.axis_size("lat")
    row_count, link_count = dep_owner.shape
    entries = row_count * link_count
    me = lax.axis_index("lat")
    owner_ids = dep_owner.reshape(entries)
    source = dep_row.reshape(entries)
    positions = jnp.arange(entries)
    earlier = (owner_ids[:, None] == owner_ids[None, :]) & (positions[None, :] < positions[:, None])
    slot_ids = jnp.sum(earlier.astype(jnp.int32), axis=1)
    table = np.zeros((band_count, band_count + 2 * len(groups)), np.int32)
    table[:, :band_count] = limits
    for index, (_, pairs) in enumerate(groups):
        table[:, band_count + 2 * index + 1] = -1
        for owner, band in pairs:
            table[owner, band_count + 2 * index] = band
            table[band, band_count + 2 * index + 1] = owner
    mine = lax.dynamic_index_in_dim(jnp.asarray(table), me, axis=0, keepdims=False)
    outside = jnp.sum((slot_ids >= mine[:band_count][owner_ids]).astype(jnp.int32))
    band_ids = jnp.arange(band_count, dtype=jnp.int32)
    slot_range = jnp.arange(capacity, dtype=jnp.int32)
    matches = (owner_ids[:, None, None] == band_ids[None, :, None]) & (
        slot_ids[:, None, None] == slot_range[None, None, :]
    )
    request = jnp.sum(jnp.where(matches, source[:, None, None], 0), axis=0)
    flag = jnp.broadcast_to(outside, (band_count, 1)).astype(jnp.int32)
    message = jnp.concatenate([request, flag], axis=1)
    wanted = lax.all_to_all(message, "lat", split_axis=0, concat_axis=0, tiled=True)
    covered = jnp.all(wanted[:, capacity] == 0)
    weights = dep_weight.reshape(entries)
    row_range = jnp.arange(row_count, dtype=jnp.int32)
    own = jnp.where((owner_ids == me)[:, None] & (source[:, None] == row_range[None, :]),
                    weights[:, None], 0.0)
    own_weights = jnp.sum(own.reshape(row_count, link_count, row_count), axis=1)
    total = jnp.einsum("jr,flri->flji", own_weights, tracers, precision=PRECISE)
    by_size = {}
    for index, ((_, size), pairs) in enumerate(groups):
        receiver = mine[band_count + 2 * index]
        chosen = wanted[receiver, :size]
        select = (chosen[:, None] == row_range[None, :]).astype(jnp.float32)
        outgoing = jnp.einsum("sr,flri->flsi", select, tracers, precision=PRECISE)
        incoming = lax.ppermute(outgoing, "lat", pairs)
        incoming, held = lax.optimization_barrier((incoming, held))
        sender = mine[band_count + 2 * index + 1]
        hit = (owner_ids[:, None] == sender) & (slot_ids[:, None] == slot_range[None, :size])
        part = jnp.where(hit, weights[:, None], 0.0)
        part_weights = jnp.sum(part.reshape(row_count, link_count, size), axis=1)
        by_size.setdefault(size, []).append((part_weights, incoming))
    for size, items in sorted(by_size.items()):
        part_weights = jnp.stack([w for w, _ in items], axis=0)
        incoming = jnp.stack([x for _, x in items], axis=0)
        total = total + jnp.einsum("ojs,oflsi->flji", part_weights, incoming, precision=PRECISE)
    return total, covered, held


def departure_all(tracers, dep_owner, dep_row, dep_weight, held):
    band_count = lax.axis_size("lat")
    row_count, link_count = dep_owner.shape
    entries = row_count * link_count
    capacity = max(2, -(-2 * entries // band_count))
    limits, groups = near_plan(band_count, entries, capacity)
    near, covered, held = departure_near(
        tracers, dep_owner, dep_row, dep_weight, limits, groups, capacity, held
    )
    departed = lax.cond(
        covered,
        lambda: near,
        lambda: departure_terms(tracers, dep_owner, dep_row, dep_weight),
    )
    return departed, held


def body(
    prognostic,
    tracers,
    zonal_courant,
    meridional_courant,
    filter_band,
    dep_owner,
    dep_row,
    dep_weight,
):
    row_count = prognostic.shape[2]
    lon_padded = padded(
        jnp.concatenate([prognostic, zonal_courant[None]], axis=0), (("lon", 3),), 1, True
    )
    zonal_flux = face_flux(lon_padded[:-1], lon_padded[-1:], 3)
    lat_padded = padded(
        jnp.concatenate([prognostic, meridional_courant[None]], axis=0), (("lat", 2),), 1, False
    )
    merid_flux = face_flux(lat_padded[:-1], lat_padded[-1:], 2)
    total_rows = row_count * lax.axis_size("lat")
    face_rows = lax.axis_index("lat") * row_count + jnp.arange(row_count + 1) - 1
    merid_flux = jnp.where(
        (face_rows == total_rows - 1)[None, None, :, None], jnp.float32(0.0), merid_flux
    )
    advected = (
        prognostic
        - (zonal_flux[..., 1:] - zonal_flux[..., :-1])
        - (merid_flux[:, :, 1:] - merid_flux[:, :, :-1])
    )
    new_prognostic = polar_filter(advected, filter_band)
    departed, new_prognostic = departure_all(tracers, dep_owner, dep_row, dep_weight, new_prognostic)
    return (new_prognostic, departed)


def solution(mesh):
    return jax.shard_map(
        body,
        mesh=mesh,
        in_specs=(
            P(None, None, "lat", "lon"),
            P(None, None, "lat", "lon"),
            P(None, "lat", "lon"),
            P(None, "lat", "lon"),
            P("lat"),
            P("lat", None),
            P("lat", None),
            P("lat", None),
        ),
        out_specs=(P(None, None, "lat", "lon"), P(None, None, "lat", "lon")),
        check_vma=False,
    )
```

```python
import math

import jax
import numpy as np
import jax.numpy as jnp
from jax import lax
from jax.sharding import PartitionSpec as P

PRECISE = lax.Precision.HIGHEST


def padded(value, sides, width, wrap):
    for axis, dim in sides:
        size, length = (lax.axis_size(axis), value.shape[dim])
        up = [(i, (i + 1) % size) for i in range(size if wrap else size - 1)]
        down = [(j, i) for i, j in up]
        last = lax.slice_in_dim(value, length - width, length, axis=dim)
        first = lax.slice_in_dim(value, 0, width, axis=dim)
        before = lax.ppermute(last, axis, up)
        after = lax.ppermute(first, axis, down)
        value = jnp.concatenate([before, value, after], axis=dim)
    return value


def face_flux(values, speeds, axis):
    count = values.shape[axis] - 2
    left_cells = lax.slice_in_dim(values, 0, count + 1, axis=axis)
    right_cells = lax.slice_in_dim(values, 1, count + 2, axis=axis)
    courant = lax.slice_in_dim(speeds, 0, count + 1, axis=axis)
    return 0.5 * courant * (left_cells + right_cells) - 0.5 * courant * courant * (
        right_cells - left_cells
    )


def column_factors(band_rows, length):
    column = jnp.arange(length, dtype=jnp.int32)
    half_length = length // 2
    frequency = jnp.where(column <= half_length, column, column - half_length)
    single = (column == 0) | (column == half_length)
    weights = jnp.where(single, 1.0 / length, 2.0 / length).astype(jnp.float32)
    ratios = (
        band_rows.astype(jnp.float32)[:, None]
        / jnp.maximum(frequency, 1).astype(jnp.float32)[None, :]
    )
    damping = jnp.minimum(1.0, ratios * ratios)
    return (damping - 1.0) * weights[None, :]


def column_factors(band_rows, length):
    column = jnp.arange(length, dtype=jnp.int32)
    half_length = length // 2
    frequency = jnp.where(column <= half_length, column, column - half_length)
    single = (column == 0) | (column == half_length)
    weights = jnp.where(single, 1.0 / length, 2.0 / length).astype(jnp.float32)
    ratios = (
        band_rows.astype(jnp.float32)[:, None]
        / jnp.maximum(frequency, 1).astype(jnp.float32)[None, :]
    )
    damping = jnp.minimum(1.0, ratios * ratios)
    return (damping - 1.0) * weights[None, :]


def circle_basis(length):
    half_length = length // 2
    column = jnp.arange(length, dtype=jnp.int32)
    frequency = jnp.where(column <= half_length, column, column - half_length)
    low_count = 64
    high_count = length // low_count
    low = jnp.arange(low_count, dtype=jnp.int32)
    high = jnp.arange(high_count, dtype=jnp.int32) * low_count
    scale = 2.0 * math.pi / length
    low_angle = scale * (low[:, None] * frequency[None, :] % length).astype(jnp.float32)
    high_angle = scale * (high[:, None] * frequency[None, :] % length).astype(jnp.float32)
    low_cos, low_sin = jnp.cos(low_angle), jnp.sin(low_angle)
    high_cos, high_sin = jnp.cos(high_angle), jnp.sin(high_angle)
    cos_part = high_cos[:, None] * low_cos[None] - high_sin[:, None] * low_sin[None]
    sin_part = high_sin[:, None] * low_cos[None] + high_cos[:, None] * low_sin[None]
    basis = jnp.where((column <= half_length)[None, None, :], cos_part, sin_part)
    return basis.reshape(length, length)


def departure_terms(tracers, dep_owner, dep_row, dep_weight):
    band_count = lax.axis_size("lat")
    row_count, link_count = dep_owner.shape
    entries = row_count * link_count
    capacity = max(2, -(-2 * entries // band_count))
    owner_ids = dep_owner.reshape(entries)
    source = dep_row.reshape(entries)
    positions = jnp.arange(entries)
    earlier = (owner_ids[:, None] == owner_ids[None, :]) & (positions[None, :] < positions[:, None])
    slot_ids = jnp.sum(earlier.astype(jnp.int32), axis=1)
    band_ids = jnp.arange(band_count, dtype=jnp.int32)
    slot_range = jnp.arange(capacity, dtype=jnp.int32)
    matches = (owner_ids[:, None, None] == band_ids[None, :, None]) & (
        slot_ids[:, None, None] == slot_range[None, None, :]
    )
    request = jnp.sum(jnp.where(matches, source[:, None, None], 0), axis=0)
    wanted = lax.all_to_all(request, "lat", split_axis=0, concat_axis=0, tiled=True)
    by_row = jnp.transpose(tracers, (2, 0, 1, 3))
    outgoing = by_row[wanted]
    incoming = lax.all_to_all(outgoing, "lat", split_axis=0, concat_axis=0, tiled=True)
    stacked_rows = incoming.reshape((band_count * capacity,) + incoming.shape[2:])
    picked = stacked_rows[owner_ids * capacity + slot_ids].reshape(
        (row_count, link_count) + stacked_rows.shape[1:]
    )
    summed = dep_weight[:, 0][:, None, None, None] * picked[:, 0]
    summed = summed + dep_weight[:, 1][:, None, None, None] * picked[:, 1]
    return jnp.transpose(summed, (1, 2, 0, 3))


def circle_basis(cells, length):
    half_length = length // 2
    column = jnp.arange(length, dtype=jnp.int32)
    frequency = jnp.where(column <= half_length, column, column - half_length)
    low_count = math.gcd(cells.shape[0], 64)
    low = jnp.arange(low_count, dtype=jnp.int32)
    high = cells.reshape(-1, low_count)[:, 0]
    scale = 2.0 * math.pi / length
    low_angle = scale * (low[:, None] * frequency[None, :] % length).astype(jnp.float32)
    high_angle = scale * (high[:, None] * frequency[None, :] % length).astype(jnp.float32)
    low_cos, low_sin = jnp.cos(low_angle), jnp.sin(low_angle)
    high_cos, high_sin = jnp.cos(high_angle), jnp.sin(high_angle)
    cos_part = high_cos[:, None] * low_cos[None] - high_sin[:, None] * low_sin[None]
    sin_part = high_sin[:, None] * low_cos[None] + high_cos[:, None] * low_sin[None]
    basis = jnp.where((column <= half_length)[None, None, :], cos_part, sin_part)
    return basis.reshape(cells.shape[0], length)


def polar_filter(values, band_rows):
    fields, levels, rows, block_cells = values.shape
    parts = lax.axis_size("lon")
    me = lax.axis_index("lon")
    length = block_cells * parts
    flat = values.reshape(fields * levels * rows, block_cells)
    chunk = flat.shape[0] // parts
    blocks = [lax.dynamic_slice_in_dim(flat, me * chunk, chunk, axis=0)]
    for shift in range(1, parts):
        target = (me + shift) % parts
        piece = lax.dynamic_slice_in_dim(flat, target * chunk, chunk, axis=0)
        pairs = [(i, (i + shift) % parts) for i in range(parts)]
        blocks.append(lax.ppermute(piece, "lon", pairs))
    circles = jnp.concatenate(blocks, axis=1)
    shifts = jnp.arange(parts, dtype=jnp.int32)
    sources = (me - shifts) % parts
    cells = (sources[:, None] * block_cells + jnp.arange(block_cells, dtype=jnp.int32)[None]).reshape(length)
    basis_table = circle_basis(cells, length)
    spectrum = jnp.dot(circles, basis_table, precision=lax.Precision.HIGH)
    factors = column_factors(band_rows, length)
    scaled = (spectrum.reshape(chunk // rows, rows, length) * factors[None]).reshape(chunk, length)
    change = lax.dot_general(
        scaled, basis_table, (((1,), (1,)), ((), ())), precision=lax.Precision.HIGH
    )
    updated = circles + change
    returned = [updated[:, :block_cells]]
    for shift in range(1, parts):
        pairs = [(i, (i - shift) % parts) for i in range(parts)]
        piece = updated[:, shift * block_cells:(shift + 1) * block_cells]
        returned.append(lax.ppermute(piece, "lon", pairs))
    placed = [lax.select_n((index - me) % parts, *returned) for index in range(parts)]
    return jnp.concatenate(placed, axis=0).reshape(values.shape)


def band_distance(a, b, band_count):
    return min(abs(a - b), a + b + 1, 2 * band_count - 1 - a - b)


def near_plan(band_count, entries, capacity):
    reach = min(band_count, -(-entries // capacity) + 1)
    tail = max(1, capacity // 3)
    nearest = []
    limits = np.zeros((band_count, band_count), np.int32)
    for band in range(band_count):
        order = sorted(range(band_count), key=lambda o: (band_distance(band, o, band_count), o))
        nearest.append(order[:reach])
        for owner in order[:reach]:
            limits[band, owner] = capacity
        if reach < band_count and reach > 2:
            last, before = order[reach - 1], order[reach - 2]
            if band_distance(band, last, band_count) > band_distance(band, before, band_count):
                limits[band, last] = tail
    groups = {}
    for band in range(band_count):
        for owner in nearest[band]:
            if owner != band:
                groups.setdefault((owner - band, int(limits[band, owner])), []).append((owner, band))
    merged = []
    for (offset, size), pairs in sorted(groups.items(), key=lambda g: -len(g[1])):
        for held in merged:
            sources = {o for o, _ in held[1]}
            targets = {b for _, b in held[1]}
            if held[0] == size and not sources & {o for o, _ in pairs} and not targets & {b for _, b in pairs}:
                held[1].extend(pairs)
                break
        else:
            merged.append((size, list(pairs)))
    return limits, [((index, size), pairs) for index, (size, pairs) in enumerate(merged)]


def departure_near(tracers, dep_owner, dep_row, dep_weight, limits, groups, capacity):
    band_count = lax.axis_size("lat")
    row_count, link_count = dep_owner.shape
    entries = row_count * link_count
    me = lax.axis_index("lat")
    owner_ids = dep_owner.reshape(entries)
    source = dep_row.reshape(entries)
    positions = jnp.arange(entries)
    earlier = (owner_ids[:, None] == owner_ids[None, :]) & (positions[None, :] < positions[:, None])
    slot_ids = jnp.sum(earlier.astype(jnp.int32), axis=1)
    table = np.zeros((band_count, band_count + 2 * len(groups)), np.int32)
    table[:, :band_count] = limits
    for index, (_, pairs) in enumerate(groups):
        table[:, band_count + 2 * index + 1] = -1
        for owner, band in pairs:
            table[owner, band_count + 2 * index] = band
            table[band, band_count + 2 * index + 1] = owner
    mine = lax.dynamic_index_in_dim(jnp.asarray(table), me, axis=0, keepdims=False)
    outside = jnp.sum((slot_ids >= mine[:band_count][owner_ids]).astype(jnp.int32))
    band_ids = jnp.arange(band_count, dtype=jnp.int32)
    slot_range = jnp.arange(capacity, dtype=jnp.int32)
    matches = (owner_ids[:, None, None] == band_ids[None, :, None]) & (
        slot_ids[:, None, None] == slot_range[None, None, :]
    )
    request = jnp.sum(jnp.where(matches, source[:, None, None], 0), axis=0)
    flag = jnp.broadcast_to(outside, (band_count, 1)).astype(jnp.int32)
    message = jnp.concatenate([request, flag], axis=1)
    wanted = lax.all_to_all(message, "lat", split_axis=0, concat_axis=0, tiled=True)
    covered = jnp.all(wanted[:, capacity] == 0)
    weights = dep_weight.reshape(entries)
    row_range = jnp.arange(row_count, dtype=jnp.int32)
    own = jnp.where((owner_ids == me)[:, None] & (source[:, None] == row_range[None, :]),
                    weights[:, None], 0.0)
    own_weights = jnp.sum(own.reshape(row_count, link_count, row_count), axis=1)
    total = jnp.einsum("jr,flri->flji", own_weights, tracers, precision=PRECISE)
    by_size = {}
    for index, ((_, size), pairs) in enumerate(groups):
        receiver = mine[band_count + 2 * index]
        chosen = wanted[receiver, :size]
        select = (chosen[:, None] == row_range[None, :]).astype(jnp.float32)
        outgoing = jnp.einsum("sr,flri->flsi", select, tracers, precision=PRECISE)
        incoming = lax.ppermute(outgoing, "lat", pairs)
        sender = mine[band_count + 2 * index + 1]
        hit = (owner_ids[:, None] == sender) & (slot_ids[:, None] == slot_range[None, :size])
        part = jnp.where(hit, weights[:, None], 0.0)
        part_weights = jnp.sum(part.reshape(row_count, link_count, size), axis=1)
        by_size.setdefault(size, []).append((part_weights, incoming))
    for size, items in sorted(by_size.items()):
        part_weights = jnp.stack([w for w, _ in items], axis=0)
        incoming = jnp.stack([x for _, x in items], axis=0)
        total = total + jnp.einsum("ojs,oflsi->flji", part_weights, incoming, precision=PRECISE)
    return total, covered


def departure_all(tracers, dep_owner, dep_row, dep_weight):
    band_count = lax.axis_size("lat")
    row_count, link_count = dep_owner.shape
    entries = row_count * link_count
    capacity = max(2, -(-2 * entries // band_count))
    limits, groups = near_plan(band_count, entries, capacity)
    near, covered = departure_near(
        tracers, dep_owner, dep_row, dep_weight, limits, groups, capacity
    )
    return lax.cond(
        covered,
        lambda: near,
        lambda: departure_terms(tracers, dep_owner, dep_row, dep_weight),
    )


def body(
    prognostic,
    tracers,
    zonal_courant,
    meridional_courant,
    filter_band,
    dep_owner,
    dep_row,
    dep_weight,
):
    row_count = prognostic.shape[2]
    departed = departure_all(tracers, dep_owner, dep_row, dep_weight)
    lon_padded = padded(
        jnp.concatenate([prognostic, zonal_courant[None]], axis=0), (("lon", 3),), 1, True
    )
    zonal_flux = face_flux(lon_padded[:-1], lon_padded[-1:], 3)
    lat_padded = padded(
        jnp.concatenate([prognostic, meridional_courant[None]], axis=0), (("lat", 2),), 1, False
    )
    merid_flux = face_flux(lat_padded[:-1], lat_padded[-1:], 2)
    total_rows = row_count * lax.axis_size("lat")
    face_rows = lax.axis_index("lat") * row_count + jnp.arange(row_count + 1) - 1
    merid_flux = jnp.where(
        (face_rows == total_rows - 1)[None, None, :, None], jnp.float32(0.0), merid_flux
    )
    advected = (
        prognostic
        - (zonal_flux[..., 1:] - zonal_flux[..., :-1])
        - (merid_flux[:, :, 1:] - merid_flux[:, :, :-1])
    )
    new_prognostic = polar_filter(advected, filter_band)
    return (new_prognostic, departed)


def solution(mesh):
    return jax.shard_map(
        body,
        mesh=mesh,
        in_specs=(
            P(None, None, "lat", "lon"),
            P(None, None, "lat", "lon"),
            P(None, "lat", "lon"),
            P(None, "lat", "lon"),
            P("lat"),
            P("lat", None),
            P("lat", None),
            P("lat", None),
        ),
        out_specs=(P(None, None, "lat", "lon"), P(None, None, "lat", "lon")),
        check_vma=False,
    )
```

```python
import math

import jax
import numpy as np
import jax.numpy as jnp
from jax import lax
from jax.sharding import PartitionSpec as P

PRECISE = lax.Precision.HIGHEST


def padded(value, sides, width, wrap):
    for axis, dim in sides:
        size, length = (lax.axis_size(axis), value.shape[dim])
        up = [(i, (i + 1) % size) for i in range(size if wrap else size - 1)]
        down = [(j, i) for i, j in up]
        last = lax.slice_in_dim(value, length - width, length, axis=dim)
        first = lax.slice_in_dim(value, 0, width, axis=dim)
        before = lax.ppermute(last, axis, up)
        after = lax.ppermute(first, axis, down)
        value = jnp.concatenate([before, value, after], axis=dim)
    return value


def face_flux(values, speeds, axis):
    count = values.shape[axis] - 2
    left_cells = lax.slice_in_dim(values, 0, count + 1, axis=axis)
    right_cells = lax.slice_in_dim(values, 1, count + 2, axis=axis)
    courant = lax.slice_in_dim(speeds, 0, count + 1, axis=axis)
    return 0.5 * courant * (left_cells + right_cells) - 0.5 * courant * courant * (
        right_cells - left_cells
    )


def column_factors(band_rows, length):
    column = jnp.arange(length, dtype=jnp.int32)
    half_length = length // 2
    frequency = jnp.where(column <= half_length, column, column - half_length)
    single = (column == 0) | (column == half_length)
    weights = jnp.where(single, 1.0 / length, 2.0 / length).astype(jnp.float32)
    ratios = (
        band_rows.astype(jnp.float32)[:, None]
        / jnp.maximum(frequency, 1).astype(jnp.float32)[None, :]
    )
    damping = jnp.minimum(1.0, ratios * ratios)
    return (damping - 1.0) * weights[None, :]


def column_factors(band_rows, length):
    column = jnp.arange(length, dtype=jnp.int32)
    half_length = length // 2
    frequency = jnp.where(column <= half_length, column, column - half_length)
    single = (column == 0) | (column == half_length)
    weights = jnp.where(single, 1.0 / length, 2.0 / length).astype(jnp.float32)
    ratios = (
        band_rows.astype(jnp.float32)[:, None]
        / jnp.maximum(frequency, 1).astype(jnp.float32)[None, :]
    )
    damping = jnp.minimum(1.0, ratios * ratios)
    return (damping - 1.0) * weights[None, :]


def circle_basis(length):
    half_length = length // 2
    column = jnp.arange(length, dtype=jnp.int32)
    frequency = jnp.where(column <= half_length, column, column - half_length)
    low_count = 64
    high_count = length // low_count
    low = jnp.arange(low_count, dtype=jnp.int32)
    high = jnp.arange(high_count, dtype=jnp.int32) * low_count
    scale = 2.0 * math.pi / length
    low_angle = scale * (low[:, None] * frequency[None, :] % length).astype(jnp.float32)
    high_angle = scale * (high[:, None] * frequency[None, :] % length).astype(jnp.float32)
    low_cos, low_sin = jnp.cos(low_angle), jnp.sin(low_angle)
    high_cos, high_sin = jnp.cos(high_angle), jnp.sin(high_angle)
    cos_part = high_cos[:, None] * low_cos[None] - high_sin[:, None] * low_sin[None]
    sin_part = high_sin[:, None] * low_cos[None] + high_cos[:, None] * low_sin[None]
    basis = jnp.where((column <= half_length)[None, None, :], cos_part, sin_part)
    return basis.reshape(length, length)


def departure_terms(tracers, dep_owner, dep_row, dep_weight):
    band_count = lax.axis_size("lat")
    row_count, link_count = dep_owner.shape
    entries = row_count * link_count
    capacity = max(2, -(-2 * entries // band_count))
    owner_ids = dep_owner.reshape(entries)
    source = dep_row.reshape(entries)
    positions = jnp.arange(entries)
    earlier = (owner_ids[:, None] == owner_ids[None, :]) & (positions[None, :] < positions[:, None])
    slot_ids = jnp.sum(earlier.astype(jnp.int32), axis=1)
    band_ids = jnp.arange(band_count, dtype=jnp.int32)
    slot_range = jnp.arange(capacity, dtype=jnp.int32)
    matches = (owner_ids[:, None, None] == band_ids[None, :, None]) & (
        slot_ids[:, None, None] == slot_range[None, None, :]
    )
    request = jnp.sum(jnp.where(matches, source[:, None, None], 0), axis=0)
    wanted = lax.all_to_all(request, "lat", split_axis=0, concat_axis=0, tiled=True)
    by_row = jnp.transpose(tracers, (2, 0, 1, 3))
    outgoing = by_row[wanted]
    incoming = lax.all_to_all(outgoing, "lat", split_axis=0, concat_axis=0, tiled=True)
    stacked_rows = incoming.reshape((band_count * capacity,) + incoming.shape[2:])
    picked = stacked_rows[owner_ids * capacity + slot_ids].reshape(
        (row_count, link_count) + stacked_rows.shape[1:]
    )
    summed = dep_weight[:, 0][:, None, None, None] * picked[:, 0]
    summed = summed + dep_weight[:, 1][:, None, None, None] * picked[:, 1]
    return jnp.transpose(summed, (1, 2, 0, 3))


def circle_basis(cells, length):
    half_length = length // 2
    column = jnp.arange(length, dtype=jnp.int32)
    frequency = jnp.where(column <= half_length, column, column - half_length)
    low_count = math.gcd(cells.shape[0], 64)
    low = jnp.arange(low_count, dtype=jnp.int32)
    high = cells.reshape(-1, low_count)[:, 0]
    scale = 2.0 * math.pi / length
    low_angle = scale * (low[:, None] * frequency[None, :] % length).astype(jnp.float32)
    high_angle = scale * (high[:, None] * frequency[None, :] % length).astype(jnp.float32)
    low_cos, low_sin = jnp.cos(low_angle), jnp.sin(low_angle)
    high_cos, high_sin = jnp.cos(high_angle), jnp.sin(high_angle)
    cos_part = high_cos[:, None] * low_cos[None] - high_sin[:, None] * low_sin[None]
    sin_part = high_sin[:, None] * low_cos[None] + high_cos[:, None] * low_sin[None]
    basis = jnp.where((column <= half_length)[None, None, :], cos_part, sin_part)
    return basis.reshape(cells.shape[0], length)


def polar_filter(values, band_rows):
    fields, levels, rows, block_cells = values.shape
    parts = lax.axis_size("lon")
    me = lax.axis_index("lon")
    length = block_cells * parts
    flat = values.reshape(fields * levels * rows, block_cells)
    chunk = flat.shape[0] // parts
    blocks = [lax.dynamic_slice_in_dim(flat, me * chunk, chunk, axis=0)]
    for shift in range(1, parts):
        target = (me + shift) % parts
        piece = lax.dynamic_slice_in_dim(flat, target * chunk, chunk, axis=0)
        pairs = [(i, (i + shift) % parts) for i in range(parts)]
        blocks.append(lax.ppermute(piece, "lon", pairs))
    circles = jnp.concatenate(blocks, axis=1)
    shifts = jnp.arange(parts, dtype=jnp.int32)
    sources = (me - shifts) % parts
    cells = (sources[:, None] * block_cells + jnp.arange(block_cells, dtype=jnp.int32)[None]).reshape(length)
    basis_table = circle_basis(cells, length)
    spectrum = jnp.dot(circles, basis_table, precision=lax.Precision.HIGH)
    factors = column_factors(band_rows, length)
    scaled = (spectrum.reshape(chunk // rows, rows, length) * factors[None]).reshape(chunk, length)
    change = lax.dot_general(
        scaled, basis_table, (((1,), (1,)), ((), ())), precision=lax.Precision.HIGH
    )
    updated = circles + change
    returned = [updated[:, :block_cells]]
    for shift in range(1, parts):
        pairs = [(i, (i - shift) % parts) for i in range(parts)]
        piece = updated[:, shift * block_cells:(shift + 1) * block_cells]
        returned.append(lax.ppermute(piece, "lon", pairs))
    placed = [lax.select_n((index - me) % parts, *returned) for index in range(parts)]
    return jnp.concatenate(placed, axis=0).reshape(values.shape)


def band_distance(a, b, band_count):
    return min(abs(a - b), a + b + 1, 2 * band_count - 1 - a - b)


def near_plan(band_count, entries, capacity):
    reach = min(band_count, -(-entries // capacity) + 1)
    tail = max(1, capacity // 4)
    nearest = []
    limits = np.zeros((band_count, band_count), np.int32)
    for band in range(band_count):
        order = sorted(range(band_count), key=lambda o: (band_distance(band, o, band_count), o))
        nearest.append(order[:reach])
        for owner in order[:reach]:
            limits[band, owner] = capacity
        if reach < band_count and reach > 2:
            last, before = order[reach - 1], order[reach - 2]
            if band_distance(band, last, band_count) > band_distance(band, before, band_count):
                limits[band, last] = tail
    groups = {}
    for band in range(band_count):
        for owner in nearest[band]:
            if owner != band:
                groups.setdefault((owner - band, int(limits[band, owner])), []).append((owner, band))
    merged = []
    for (offset, size), pairs in sorted(groups.items(), key=lambda g: -len(g[1])):
        for held in merged:
            sources = {o for o, _ in held[1]}
            targets = {b for _, b in held[1]}
            if held[0] == size and not sources & {o for o, _ in pairs} and not targets & {b for _, b in pairs}:
                held[1].extend(pairs)
                break
        else:
            merged.append((size, list(pairs)))
    return limits, [((index, size), pairs) for index, (size, pairs) in enumerate(merged)]


def departure_near(tracers, dep_owner, dep_row, dep_weight, limits, groups, capacity):
    band_count = lax.axis_size("lat")
    row_count, link_count = dep_owner.shape
    entries = row_count * link_count
    me = lax.axis_index("lat")
    owner_ids = dep_owner.reshape(entries)
    source = dep_row.reshape(entries)
    positions = jnp.arange(entries)
    earlier = (owner_ids[:, None] == owner_ids[None, :]) & (positions[None, :] < positions[:, None])
    slot_ids = jnp.sum(earlier.astype(jnp.int32), axis=1)
    table = np.zeros((band_count, band_count + 2 * len(groups)), np.int32)
    table[:, :band_count] = limits
    for index, (_, pairs) in enumerate(groups):
        table[:, band_count + 2 * index + 1] = -1
        for owner, band in pairs:
            table[owner, band_count + 2 * index] = band
            table[band, band_count + 2 * index + 1] = owner
    mine = lax.dynamic_index_in_dim(jnp.asarray(table), me, axis=0, keepdims=False)
    outside = jnp.sum((slot_ids >= mine[:band_count][owner_ids]).astype(jnp.int32))
    band_ids = jnp.arange(band_count, dtype=jnp.int32)
    slot_range = jnp.arange(capacity, dtype=jnp.int32)
    matches = (owner_ids[:, None, None] == band_ids[None, :, None]) & (
        slot_ids[:, None, None] == slot_range[None, None, :]
    )
    request = jnp.sum(jnp.where(matches, source[:, None, None], 0), axis=0)
    flag = jnp.broadcast_to(outside, (band_count, 1)).astype(jnp.int32)
    message = jnp.concatenate([request, flag], axis=1)
    wanted = lax.all_to_all(message, "lat", split_axis=0, concat_axis=0, tiled=True)
    covered = jnp.all(wanted[:, capacity] == 0)
    weights = dep_weight.reshape(entries)
    row_range = jnp.arange(row_count, dtype=jnp.int32)
    own = jnp.where((owner_ids == me)[:, None] & (source[:, None] == row_range[None, :]),
                    weights[:, None], 0.0)
    own_weights = jnp.sum(own.reshape(row_count, link_count, row_count), axis=1)
    total = jnp.einsum("jr,flri->flji", own_weights, tracers, precision=PRECISE)
    by_size = {}
    for index, ((_, size), pairs) in enumerate(groups):
        receiver = mine[band_count + 2 * index]
        chosen = wanted[receiver, :size]
        select = (chosen[:, None] == row_range[None, :]).astype(jnp.float32)
        outgoing = jnp.einsum("sr,flri->flsi", select, tracers, precision=PRECISE)
        incoming = lax.ppermute(outgoing, "lat", pairs)
        sender = mine[band_count + 2 * index + 1]
        hit = (owner_ids[:, None] == sender) & (slot_ids[:, None] == slot_range[None, :size])
        part = jnp.where(hit, weights[:, None], 0.0)
        part_weights = jnp.sum(part.reshape(row_count, link_count, size), axis=1)
        by_size.setdefault(size, []).append((part_weights, incoming))
    for size, items in sorted(by_size.items()):
        part_weights = jnp.stack([w for w, _ in items], axis=0)
        incoming = jnp.stack([x for _, x in items], axis=0)
        total = total + jnp.einsum("ojs,oflsi->flji", part_weights, incoming, precision=PRECISE)
    return total, covered


def departure_all(tracers, dep_owner, dep_row, dep_weight):
    band_count = lax.axis_size("lat")
    row_count, link_count = dep_owner.shape
    entries = row_count * link_count
    capacity = max(2, -(-2 * entries // band_count))
    limits, groups = near_plan(band_count, entries, capacity)
    near, covered = departure_near(
        tracers, dep_owner, dep_row, dep_weight, limits, groups, capacity
    )
    return lax.cond(
        covered,
        lambda: near,
        lambda: departure_terms(tracers, dep_owner, dep_row, dep_weight),
    )


def body(
    prognostic,
    tracers,
    zonal_courant,
    meridional_courant,
    filter_band,
    dep_owner,
    dep_row,
    dep_weight,
):
    row_count = prognostic.shape[2]
    departed = departure_all(tracers, dep_owner, dep_row, dep_weight)
    lon_padded = padded(
        jnp.concatenate([prognostic, zonal_courant[None]], axis=0), (("lon", 3),), 1, True
    )
    zonal_flux = face_flux(lon_padded[:-1], lon_padded[-1:], 3)
    lat_padded = padded(
        jnp.concatenate([prognostic, meridional_courant[None]], axis=0), (("lat", 2),), 1, False
    )
    merid_flux = face_flux(lat_padded[:-1], lat_padded[-1:], 2)
    total_rows = row_count * lax.axis_size("lat")
    face_rows = lax.axis_index("lat") * row_count + jnp.arange(row_count + 1) - 1
    merid_flux = jnp.where(
        (face_rows == total_rows - 1)[None, None, :, None], jnp.float32(0.0), merid_flux
    )
    advected = (
        prognostic
        - (zonal_flux[..., 1:] - zonal_flux[..., :-1])
        - (merid_flux[:, :, 1:] - merid_flux[:, :, :-1])
    )
    new_prognostic = polar_filter(advected, filter_band)
    return (new_prognostic, departed)


def solution(mesh):
    return jax.shard_map(
        body,
        mesh=mesh,
        in_specs=(
            P(None, None, "lat", "lon"),
            P(None, None, "lat", "lon"),
            P(None, "lat", "lon"),
            P(None, "lat", "lon"),
            P("lat"),
            P("lat", None),
            P("lat", None),
            P("lat", None),
        ),
        out_specs=(P(None, None, "lat", "lon"), P(None, None, "lat", "lon")),
        check_vma=False,
    )
```

```python
import math

import jax
import numpy as np
import jax.numpy as jnp
from jax import lax
from jax.sharding import PartitionSpec as P

PRECISE = lax.Precision.HIGHEST


def padded(value, sides, width, wrap):
    for axis, dim in sides:
        size, length = (lax.axis_size(axis), value.shape[dim])
        up = [(i, (i + 1) % size) for i in range(size if wrap else size - 1)]
        down = [(j, i) for i, j in up]
        last = lax.slice_in_dim(value, length - width, length, axis=dim)
        first = lax.slice_in_dim(value, 0, width, axis=dim)
        before = lax.ppermute(last, axis, up)
        after = lax.ppermute(first, axis, down)
        value = jnp.concatenate([before, value, after], axis=dim)
    return value


def face_flux(values, speeds, axis):
    count = values.shape[axis] - 2
    left_cells = lax.slice_in_dim(values, 0, count + 1, axis=axis)
    right_cells = lax.slice_in_dim(values, 1, count + 2, axis=axis)
    courant = lax.slice_in_dim(speeds, 0, count + 1, axis=axis)
    return 0.5 * courant * (left_cells + right_cells) - 0.5 * courant * courant * (
        right_cells - left_cells
    )


def column_factors(band_rows, length):
    column = jnp.arange(length, dtype=jnp.int32)
    half_length = length // 2
    frequency = jnp.where(column <= half_length, column, column - half_length)
    single = (column == 0) | (column == half_length)
    weights = jnp.where(single, 1.0 / length, 2.0 / length).astype(jnp.float32)
    ratios = (
        band_rows.astype(jnp.float32)[:, None]
        / jnp.maximum(frequency, 1).astype(jnp.float32)[None, :]
    )
    damping = jnp.minimum(1.0, ratios * ratios)
    return (damping - 1.0) * weights[None, :]


def column_factors(band_rows, length):
    column = jnp.arange(length, dtype=jnp.int32)
    half_length = length // 2
    frequency = jnp.where(column <= half_length, column, column - half_length)
    single = (column == 0) | (column == half_length)
    weights = jnp.where(single, 1.0 / length, 2.0 / length).astype(jnp.float32)
    ratios = (
        band_rows.astype(jnp.float32)[:, None]
        / jnp.maximum(frequency, 1).astype(jnp.float32)[None, :]
    )
    damping = jnp.minimum(1.0, ratios * ratios)
    return (damping - 1.0) * weights[None, :]


def circle_basis(length):
    half_length = length // 2
    column = jnp.arange(length, dtype=jnp.int32)
    frequency = jnp.where(column <= half_length, column, column - half_length)
    low_count = 64
    high_count = length // low_count
    low = jnp.arange(low_count, dtype=jnp.int32)
    high = jnp.arange(high_count, dtype=jnp.int32) * low_count
    scale = 2.0 * math.pi / length
    low_angle = scale * (low[:, None] * frequency[None, :] % length).astype(jnp.float32)
    high_angle = scale * (high[:, None] * frequency[None, :] % length).astype(jnp.float32)
    low_cos, low_sin = jnp.cos(low_angle), jnp.sin(low_angle)
    high_cos, high_sin = jnp.cos(high_angle), jnp.sin(high_angle)
    cos_part = high_cos[:, None] * low_cos[None] - high_sin[:, None] * low_sin[None]
    sin_part = high_sin[:, None] * low_cos[None] + high_cos[:, None] * low_sin[None]
    basis = jnp.where((column <= half_length)[None, None, :], cos_part, sin_part)
    return basis.reshape(length, length)


def departure_terms(tracers, dep_owner, dep_row, dep_weight):
    band_count = lax.axis_size("lat")
    row_count, link_count = dep_owner.shape
    entries = row_count * link_count
    capacity = max(2, -(-2 * entries // band_count))
    owner_ids = dep_owner.reshape(entries)
    source = dep_row.reshape(entries)
    positions = jnp.arange(entries)
    earlier = (owner_ids[:, None] == owner_ids[None, :]) & (positions[None, :] < positions[:, None])
    slot_ids = jnp.sum(earlier.astype(jnp.int32), axis=1)
    band_ids = jnp.arange(band_count, dtype=jnp.int32)
    slot_range = jnp.arange(capacity, dtype=jnp.int32)
    matches = (owner_ids[:, None, None] == band_ids[None, :, None]) & (
        slot_ids[:, None, None] == slot_range[None, None, :]
    )
    request = jnp.sum(jnp.where(matches, source[:, None, None], 0), axis=0)
    wanted = lax.all_to_all(request, "lat", split_axis=0, concat_axis=0, tiled=True)
    by_row = jnp.transpose(tracers, (2, 0, 1, 3))
    outgoing = by_row[wanted]
    incoming = lax.all_to_all(outgoing, "lat", split_axis=0, concat_axis=0, tiled=True)
    stacked_rows = incoming.reshape((band_count * capacity,) + incoming.shape[2:])
    picked = stacked_rows[owner_ids * capacity + slot_ids].reshape(
        (row_count, link_count) + stacked_rows.shape[1:]
    )
    summed = dep_weight[:, 0][:, None, None, None] * picked[:, 0]
    summed = summed + dep_weight[:, 1][:, None, None, None] * picked[:, 1]
    return jnp.transpose(summed, (1, 2, 0, 3))


def circle_basis(cells, length):
    half_length = length // 2
    column = jnp.arange(length, dtype=jnp.int32)
    frequency = jnp.where(column <= half_length, column, column - half_length)
    low_count = math.gcd(cells.shape[0], 64)
    low = jnp.arange(low_count, dtype=jnp.int32)
    high = cells.reshape(-1, low_count)[:, 0]
    scale = 2.0 * math.pi / length
    low_angle = scale * (low[:, None] * frequency[None, :] % length).astype(jnp.float32)
    high_angle = scale * (high[:, None] * frequency[None, :] % length).astype(jnp.float32)
    low_cos, low_sin = jnp.cos(low_angle), jnp.sin(low_angle)
    high_cos, high_sin = jnp.cos(high_angle), jnp.sin(high_angle)
    cos_part = high_cos[:, None] * low_cos[None] - high_sin[:, None] * low_sin[None]
    sin_part = high_sin[:, None] * low_cos[None] + high_cos[:, None] * low_sin[None]
    basis = jnp.where((column <= half_length)[None, None, :], cos_part, sin_part)
    return basis.reshape(cells.shape[0], length)


def polar_filter(values, band_rows):
    fields, levels, rows, block_cells = values.shape
    parts = lax.axis_size("lon")
    me = lax.axis_index("lon")
    length = block_cells * parts
    flat = values.reshape(fields * levels * rows, block_cells)
    chunk = flat.shape[0] // parts
    blocks = [lax.dynamic_slice_in_dim(flat, me * chunk, chunk, axis=0)]
    for shift in range(1, parts):
        target = (me + shift) % parts
        piece = lax.dynamic_slice_in_dim(flat, target * chunk, chunk, axis=0)
        pairs = [(i, (i + shift) % parts) for i in range(parts)]
        blocks.append(lax.ppermute(piece, "lon", pairs))
    circles = jnp.concatenate(blocks, axis=1)
    shifts = jnp.arange(parts, dtype=jnp.int32)
    sources = (me - shifts) % parts
    cells = (sources[:, None] * block_cells + jnp.arange(block_cells, dtype=jnp.int32)[None]).reshape(length)
    basis_table = circle_basis(cells, length)
    spectrum = jnp.dot(circles, basis_table, precision=lax.Precision.HIGH)
    factors = column_factors(band_rows, length)
    scaled = (spectrum.reshape(chunk // rows, rows, length) * factors[None]).reshape(chunk, length)
    change = lax.dot_general(
        scaled, basis_table, (((1,), (1,)), ((), ())), precision=lax.Precision.HIGH
    )
    updated = circles + change
    returned = [updated[:, :block_cells]]
    for shift in range(1, parts):
        pairs = [(i, (i - shift) % parts) for i in range(parts)]
        piece = updated[:, shift * block_cells:(shift + 1) * block_cells]
        returned.append(lax.ppermute(piece, "lon", pairs))
    placed = [lax.select_n((index - me) % parts, *returned) for index in range(parts)]
    return jnp.concatenate(placed, axis=0).reshape(values.shape)


def band_distance(a, b, band_count):
    return min(abs(a - b), a + b + 1, 2 * band_count - 1 - a - b)


def near_plan(band_count, entries, capacity):
    reach = min(band_count, -(-entries // capacity) + 1)
    tail = max(1, capacity // 3)
    nearest = []
    limits = np.zeros((band_count, band_count), np.int32)
    for band in range(band_count):
        order = sorted(range(band_count), key=lambda o: (band_distance(band, o, band_count), o))
        nearest.append(order[:reach])
        for owner in order[:reach]:
            limits[band, owner] = capacity
        if reach < band_count and reach > 2:
            last, before = order[reach - 1], order[reach - 2]
            if band_distance(band, last, band_count) > band_distance(band, before, band_count):
                limits[band, last] = tail
    groups = {}
    for band in range(band_count):
        for owner in nearest[band]:
            if owner != band:
                groups.setdefault((owner - band, int(limits[band, owner])), []).append((owner, band))
    merged = []
    for (offset, size), pairs in sorted(groups.items(), key=lambda g: -len(g[1])):
        for held in merged:
            sources = {o for o, _ in held[1]}
            targets = {b for _, b in held[1]}
            if held[0] == size and not sources & {o for o, _ in pairs} and not targets & {b for _, b in pairs}:
                held[1].extend(pairs)
                break
        else:
            merged.append((size, list(pairs)))
    return limits, [((index, size), pairs) for index, (size, pairs) in enumerate(merged)]


def departure_near(tracers, dep_owner, dep_row, dep_weight, limits, groups, capacity):
    band_count = lax.axis_size("lat")
    row_count, link_count = dep_owner.shape
    entries = row_count * link_count
    me = lax.axis_index("lat")
    owner_ids = dep_owner.reshape(entries)
    source = dep_row.reshape(entries)
    positions = jnp.arange(entries)
    earlier = (owner_ids[:, None] == owner_ids[None, :]) & (positions[None, :] < positions[:, None])
    slot_ids = jnp.sum(earlier.astype(jnp.int32), axis=1)
    table = np.zeros((band_count, band_count + 2 * len(groups)), np.int32)
    table[:, :band_count] = limits
    for index, (_, pairs) in enumerate(groups):
        table[:, band_count + 2 * index + 1] = -1
        for owner, band in pairs:
            table[owner, band_count + 2 * index] = band
            table[band, band_count + 2 * index + 1] = owner
    mine = lax.dynamic_index_in_dim(jnp.asarray(table), me, axis=0, keepdims=False)
    outside = jnp.sum((slot_ids >= mine[:band_count][owner_ids]).astype(jnp.int32))
    band_ids = jnp.arange(band_count, dtype=jnp.int32)
    slot_range = jnp.arange(capacity, dtype=jnp.int32)
    matches = (owner_ids[:, None, None] == band_ids[None, :, None]) & (
        slot_ids[:, None, None] == slot_range[None, None, :]
    )
    request = jnp.sum(jnp.where(matches, source[:, None, None], 0), axis=0)
    flag = jnp.broadcast_to(outside, (band_count, 1)).astype(jnp.int32)
    message = jnp.concatenate([request, flag], axis=1)
    wanted = lax.all_to_all(message, "lat", split_axis=0, concat_axis=0, tiled=True)
    covered = jnp.all(wanted[:, capacity] == 0)
    weights = dep_weight.reshape(entries)
    row_range = jnp.arange(row_count, dtype=jnp.int32)
    own = jnp.where((owner_ids == me)[:, None] & (source[:, None] == row_range[None, :]),
                    weights[:, None], 0.0)
    own_weights = jnp.sum(own.reshape(row_count, link_count, row_count), axis=1)
    total = jnp.einsum("jr,flri->flji", own_weights, tracers, precision=PRECISE)
    by_size = {}
    for index, ((_, size), pairs) in enumerate(groups):
        receiver = mine[band_count + 2 * index]
        chosen = wanted[receiver, :size]
        select = (chosen[:, None] == row_range[None, :]).astype(jnp.float32)
        outgoing = jnp.einsum("sr,flri->flsi", select, tracers, precision=PRECISE)
        incoming = lax.ppermute(outgoing, "lat", pairs)
        sender = mine[band_count + 2 * index + 1]
        hit = (owner_ids[:, None] == sender) & (slot_ids[:, None] == slot_range[None, :size])
        part = jnp.where(hit, weights[:, None], 0.0)
        part_weights = jnp.sum(part.reshape(row_count, link_count, size), axis=1)
        by_size.setdefault(size, []).append((part_weights, incoming))
    for size, items in sorted(by_size.items()):
        part_weights = jnp.stack([w for w, _ in items], axis=0)
        incoming = jnp.stack([x for _, x in items], axis=0)
        total = total + jnp.einsum("ojs,oflsi->flji", part_weights, incoming, precision=PRECISE)
    return total, covered


def departure_all(tracers, dep_owner, dep_row, dep_weight):
    band_count = lax.axis_size("lat")
    row_count, link_count = dep_owner.shape
    entries = row_count * link_count
    capacity = max(2, -(-2 * entries // band_count))
    limits, groups = near_plan(band_count, entries, capacity)
    near, covered = departure_near(
        tracers, dep_owner, dep_row, dep_weight, limits, groups, capacity
    )
    general = lax.cond(
        covered,
        lambda: jnp.zeros_like(near),
        lambda: departure_terms(tracers, dep_owner, dep_row, dep_weight),
    )
    return jnp.where(covered, near, general)


def body(
    prognostic,
    tracers,
    zonal_courant,
    meridional_courant,
    filter_band,
    dep_owner,
    dep_row,
    dep_weight,
):
    row_count = prognostic.shape[2]
    departed = departure_all(tracers, dep_owner, dep_row, dep_weight)
    lon_padded = padded(
        jnp.concatenate([prognostic, zonal_courant[None]], axis=0), (("lon", 3),), 1, True
    )
    zonal_flux = face_flux(lon_padded[:-1], lon_padded[-1:], 3)
    lat_padded = padded(
        jnp.concatenate([prognostic, meridional_courant[None]], axis=0), (("lat", 2),), 1, False
    )
    merid_flux = face_flux(lat_padded[:-1], lat_padded[-1:], 2)
    total_rows = row_count * lax.axis_size("lat")
    face_rows = lax.axis_index("lat") * row_count + jnp.arange(row_count + 1) - 1
    merid_flux = jnp.where(
        (face_rows == total_rows - 1)[None, None, :, None], jnp.float32(0.0), merid_flux
    )
    advected = (
        prognostic
        - (zonal_flux[..., 1:] - zonal_flux[..., :-1])
        - (merid_flux[:, :, 1:] - merid_flux[:, :, :-1])
    )
    new_prognostic = polar_filter(advected, filter_band)
    return (new_prognostic, departed)


def solution(mesh):
    return jax.shard_map(
        body,
        mesh=mesh,
        in_specs=(
            P(None, None, "lat", "lon"),
            P(None, None, "lat", "lon"),
            P(None, "lat", "lon"),
            P(None, "lat", "lon"),
            P("lat"),
            P("lat", None),
            P("lat", None),
            P("lat", None),
        ),
        out_specs=(P(None, None, "lat", "lon"), P(None, None, "lat", "lon")),
        check_vma=False,
    )
```

```python
import math

import jax
import numpy as np
import jax.numpy as jnp
from jax import lax
from jax.sharding import PartitionSpec as P

PRECISE = lax.Precision.HIGHEST


def padded(value, sides, width, wrap):
    for axis, dim in sides:
        size, length = (lax.axis_size(axis), value.shape[dim])
        up = [(i, (i + 1) % size) for i in range(size if wrap else size - 1)]
        down = [(j, i) for i, j in up]
        last = lax.slice_in_dim(value, length - width, length, axis=dim)
        first = lax.slice_in_dim(value, 0, width, axis=dim)
        before = lax.ppermute(last, axis, up)
        after = lax.ppermute(first, axis, down)
        value = jnp.concatenate([before, value, after], axis=dim)
    return value


def face_flux(values, speeds, axis):
    count = values.shape[axis] - 2
    left_cells = lax.slice_in_dim(values, 0, count + 1, axis=axis)
    right_cells = lax.slice_in_dim(values, 1, count + 2, axis=axis)
    courant = lax.slice_in_dim(speeds, 0, count + 1, axis=axis)
    return 0.5 * courant * (left_cells + right_cells) - 0.5 * courant * courant * (
        right_cells - left_cells
    )


def column_factors(band_rows, length):
    column = jnp.arange(length, dtype=jnp.int32)
    half_length = length // 2
    frequency = jnp.where(column <= half_length, column, column - half_length)
    single = (column == 0) | (column == half_length)
    weights = jnp.where(single, 1.0 / length, 2.0 / length).astype(jnp.float32)
    ratios = (
        band_rows.astype(jnp.float32)[:, None]
        / jnp.maximum(frequency, 1).astype(jnp.float32)[None, :]
    )
    damping = jnp.minimum(1.0, ratios * ratios)
    return (damping - 1.0) * weights[None, :]


def column_factors(band_rows, length):
    column = jnp.arange(length, dtype=jnp.int32)
    half_length = length // 2
    frequency = jnp.where(column <= half_length, column, column - half_length)
    single = (column == 0) | (column == half_length)
    weights = jnp.where(single, 1.0 / length, 2.0 / length).astype(jnp.float32)
    ratios = (
        band_rows.astype(jnp.float32)[:, None]
        / jnp.maximum(frequency, 1).astype(jnp.float32)[None, :]
    )
    damping = jnp.minimum(1.0, ratios * ratios)
    return (damping - 1.0) * weights[None, :]


def circle_basis(length):
    half_length = length // 2
    column = jnp.arange(length, dtype=jnp.int32)
    frequency = jnp.where(column <= half_length, column, column - half_length)
    low_count = 64
    high_count = length // low_count
    low = jnp.arange(low_count, dtype=jnp.int32)
    high = jnp.arange(high_count, dtype=jnp.int32) * low_count
    scale = 2.0 * math.pi / length
    low_angle = scale * (low[:, None] * frequency[None, :] % length).astype(jnp.float32)
    high_angle = scale * (high[:, None] * frequency[None, :] % length).astype(jnp.float32)
    low_cos, low_sin = jnp.cos(low_angle), jnp.sin(low_angle)
    high_cos, high_sin = jnp.cos(high_angle), jnp.sin(high_angle)
    cos_part = high_cos[:, None] * low_cos[None] - high_sin[:, None] * low_sin[None]
    sin_part = high_sin[:, None] * low_cos[None] + high_cos[:, None] * low_sin[None]
    basis = jnp.where((column <= half_length)[None, None, :], cos_part, sin_part)
    return basis.reshape(length, length)


def departure_terms(tracers, dep_owner, dep_row, dep_weight):
    band_count = lax.axis_size("lat")
    row_count, link_count = dep_owner.shape
    entries = row_count * link_count
    capacity = max(2, -(-2 * entries // band_count))
    owner_ids = dep_owner.reshape(entries)
    source = dep_row.reshape(entries)
    positions = jnp.arange(entries)
    earlier = (owner_ids[:, None] == owner_ids[None, :]) & (positions[None, :] < positions[:, None])
    slot_ids = jnp.sum(earlier.astype(jnp.int32), axis=1)
    band_ids = jnp.arange(band_count, dtype=jnp.int32)
    slot_range = jnp.arange(capacity, dtype=jnp.int32)
    matches = (owner_ids[:, None, None] == band_ids[None, :, None]) & (
        slot_ids[:, None, None] == slot_range[None, None, :]
    )
    request = jnp.sum(jnp.where(matches, source[:, None, None], 0), axis=0)
    wanted = lax.all_to_all(request, "lat", split_axis=0, concat_axis=0, tiled=True)
    by_row = jnp.transpose(tracers, (2, 0, 1, 3))
    outgoing = by_row[wanted]
    incoming = lax.all_to_all(outgoing, "lat", split_axis=0, concat_axis=0, tiled=True)
    stacked_rows = incoming.reshape((band_count * capacity,) + incoming.shape[2:])
    picked = stacked_rows[owner_ids * capacity + slot_ids].reshape(
        (row_count, link_count) + stacked_rows.shape[1:]
    )
    summed = dep_weight[:, 0][:, None, None, None] * picked[:, 0]
    summed = summed + dep_weight[:, 1][:, None, None, None] * picked[:, 1]
    return jnp.transpose(summed, (1, 2, 0, 3))


def circle_basis(cells, length):
    half_length = length // 2
    column = jnp.arange(length, dtype=jnp.int32)
    frequency = jnp.where(column <= half_length, column, column - half_length)
    low_count = math.gcd(cells.shape[0], 64)
    low = jnp.arange(low_count, dtype=jnp.int32)
    high = cells.reshape(-1, low_count)[:, 0]
    scale = 2.0 * math.pi / length
    low_angle = scale * (low[:, None] * frequency[None, :] % length).astype(jnp.float32)
    high_angle = scale * (high[:, None] * frequency[None, :] % length).astype(jnp.float32)
    low_cos, low_sin = jnp.cos(low_angle), jnp.sin(low_angle)
    high_cos, high_sin = jnp.cos(high_angle), jnp.sin(high_angle)
    cos_part = high_cos[:, None] * low_cos[None] - high_sin[:, None] * low_sin[None]
    sin_part = high_sin[:, None] * low_cos[None] + high_cos[:, None] * low_sin[None]
    basis = jnp.where((column <= half_length)[None, None, :], cos_part, sin_part)
    return basis.reshape(cells.shape[0], length)


def polar_filter(values, band_rows):
    fields, levels, rows, block_cells = values.shape
    parts = lax.axis_size("lon")
    me = lax.axis_index("lon")
    length = block_cells * parts
    flat = values.reshape(fields * levels * rows, block_cells)
    chunk = flat.shape[0] // parts
    blocks = [lax.dynamic_slice_in_dim(flat, me * chunk, chunk, axis=0)]
    for shift in range(1, parts):
        target = (me + shift) % parts
        piece = lax.dynamic_slice_in_dim(flat, target * chunk, chunk, axis=0)
        pairs = [(i, (i + shift) % parts) for i in range(parts)]
        blocks.append(lax.ppermute(piece, "lon", pairs))
    circles = jnp.concatenate(blocks, axis=1)
    shifts = jnp.arange(parts, dtype=jnp.int32)
    sources = (me - shifts) % parts
    cells = (sources[:, None] * block_cells + jnp.arange(block_cells, dtype=jnp.int32)[None]).reshape(length)
    basis_table = circle_basis(cells, length)
    spectrum = jnp.dot(circles, basis_table, precision=lax.Precision.HIGH)
    factors = column_factors(band_rows, length)
    scaled = (spectrum.reshape(chunk // rows, rows, length) * factors[None]).reshape(chunk, length)
    change = lax.dot_general(
        scaled, basis_table, (((1,), (1,)), ((), ())), precision=lax.Precision.HIGH
    )
    updated = circles + change
    returned = [updated[:, :block_cells]]
    for shift in range(1, parts):
        pairs = [(i, (i - shift) % parts) for i in range(parts)]
        piece = updated[:, shift * block_cells:(shift + 1) * block_cells]
        returned.append(lax.ppermute(piece, "lon", pairs))
    placed = [lax.select_n((index - me) % parts, *returned) for index in range(parts)]
    return jnp.concatenate(placed, axis=0).reshape(values.shape)


def band_distance(a, b, band_count):
    return min(abs(a - b), a + b + 1, 2 * band_count - 1 - a - b)


def near_plan(band_count, entries, capacity):
    reach = min(band_count, -(-entries // capacity) + 1)
    tail = max(1, capacity // 3)
    nearest = []
    limits = np.zeros((band_count, band_count), np.int32)
    for band in range(band_count):
        order = sorted(range(band_count), key=lambda o: (band_distance(band, o, band_count), o))
        nearest.append(order[:reach])
        for owner in order[:reach]:
            limits[band, owner] = capacity
        if reach < band_count and reach > 2:
            last, before = order[reach - 1], order[reach - 2]
            if band_distance(band, last, band_count) > band_distance(band, before, band_count):
                limits[band, last] = tail
    groups = {}
    for band in range(band_count):
        for owner in nearest[band]:
            if owner != band:
                groups.setdefault((owner - band, int(limits[band, owner])), []).append((owner, band))
    merged = []
    for (offset, size), pairs in sorted(groups.items(), key=lambda g: -len(g[1])):
        for held in merged:
            sources = {o for o, _ in held[1]}
            targets = {b for _, b in held[1]}
            if held[0] == size and not sources & {o for o, _ in pairs} and not targets & {b for _, b in pairs}:
                held[1].extend(pairs)
                break
        else:
            merged.append((size, list(pairs)))
    return limits, [((index, size), pairs) for index, (size, pairs) in enumerate(merged)]


def departure_near(tracers, dep_owner, dep_row, dep_weight, limits, groups, capacity):
    band_count = lax.axis_size("lat")
    row_count, link_count = dep_owner.shape
    entries = row_count * link_count
    me = lax.axis_index("lat")
    owner_ids = dep_owner.reshape(entries)
    source = dep_row.reshape(entries)
    positions = jnp.arange(entries)
    earlier = (owner_ids[:, None] == owner_ids[None, :]) & (positions[None, :] < positions[:, None])
    slot_ids = jnp.sum(earlier.astype(jnp.int32), axis=1)
    table = np.zeros((band_count, band_count + 2 * len(groups)), np.int32)
    table[:, :band_count] = limits
    for index, (_, pairs) in enumerate(groups):
        table[:, band_count + 2 * index + 1] = -1
        for owner, band in pairs:
            table[owner, band_count + 2 * index] = band
            table[band, band_count + 2 * index + 1] = owner
    mine = lax.dynamic_index_in_dim(jnp.asarray(table), me, axis=0, keepdims=False)
    outside = jnp.sum((slot_ids >= mine[:band_count][owner_ids]).astype(jnp.int32))
    band_ids = jnp.arange(band_count, dtype=jnp.int32)
    slot_range = jnp.arange(capacity, dtype=jnp.int32)
    matches = (owner_ids[:, None, None] == band_ids[None, :, None]) & (
        slot_ids[:, None, None] == slot_range[None, None, :]
    )
    request = jnp.sum(jnp.where(matches, source[:, None, None], 0), axis=0)
    flag = jnp.broadcast_to(outside, (band_count, 1)).astype(jnp.int32)
    message = jnp.concatenate([request, flag], axis=1)
    wanted = lax.all_to_all(message, "lat", split_axis=0, concat_axis=0, tiled=True)
    covered = jnp.all(wanted[:, capacity] == 0)
    weights = dep_weight.reshape(entries)
    row_range = jnp.arange(row_count, dtype=jnp.int32)
    own = jnp.where((owner_ids == me)[:, None] & (source[:, None] == row_range[None, :]),
                    weights[:, None], 0.0)
    own_weights = jnp.sum(own.reshape(row_count, link_count, row_count), axis=1)
    total = jnp.einsum("jr,flri->flji", own_weights, tracers, precision=PRECISE)
    by_size = {}
    for index, ((_, size), pairs) in enumerate(groups):
        receiver = mine[band_count + 2 * index]
        chosen = wanted[receiver, :size]
        select = (chosen[:, None] == row_range[None, :]).astype(jnp.float32)
        outgoing = jnp.einsum("sr,flri->flsi", select, tracers, precision=PRECISE)
        incoming = lax.ppermute(outgoing, "lat", pairs)
        sender = mine[band_count + 2 * index + 1]
        hit = (owner_ids[:, None] == sender) & (slot_ids[:, None] == slot_range[None, :size])
        part = jnp.where(hit, weights[:, None], 0.0)
        part_weights = jnp.sum(part.reshape(row_count, link_count, size), axis=1)
        by_size.setdefault(size, []).append((part_weights, incoming))
    for size, items in sorted(by_size.items()):
        for part_weights, incoming in items:
            total = total + jnp.einsum("js,flsi->flji", part_weights, incoming, precision=PRECISE)
    return total, covered


def departure_all(tracers, dep_owner, dep_row, dep_weight):
    band_count = lax.axis_size("lat")
    row_count, link_count = dep_owner.shape
    entries = row_count * link_count
    capacity = max(2, -(-2 * entries // band_count))
    limits, groups = near_plan(band_count, entries, capacity)
    near, covered = departure_near(
        tracers, dep_owner, dep_row, dep_weight, limits, groups, capacity
    )
    general = lax.cond(
        covered,
        lambda: jnp.zeros_like(near),
        lambda: departure_terms(tracers, dep_owner, dep_row, dep_weight),
    )
    return jnp.where(covered, near, general)


def body(
    prognostic,
    tracers,
    zonal_courant,
    meridional_courant,
    filter_band,
    dep_owner,
    dep_row,
    dep_weight,
):
    row_count = prognostic.shape[2]
    departed = departure_all(tracers, dep_owner, dep_row, dep_weight)
    lon_padded = padded(
        jnp.concatenate([prognostic, zonal_courant[None]], axis=0), (("lon", 3),), 1, True
    )
    zonal_flux = face_flux(lon_padded[:-1], lon_padded[-1:], 3)
    lat_padded = padded(
        jnp.concatenate([prognostic, meridional_courant[None]], axis=0), (("lat", 2),), 1, False
    )
    merid_flux = face_flux(lat_padded[:-1], lat_padded[-1:], 2)
    total_rows = row_count * lax.axis_size("lat")
    face_rows = lax.axis_index("lat") * row_count + jnp.arange(row_count + 1) - 1
    merid_flux = jnp.where(
        (face_rows == total_rows - 1)[None, None, :, None], jnp.float32(0.0), merid_flux
    )
    advected = (
        prognostic
        - (zonal_flux[..., 1:] - zonal_flux[..., :-1])
        - (merid_flux[:, :, 1:] - merid_flux[:, :, :-1])
    )
    new_prognostic = polar_filter(advected, filter_band)
    return (new_prognostic, departed)


def solution(mesh):
    return jax.shard_map(
        body,
        mesh=mesh,
        in_specs=(
            P(None, None, "lat", "lon"),
            P(None, None, "lat", "lon"),
            P(None, "lat", "lon"),
            P(None, "lat", "lon"),
            P("lat"),
            P("lat", None),
            P("lat", None),
            P("lat", None),
        ),
        out_specs=(P(None, None, "lat", "lon"), P(None, None, "lat", "lon")),
        check_vma=False,
    )
```

```python
import math

import jax
import numpy as np
import jax.numpy as jnp
from jax import lax
from jax.sharding import PartitionSpec as P

PRECISE = lax.Precision.HIGHEST


def padded(value, sides, width, wrap):
    for axis, dim in sides:
        size, length = (lax.axis_size(axis), value.shape[dim])
        up = [(i, (i + 1) % size) for i in range(size if wrap else size - 1)]
        down = [(j, i) for i, j in up]
        last = lax.slice_in_dim(value, length - width, length, axis=dim)
        first = lax.slice_in_dim(value, 0, width, axis=dim)
        before = lax.ppermute(last, axis, up)
        after = lax.ppermute(first, axis, down)
        value = jnp.concatenate([before, value, after], axis=dim)
    return value


def face_flux(values, speeds, axis):
    count = values.shape[axis] - 2
    left_cells = lax.slice_in_dim(values, 0, count + 1, axis=axis)
    right_cells = lax.slice_in_dim(values, 1, count + 2, axis=axis)
    courant = lax.slice_in_dim(speeds, 0, count + 1, axis=axis)
    return 0.5 * courant * (left_cells + right_cells) - 0.5 * courant * courant * (
        right_cells - left_cells
    )


def column_factors(band_rows, length):
    column = jnp.arange(length, dtype=jnp.int32)
    half_length = length // 2
    frequency = jnp.where(column <= half_length, column, column - half_length)
    single = (column == 0) | (column == half_length)
    weights = jnp.where(single, 1.0 / length, 2.0 / length).astype(jnp.float32)
    ratios = (
        band_rows.astype(jnp.float32)[:, None]
        / jnp.maximum(frequency, 1).astype(jnp.float32)[None, :]
    )
    damping = jnp.minimum(1.0, ratios * ratios)
    return (damping - 1.0) * weights[None, :]


def column_factors(band_rows, length):
    column = jnp.arange(length, dtype=jnp.int32)
    half_length = length // 2
    frequency = jnp.where(column <= half_length, column, column - half_length)
    single = (column == 0) | (column == half_length)
    weights = jnp.where(single, 1.0 / length, 2.0 / length).astype(jnp.float32)
    ratios = (
        band_rows.astype(jnp.float32)[:, None]
        / jnp.maximum(frequency, 1).astype(jnp.float32)[None, :]
    )
    damping = jnp.minimum(1.0, ratios * ratios)
    return (damping - 1.0) * weights[None, :]


def circle_basis(length):
    half_length = length // 2
    column = jnp.arange(length, dtype=jnp.int32)
    frequency = jnp.where(column <= half_length, column, column - half_length)
    low_count = 64
    high_count = length // low_count
    low = jnp.arange(low_count, dtype=jnp.int32)
    high = jnp.arange(high_count, dtype=jnp.int32) * low_count
    scale = 2.0 * math.pi / length
    low_angle = scale * (low[:, None] * frequency[None, :] % length).astype(jnp.float32)
    high_angle = scale * (high[:, None] * frequency[None, :] % length).astype(jnp.float32)
    low_cos, low_sin = jnp.cos(low_angle), jnp.sin(low_angle)
    high_cos, high_sin = jnp.cos(high_angle), jnp.sin(high_angle)
    cos_part = high_cos[:, None] * low_cos[None] - high_sin[:, None] * low_sin[None]
    sin_part = high_sin[:, None] * low_cos[None] + high_cos[:, None] * low_sin[None]
    basis = jnp.where((column <= half_length)[None, None, :], cos_part, sin_part)
    return basis.reshape(length, length)


def departure_terms(tracers, dep_owner, dep_row, dep_weight):
    band_count = lax.axis_size("lat")
    row_count, link_count = dep_owner.shape
    entries = row_count * link_count
    capacity = max(2, -(-2 * entries // band_count))
    owner_ids = dep_owner.reshape(entries)
    source = dep_row.reshape(entries)
    positions = jnp.arange(entries)
    earlier = (owner_ids[:, None] == owner_ids[None, :]) & (positions[None, :] < positions[:, None])
    slot_ids = jnp.sum(earlier.astype(jnp.int32), axis=1)
    band_ids = jnp.arange(band_count, dtype=jnp.int32)
    slot_range = jnp.arange(capacity, dtype=jnp.int32)
    matches = (owner_ids[:, None, None] == band_ids[None, :, None]) & (
        slot_ids[:, None, None] == slot_range[None, None, :]
    )
    request = jnp.sum(jnp.where(matches, source[:, None, None], 0), axis=0)
    wanted = lax.all_to_all(request, "lat", split_axis=0, concat_axis=0, tiled=True)
    by_row = jnp.transpose(tracers, (2, 0, 1, 3))
    outgoing = by_row[wanted]
    incoming = lax.all_to_all(outgoing, "lat", split_axis=0, concat_axis=0, tiled=True)
    stacked_rows = incoming.reshape((band_count * capacity,) + incoming.shape[2:])
    picked = stacked_rows[owner_ids * capacity + slot_ids].reshape(
        (row_count, link_count) + stacked_rows.shape[1:]
    )
    summed = dep_weight[:, 0][:, None, None, None] * picked[:, 0]
    summed = summed + dep_weight[:, 1][:, None, None, None] * picked[:, 1]
    return jnp.transpose(summed, (1, 2, 0, 3))


def circle_basis(cells, length):
    half_length = length // 2
    column = jnp.arange(length, dtype=jnp.int32)
    frequency = jnp.where(column <= half_length, column, column - half_length)
    low_count = math.gcd(cells.shape[0], 64)
    low = jnp.arange(low_count, dtype=jnp.int32)
    high = cells.reshape(-1, low_count)[:, 0]
    scale = 2.0 * math.pi / length
    low_angle = scale * (low[:, None] * frequency[None, :] % length).astype(jnp.float32)
    high_angle = scale * (high[:, None] * frequency[None, :] % length).astype(jnp.float32)
    low_cos, low_sin = jnp.cos(low_angle), jnp.sin(low_angle)
    high_cos, high_sin = jnp.cos(high_angle), jnp.sin(high_angle)
    cos_part = high_cos[:, None] * low_cos[None] - high_sin[:, None] * low_sin[None]
    sin_part = high_sin[:, None] * low_cos[None] + high_cos[:, None] * low_sin[None]
    basis = jnp.where((column <= half_length)[None, None, :], cos_part, sin_part)
    return basis.reshape(cells.shape[0], length)


def polar_filter(values, band_rows):
    fields, levels, rows, block_cells = values.shape
    parts = lax.axis_size("lon")
    me = lax.axis_index("lon")
    length = block_cells * parts
    flat = values.reshape(fields * levels * rows, block_cells)
    chunk = flat.shape[0] // parts
    blocks = [lax.dynamic_slice_in_dim(flat, me * chunk, chunk, axis=0)]
    for shift in range(1, parts):
        target = (me + shift) % parts
        piece = lax.dynamic_slice_in_dim(flat, target * chunk, chunk, axis=0)
        pairs = [(i, (i + shift) % parts) for i in range(parts)]
        blocks.append(lax.ppermute(piece, "lon", pairs))
    circles = jnp.concatenate(blocks, axis=1)
    shifts = jnp.arange(parts, dtype=jnp.int32)
    sources = (me - shifts) % parts
    cells = (sources[:, None] * block_cells + jnp.arange(block_cells, dtype=jnp.int32)[None]).reshape(length)
    basis_table = circle_basis(cells, length)
    spectrum = jnp.dot(circles, basis_table, precision=lax.Precision.HIGH)
    factors = column_factors(band_rows, length)
    scaled = (spectrum.reshape(chunk // rows, rows, length) * factors[None]).reshape(chunk, length)
    change = lax.dot_general(
        scaled, basis_table, (((1,), (1,)), ((), ())), precision=lax.Precision.HIGH
    )
    updated = circles + change
    returned = [updated[:, :block_cells]]
    for shift in range(1, parts):
        pairs = [(i, (i - shift) % parts) for i in range(parts)]
        piece = updated[:, shift * block_cells:(shift + 1) * block_cells]
        returned.append(lax.ppermute(piece, "lon", pairs))
    placed = [lax.select_n((index - me) % parts, *returned) for index in range(parts)]
    return jnp.concatenate(placed, axis=0).reshape(values.shape)


def band_distance(a, b, band_count):
    return min(abs(a - b), a + b + 1, 2 * band_count - 1 - a - b)


def near_plan(band_count, entries, capacity):
    reach = min(band_count, -(-entries // capacity) + 1)
    tail = max(1, capacity // 3)
    nearest = []
    limits = np.zeros((band_count, band_count), np.int32)
    for band in range(band_count):
        order = sorted(range(band_count), key=lambda o: (band_distance(band, o, band_count), o))
        nearest.append(order[:reach])
        for owner in order[:reach]:
            limits[band, owner] = capacity
        if reach < band_count and reach > 2:
            last, before = order[reach - 1], order[reach - 2]
            if band_distance(band, last, band_count) > band_distance(band, before, band_count):
                limits[band, last] = tail
    groups = {}
    for band in range(band_count):
        for owner in nearest[band]:
            if owner != band:
                groups.setdefault((owner - band, int(limits[band, owner])), []).append((owner, band))
    merged = []
    for (offset, size), pairs in sorted(groups.items(), key=lambda g: -len(g[1])):
        for held in merged:
            sources = {o for o, _ in held[1]}
            targets = {b for _, b in held[1]}
            if held[0] == size and not sources & {o for o, _ in pairs} and not targets & {b for _, b in pairs}:
                held[1].extend(pairs)
                break
        else:
            merged.append((size, list(pairs)))
    return limits, [((index, size), pairs) for index, (size, pairs) in enumerate(merged)]


def departure_near(tracers, dep_owner, dep_row, dep_weight, limits, groups, capacity):
    band_count = lax.axis_size("lat")
    row_count, link_count = dep_owner.shape
    entries = row_count * link_count
    me = lax.axis_index("lat")
    owner_ids = dep_owner.reshape(entries)
    source = dep_row.reshape(entries)
    positions = jnp.arange(entries)
    earlier = (owner_ids[:, None] == owner_ids[None, :]) & (positions[None, :] < positions[:, None])
    slot_ids = jnp.sum(earlier.astype(jnp.int32), axis=1)
    table = np.zeros((band_count, band_count + 2 * len(groups)), np.int32)
    table[:, :band_count] = limits
    for index, (_, pairs) in enumerate(groups):
        table[:, band_count + 2 * index + 1] = -1
        for owner, band in pairs:
            table[owner, band_count + 2 * index] = band
            table[band, band_count + 2 * index + 1] = owner
    mine = lax.dynamic_index_in_dim(jnp.asarray(table), me, axis=0, keepdims=False)
    outside = jnp.sum((slot_ids >= mine[:band_count][owner_ids]).astype(jnp.int32))
    band_ids = jnp.arange(band_count, dtype=jnp.int32)
    slot_range = jnp.arange(capacity, dtype=jnp.int32)
    matches = (owner_ids[:, None, None] == band_ids[None, :, None]) & (
        slot_ids[:, None, None] == slot_range[None, None, :]
    )
    request = jnp.sum(jnp.where(matches, source[:, None, None], 0), axis=0)
    flag = jnp.broadcast_to(outside, (band_count, 1)).astype(jnp.int32)
    message = jnp.concatenate([request, flag], axis=1)
    wanted = lax.all_to_all(message, "lat", split_axis=0, concat_axis=0, tiled=True)
    covered = jnp.all(wanted[:, capacity] == 0)
    weights = dep_weight.reshape(entries)
    row_range = jnp.arange(row_count, dtype=jnp.int32)
    own = jnp.where((owner_ids == me)[:, None] & (source[:, None] == row_range[None, :]),
                    weights[:, None], 0.0)
    own_weights = jnp.sum(own.reshape(row_count, link_count, row_count), axis=1)
    total = jnp.einsum("jr,flri->flji", own_weights, tracers, precision=lax.Precision.HIGH)
    by_size = {}
    for index, ((_, size), pairs) in enumerate(groups):
        receiver = mine[band_count + 2 * index]
        chosen = wanted[receiver, :size]
        select = (chosen[:, None] == row_range[None, :]).astype(jnp.float32)
        outgoing = jnp.einsum("sr,flri->flsi", select, tracers, precision=PRECISE)
        incoming = lax.ppermute(outgoing, "lat", pairs)
        sender = mine[band_count + 2 * index + 1]
        hit = (owner_ids[:, None] == sender) & (slot_ids[:, None] == slot_range[None, :size])
        part = jnp.where(hit, weights[:, None], 0.0)
        part_weights = jnp.sum(part.reshape(row_count, link_count, size), axis=1)
        by_size.setdefault(size, []).append((part_weights, incoming))
    for size, items in sorted(by_size.items()):
        part_weights = jnp.stack([w for w, _ in items], axis=0)
        incoming = jnp.stack([x for _, x in items], axis=0)
        total = total + jnp.einsum("ojs,oflsi->flji", part_weights, incoming, precision=lax.Precision.HIGH)
    return total, covered


def departure_all(tracers, dep_owner, dep_row, dep_weight):
    band_count = lax.axis_size("lat")
    row_count, link_count = dep_owner.shape
    entries = row_count * link_count
    capacity = max(2, -(-2 * entries // band_count))
    limits, groups = near_plan(band_count, entries, capacity)
    near, covered = departure_near(
        tracers, dep_owner, dep_row, dep_weight, limits, groups, capacity
    )
    general = lax.cond(
        covered,
        lambda: jnp.zeros_like(near),
        lambda: departure_terms(tracers, dep_owner, dep_row, dep_weight),
    )
    return jnp.where(covered, near, general)


def body(
    prognostic,
    tracers,
    zonal_courant,
    meridional_courant,
    filter_band,
    dep_owner,
    dep_row,
    dep_weight,
):
    row_count = prognostic.shape[2]
    departed = departure_all(tracers, dep_owner, dep_row, dep_weight)
    lon_padded = padded(
        jnp.concatenate([prognostic, zonal_courant[None]], axis=0), (("lon", 3),), 1, True
    )
    zonal_flux = face_flux(lon_padded[:-1], lon_padded[-1:], 3)
    lat_padded = padded(
        jnp.concatenate([prognostic, meridional_courant[None]], axis=0), (("lat", 2),), 1, False
    )
    merid_flux = face_flux(lat_padded[:-1], lat_padded[-1:], 2)
    total_rows = row_count * lax.axis_size("lat")
    face_rows = lax.axis_index("lat") * row_count + jnp.arange(row_count + 1) - 1
    merid_flux = jnp.where(
        (face_rows == total_rows - 1)[None, None, :, None], jnp.float32(0.0), merid_flux
    )
    advected = (
        prognostic
        - (zonal_flux[..., 1:] - zonal_flux[..., :-1])
        - (merid_flux[:, :, 1:] - merid_flux[:, :, :-1])
    )
    new_prognostic = polar_filter(advected, filter_band)
    return (new_prognostic, departed)


def solution(mesh):
    return jax.shard_map(
        body,
        mesh=mesh,
        in_specs=(
            P(None, None, "lat", "lon"),
            P(None, None, "lat", "lon"),
            P(None, "lat", "lon"),
            P(None, "lat", "lon"),
            P("lat"),
            P("lat", None),
            P("lat", None),
            P("lat", None),
        ),
        out_specs=(P(None, None, "lat", "lon"), P(None, None, "lat", "lon")),
        check_vma=False,
    )
```
